32 devices in a mesh: ctx: 16 (over z, x, core), ch: 2 (over y).
Axes of the slice: x: 2, y: 2, z: 4, core: 2. Of those that a mesh axis runs over, the one named last changes fastest.
Arguments:
- hidden: bfloat16 [4096, 2048], P(('ctx', 'ch')), may hold values from -6 to 6
- base_ids: int32 [4096], P(('ctx', 'ch')), may hold values from 0 to 4
- embed: bfloat16 [5, 2048], replicated, may hold values from -5 to 5
- w_x: bfloat16 [2048, 4096], P(None, 'ch'), may hold values from -0.125 to 0.125
- w_z: bfloat16 [2048, 4096], P(None, 'ch'), may hold values from -0.125 to 0.125
- w_bc: bfloat16 [2048, 256], replicated, may hold values from -0.125 to 0.125
- w_dt: bfloat16 [2048, 64], P(None, 'ch'), may hold values from -0.125 to 0.125
- dt_bias: float32 [64], P('ch'), may hold values from -3 to 0.5
- decay_rate: float32 [64], P('ch'), may hold values from 7.324219e-05 to 0.12
- conv_x: float32 [4, 4096], P(None, 'ch'), may hold values from -3 to 3
- conv_bc: float32 [4, 256], replicated, may hold values from -3 to 3
- d_skip: float32 [64], P('ch'), may hold values from 0.5 to 1.5
- norm_gain: bfloat16 [4096], P('ch'), may hold values from 0.25 to 1.75
- w_out: bfloat16 [4096, 2048], P('ch'), may hold values from -0.09375 to 0.09375
Outputs:
- mixed: bfloat16 [4096, 2048], P(('ctx', 'ch'))
The draws below stay inside these ranges and needn't reach their ends.
All inputs are finite; a program needn't handle non-finite values.
Results may differ from the reference program's by a relative error of at most 0.0074.
Values may be sent and summed in bfloat16 or wider, within the bound.
No kernel may reach another device: no remote copies, remote signals or barrier semaphores. Data moves between devices by JAX's collectives and lax.ppermute only.
A program may use at most 192 MiB of HBM per device.

```python
import math
import jax
import jax.numpy as jnp
from jax import lax

D = 2048
HEADS = 64
HEAD_DIM = 64
STATE = 128
CONV = 4
GROUP = 128
VOCAB = 5
DI = 4096
SEQ = 4096


def draw_decay_rate(key, part):
    key_pick = jax.random.fold_in(key, 11)
    key_slow = jax.random.fold_in(key, 12)
    key_fast = jax.random.fold_in(key, 13)
    share = 0.5
    slow = jax.random.bernoulli(key_pick, share, (HEADS,))
    slow_u = jax.random.uniform(key_slow, (HEADS,), jnp.float32)
    fast_u = jax.random.uniform(key_fast, (HEADS,), jnp.float32)
    slow_rate = 0.3 / SEQ * jnp.exp(slow_u * math.log(2.0 / 0.3))
    fast_rate = 0.04 * jnp.exp(fast_u * math.log(3.0))
    return jnp.where(slow, slow_rate, fast_rate).astype(jnp.float32)


def with_ends(drawn, rng, low, top_value):
    longest = drawn.shape.index(max(drawn.shape))
    spots = []
    for shift in (0, 1):
        where = [jax.random.randint(jax.random.fold_in(rng, axis), (), 0, length) for axis, length in enumerate(drawn.shape)]
        where[longest] = (where[longest] + shift) % drawn.shape[longest]
        spots.append(tuple(where))
    return drawn.at[spots[0]].set(low).at[spots[1]].set(top_value)


def level_of(rng, dims, pieces, smallest, largest):
    factor_of, own = 1.0, jax.random.fold_in(rng, 6)
    for dim, blocks in pieces:
        draws = jnp.exp(jax.random.uniform(jax.random.fold_in(own, dim), (blocks,), jnp.float32, smallest / len(pieces), largest / len(pieces)))
        factor_of = factor_of * jnp.repeat(draws, dims[dim] // blocks).reshape([-1 if axis == dim else 1 for axis in range(len(dims))])
    return factor_of


def bell_draw(own_key, extent, spread, limit, cuts=(), kind=jnp.bfloat16):
    factor_of = level_of(own_key, extent, cuts, -0.22, 0.18) if cuts else 1.0
    drawn = jax.random.normal(own_key, extent, jnp.float32) * spread * factor_of
    return jnp.minimum(jnp.maximum(drawn, -limit), limit).astype(kind)


def setup_inputs(seed: int = 0) -> dict:
    streams_of = jax.random.split(jax.random.key(seed), 15)
    hidden = bell_draw(streams_of[0], (SEQ, D), 1.0, 6.0, ((0, 32),))
    base_ids = with_ends(jax.random.randint(streams_of[1], (SEQ,), 0, VOCAB), jax.random.fold_in(streams_of[1], 1), 0, VOCAB - 1).astype(jnp.int32)
    embed = bell_draw(streams_of[2], (VOCAB, D), 1.0, 5.0)
    w_x = bell_draw(streams_of[3], (D, DI), D ** -0.5, 0.125, ((1, 2),))
    w_z = bell_draw(streams_of[4], (D, DI), D ** -0.5, 0.125, ((1, 2),))
    w_bc = bell_draw(streams_of[5], (D, 2 * STATE), D ** -0.5, 0.125)
    w_dt = bell_draw(streams_of[6], (D, HEADS), D ** -0.5, 0.125, ((1, 2),))
    dt_bias = jnp.clip(-3.0 + 3.5 * jax.random.uniform(streams_of[7], (HEADS,), jnp.float32) ** level_of(streams_of[7], (HEADS,), ((0, 2),), -0.2, 0.2), -3.0, 0.5)
    decay_rate = draw_decay_rate(jax.random.fold_in(streams_of[14], 71), 0)
    conv_x = bell_draw(streams_of[9], (CONV, DI), CONV ** -0.5, 3.0, ((1, 2),), jnp.float32)
    conv_bc = bell_draw(streams_of[10], (CONV, 2 * STATE), CONV ** -0.5, 3.0, (), jnp.float32)
    d_skip = jnp.clip(0.5 + 1.0 * jax.random.uniform(streams_of[11], (HEADS,), jnp.float32) ** level_of(streams_of[11], (HEADS,), ((0, 2),), -0.2, 0.2), 0.5, 1.5)
    norm_gain = jnp.clip(1.0 + 0.15 * jax.random.normal(streams_of[12], (DI,), jnp.float32), 0.25, 1.75).astype(jnp.bfloat16)
    w_out = bell_draw(streams_of[13], (DI, D), DI ** -0.5, 0.09375, ((0, 2),))
    return {"hidden": hidden, "base_ids": base_ids, "embed": embed, "w_x": w_x, "w_z": w_z, "w_bc": w_bc, "w_dt": w_dt, "dt_bias": dt_bias, "decay_rate": decay_rate, "conv_x": conv_x, "conv_bc": conv_bc, "d_skip": d_skip, "norm_gain": norm_gain, "w_out": w_out}


exact_dot = lax.Precision.HIGHEST
norm_eps = 1e-05

def group_local(x_block, step_size, b_block, c_block, decays):
    block_len = x_block.shape[0]
    log_decay = jnp.cumsum(-step_size * decays[None, :], axis=0)
    scores = jnp.dot(c_block, b_block.T, preferred_element_type=jnp.float32)
    row_ids = lax.broadcasted_iota(jnp.int32, (block_len, block_len), 0)
    col_ids = lax.broadcasted_iota(jnp.int32, (block_len, block_len), 1)
    causal = (row_ids >= col_ids)[None]
    log_heads = log_decay.T
    gap_log = jnp.where(causal, log_heads[:, :, None] - log_heads[:, None, :], 0.0)
    weights = jnp.where(causal, scores[None] * jnp.exp(gap_log) * step_size.T[:, None, :], 0.0).astype(jnp.bfloat16)
    intra_out = jnp.einsum('hij,jhp->ihp', weights.astype(jnp.float32), x_block.astype(jnp.float32), precision=exact_dot)
    tail_w = jnp.exp(log_decay[-1][None, :] - log_decay) * step_size
    operand = (tail_w.T[:, :, None] * b_block.astype(jnp.float32)[None]).astype(jnp.bfloat16)
    group_state = jnp.einsum('hqn,qhp->hnp', operand.astype(jnp.float32), x_block.astype(jnp.float32), precision=exact_dot)
    return (intra_out, log_decay, group_state)

def conv_silu(raw_proj, conv_all, rim_rows):
    padded = jnp.concatenate([rim_rows, raw_proj], axis=0)
    length = raw_proj.shape[0]
    summed = conv_all[0][None, :] * padded[0:length].astype(jnp.float32)
    for offset in range(1, CONV):
        summed = summed + conv_all[offset][None, :] * padded[offset:offset + length].astype(jnp.float32)
    return jax.nn.silu(summed).astype(jnp.bfloat16)

def run_ssd(x_all, step_size, b_mat, c_mat, decays, d_skip):
    seq_len = x_all.shape[0]
    blocks = seq_len // GROUP
    x_blocks = x_all.reshape(blocks, GROUP, HEADS, HEAD_DIM)
    step_blocks = step_size.reshape(blocks, GROUP, HEADS)
    b_blocks = b_mat.reshape(blocks, GROUP, STATE)
    c_blocks = c_mat.reshape(blocks, GROUP, STATE)

    def advance(carry, inputs):
        x_block, step_block, b_block, c_block = inputs
        intra_out, log_decay, group_state = group_local(x_block, step_block, b_block, c_block, decays)
        carried = jnp.einsum('qn,hnp->qhp', c_block.astype(jnp.float32), carry, precision=exact_dot)
        result = intra_out + carried * jnp.exp(log_decay)[:, :, None] + d_skip[None, :, None] * x_block.astype(jnp.float32)
        following = jnp.exp(log_decay[-1])[:, None, None] * carry + group_state
        return (following, result)
    start = jnp.zeros((HEADS, STATE, HEAD_DIM), jnp.float32)
    _, outputs = lax.scan(advance, start, (x_blocks, step_blocks, b_blocks, c_blocks))
    return outputs.reshape(seq_len, DI)

def strand(inputs, w_xbc, w_z, w_dt, dt_bias, decay_rate, conv_all, d_skip, norm_gain, w_out):
    raw_proj = jnp.dot(inputs, w_xbc, preferred_element_type=jnp.float32).astype(jnp.bfloat16)
    gate_z = jnp.dot(inputs, w_z, preferred_element_type=jnp.float32).astype(jnp.bfloat16)
    step_size = jax.nn.softplus(jnp.dot(inputs, w_dt, preferred_element_type=jnp.float32) + dt_bias[None, :])
    rim_rows = jnp.zeros((CONV - 1, raw_proj.shape[1]), jnp.bfloat16)
    conv_out = conv_silu(raw_proj, conv_all, rim_rows)
    x_all = conv_out[:, :DI].reshape(-1, HEADS, HEAD_DIM)
    b_mat = conv_out[:, DI:DI + STATE]
    c_mat = conv_out[:, DI + STATE:]
    y_all = run_ssd(x_all, step_size, b_mat, c_mat, decay_rate, d_skip)
    gated = (y_all * jax.nn.silu(gate_z.astype(jnp.float32))).astype(jnp.bfloat16)
    gated_wide = gated.astype(jnp.float32)
    mean_sq = lax.optimization_barrier(jnp.mean(gated_wide * gated_wide, axis=1, keepdims=True))
    normed = (gated_wide * lax.rsqrt(mean_sq + norm_eps) * norm_gain.astype(jnp.float32)[None, :]).astype(jnp.bfloat16)
    return jnp.dot(normed, w_out, preferred_element_type=jnp.float32)

def reference(hidden, base_ids, embed, w_x, w_z, w_bc, w_dt, dt_bias, decay_rate, conv_x, conv_bc, d_skip, norm_gain, w_out):
    onehot = (base_ids[:, None] == jnp.arange(embed.shape[0], dtype=jnp.int32)[None, :]).astype(jnp.bfloat16)
    mixed_in = (hidden.astype(jnp.float32) + jnp.dot(onehot, embed, preferred_element_type=jnp.float32)).astype(jnp.bfloat16)
    w_xbc = jnp.concatenate([w_x, w_bc], axis=1)
    conv_all = jnp.concatenate([conv_x, conv_bc], axis=1)
    forward = strand(mixed_in, w_xbc, w_z, w_dt, dt_bias, decay_rate, conv_all, d_skip, norm_gain, w_out)
    backward = strand(mixed_in[::-1, ::-1], w_xbc, w_z, w_dt, dt_bias, decay_rate, conv_all, d_skip, norm_gain, w_out)
    return (forward + backward[::-1, ::-1]).astype(jnp.bfloat16)
```

```python
import jax
import jax.numpy as jnp
from jax import lax
from jax.sharding import PartitionSpec as P

HEAD_DIM = 64
GROUP = 128

exact_dot = lax.Precision.HIGHEST
norm_eps = 1e-05
f32 = jnp.float32
bf16 = jnp.bfloat16


def flip_matrix(n):
    rows = lax.broadcasted_iota(jnp.int32, (n, n), 0)
    cols = lax.broadcasted_iota(jnp.int32, (n, n), 1)
    return (rows + cols == n - 1).astype(bf16)


def shifted(block, axis, distance):
    devices = range(lax.axis_size(axis))
    route = [(i, i + distance) for i in devices if i + distance in devices]
    return lax.ppermute(block, axis, route)


def conv_silu(raw, taps, rim, backward):
    conv = taps.shape[0]
    length = raw.shape[0]
    if backward:
        padded = jnp.concatenate([raw, rim], axis=0)
        summed = taps[0][None, :] * padded[conv - 1 : conv - 1 + length].astype(f32)
        for k in range(1, conv):
            start = conv - 1 - k
            summed = summed + taps[k][None, :] * padded[start : start + length].astype(f32)
    else:
        padded = jnp.concatenate([rim, raw], axis=0)
        summed = taps[0][None, :] * padded[0:length].astype(f32)
        for k in range(1, conv):
            summed = summed + taps[k][None, :] * padded[k : k + length].astype(f32)
    return jax.nn.silu(summed).astype(bf16)


def local_ssd(x, dt, b_mat, c_mat, rates, backward):
    length, inner = x.shape
    heads = dt.shape[1]
    nb = length // GROUP
    xb = x.reshape(nb, GROUP, heads, HEAD_DIM)
    dtb = dt.reshape(nb, GROUP, heads)
    bb = b_mat.reshape(nb, GROUP, -1)
    cb = c_mat.reshape(nb, GROUP, -1)
    step = -dtb * rates[None, None, :]
    cum = lax.cumsum(step, axis=1, reverse=backward)
    last = cum[:, 0, :] if backward else cum[:, -1, :]
    scores = jnp.einsum("kin,kjn->kij", cb, bb, preferred_element_type=f32)
    rows = lax.broadcasted_iota(jnp.int32, (GROUP, GROUP), 0)
    cols = lax.broadcasted_iota(jnp.int32, (GROUP, GROUP), 1)
    mask = (rows <= cols) if backward else (rows >= cols)
    mask = mask[None, None]
    cum_t = cum.transpose(0, 2, 1)
    gap = jnp.where(mask, cum_t[:, :, :, None] - cum_t[:, :, None, :], 0.0)
    dt_t = dtb.transpose(0, 2, 1)
    weights = jnp.where(mask, scores[:, None] * jnp.exp(gap) * dt_t[:, :, None, :], 0.0).astype(bf16)
    intra = jnp.einsum("khij,kjhp->kihp", weights, xb, preferred_element_type=f32)
    tail = jnp.exp(last[:, None, :] - cum) * dtb
    operand = (tail.transpose(0, 2, 1)[:, :, :, None] * bb.astype(f32)[:, None]).astype(bf16)
    block_state = jnp.einsum("khjn,kjhp->khpn", operand, xb, preferred_element_type=f32)
    block_decay = jnp.exp(last)
    return dict(xb=xb, cb=cb, cum=cum, intra=intra, block_state=block_state, block_decay=block_decay)


def stretch_states(parts, backward):
    block_state, block_decay = parts["block_state"], parts["block_decay"]
    nb = block_state.shape[0]
    order = list(range(nb - 1, -1, -1)) if backward else list(range(nb))
    starts = [None] * nb
    prefix = [None] * nb
    run_state = jnp.zeros_like(block_state[0])
    run_decay = jnp.ones_like(block_decay[0])
    for k in order:
        starts[k] = run_state
        prefix[k] = run_decay
        run_state = block_decay[k][:, None, None] * run_state + block_state[k]
        run_decay = run_decay * block_decay[k]
    return jnp.stack(starts), jnp.stack(prefix), run_state, run_decay


def scan_over(axis, own_decay, own_state, backward):
    peers = lax.axis_size(axis)
    step = -1 if backward else 1
    ex_decay = jnp.ones_like(own_decay)
    ex_state = jnp.zeros_like(own_state)
    in_decay, in_state = own_decay, own_state
    distance = 1
    while distance < peers:
        got_decay, got_state = shifted((in_decay, in_state), axis, step * distance)
        ex_state = ex_decay[:, None, None] * got_state + ex_state
        ex_decay = ex_decay * got_decay
        if distance * 2 < peers:
            in_state = in_decay[:, None, None] * got_state + in_state
            in_decay = in_decay * got_decay
        distance *= 2
    return ex_state


def strand_output(parts, starts, prefix, carry, d_skip):
    start_states = starts + prefix[:, :, None, None] * carry[None]
    carried = jnp.einsum(
        "kin,khpn->kihp", parts["cb"].astype(f32), start_states, precision=exact_dot
    )
    xb = parts["xb"]
    y = (
        parts["intra"]
        + jnp.exp(parts["cum"])[:, :, :, None] * carried
        + d_skip[None, None, :, None] * xb.astype(f32)
    )
    nb, g, h, p = y.shape
    return y.reshape(nb * g, h * p)


def per_device(
    hidden,
    base_ids,
    embed,
    w_x,
    w_z,
    w_bc,
    w_dt,
    dt_bias,
    decay_rate,
    conv_x,
    conv_bc,
    d_skip,
    norm_gain,
    w_out,
):
    inner = w_x.shape[1]
    state = w_bc.shape[1] // 2
    conv = conv_x.shape[0]
    onehot = (base_ids[:, None] == jnp.arange(embed.shape[0], dtype=jnp.int32)[None, :]).astype(bf16)
    mixed_in = (hidden.astype(f32) + jnp.dot(onehot, embed, preferred_element_type=f32)).astype(bf16)
    u = lax.all_gather(mixed_in, "ch", axis=0, tiled=True)
    length, width = u.shape
    flip = flip_matrix(width)
    u_flip = jnp.dot(u, flip, preferred_element_type=f32).astype(bf16)
    both = jnp.concatenate([u, u_flip], axis=0)
    x_raw = jnp.dot(both, w_x, preferred_element_type=f32).astype(bf16)
    z_all = jnp.dot(both, w_z, preferred_element_type=f32).astype(bf16)
    bc_raw = jnp.dot(both, w_bc, preferred_element_type=f32).astype(bf16)
    dt_all = jax.nn.softplus(jnp.dot(both, w_dt, preferred_element_type=f32) + dt_bias[None, :])

    outs = []
    sums = []
    for backward in (False, True):
        rows = slice(length, 2 * length) if backward else slice(0, length)
        xr, bcr = x_raw[rows], bc_raw[rows]
        if backward:
            rim_x = shifted(xr[: conv - 1], "ctx", -1)
            rim_bc = shifted(bcr[: conv - 1], "ctx", -1)
        else:
            rim_x = shifted(xr[length - conv + 1 :], "ctx", 1)
            rim_bc = shifted(bcr[length - conv + 1 :], "ctx", 1)
        x_c = conv_silu(xr, conv_x, rim_x, backward)
        bc_c = conv_silu(bcr, conv_bc, rim_bc, backward)
        parts = local_ssd(x_c, dt_all[rows], bc_c[:, :state], bc_c[:, state:], decay_rate, backward)
        starts, prefix, end_state, end_decay = stretch_states(parts, backward)
        carry = scan_over("ctx", end_decay, end_state, backward)
        y = strand_output(parts, starts, prefix, carry, d_skip)
        gated = (y * jax.nn.silu(z_all[rows].astype(f32))).astype(bf16).astype(f32)
        outs.append(gated)
        sums.append(jnp.sum(gated * gated, axis=1))
    total = lax.psum(jnp.stack(sums), "ch")
    full_inner = inner * lax.axis_size("ch")
    gain = norm_gain.astype(f32)[None, :]
    normed = [
        (g * lax.rsqrt(t / full_inner + norm_eps)[:, None] * gain).astype(bf16)
        for g, t in zip(outs, total)
    ]
    out_f = jnp.dot(normed[0], w_out, preferred_element_type=f32)
    out_b = jnp.dot(normed[1], w_out, preferred_element_type=f32)
    hi = out_b.astype(bf16)
    rest = out_b - hi.astype(f32)
    mid = rest.astype(bf16)
    lo = (rest - mid.astype(f32)).astype(bf16)
    pieces = jnp.dot(jnp.concatenate([hi, mid, lo], axis=0), flip, preferred_element_type=f32)
    out_b_flip = (pieces[:length] + pieces[length : 2 * length]) + pieces[2 * length :]
    summed = lax.psum_scatter(out_f + out_b_flip, "ch", scatter_dimension=0, tiled=True)
    return summed.astype(bf16)


def solution(mesh):
    placed = (
        P(("ctx", "ch"), None),
        P(("ctx", "ch")),
        P(),
        P(None, "ch"),
        P(None, "ch"),
        P(),
        P(None, "ch"),
        P("ch"),
        P("ch"),
        P(None, "ch"),
        P(),
        P("ch"),
        P("ch"),
        P("ch", None),
    )
    return jax.shard_map(
        per_device, mesh=mesh, in_specs=placed, out_specs=P(("ctx", "ch"), None), check_vma=False
    )
```

```python
import jax
import jax.numpy as jnp
from jax import lax
from jax.sharding import PartitionSpec as P

HEAD_DIM = 64
GROUP = 128

exact_dot = lax.Precision.HIGHEST
norm_eps = 1e-05
f32 = jnp.float32
bf16 = jnp.bfloat16


def flip_matrix(n):
    rows = lax.broadcasted_iota(jnp.int32, (n, n), 0)
    cols = lax.broadcasted_iota(jnp.int32, (n, n), 1)
    return (rows + cols == n - 1).astype(bf16)


def shifted(block, axis, distance):
    devices = range(lax.axis_size(axis))
    route = [(i, i + distance) for i in devices if i + distance in devices]
    return lax.ppermute(block, axis, route)


def gather_rows(block, axis):
    peers, me = lax.axis_size(axis), lax.axis_index(axis)
    got = [block] + [
        lax.ppermute(block, axis, [(i, (i + d) % peers) for i in range(peers)])
        for d in range(peers - 1, 0, -1)
    ]
    stacked = jnp.stack(got)
    rolled = jnp.roll(stacked, me, axis=0)
    return rolled.reshape(peers * block.shape[0], *block.shape[1:])


def flipped_columns(part, flip):
    hi = part.astype(bf16)
    rest = part - hi.astype(f32)
    mid = rest.astype(bf16)
    lo = (rest - mid.astype(f32)).astype(bf16)
    rows = part.shape[0]
    pieces = jnp.dot(jnp.concatenate([hi, mid, lo], axis=0), flip, preferred_element_type=f32)
    return (pieces[:rows] + pieces[rows : 2 * rows]) + pieces[2 * rows :]


def conv_silu(raw, taps, rim, backward):
    conv = taps.shape[0]
    length = raw.shape[0]
    if backward:
        padded = jnp.concatenate([raw, rim], axis=0)
        summed = taps[0][None, :] * padded[conv - 1 : conv - 1 + length].astype(f32)
        for k in range(1, conv):
            start = conv - 1 - k
            summed = summed + taps[k][None, :] * padded[start : start + length].astype(f32)
    else:
        padded = jnp.concatenate([rim, raw], axis=0)
        summed = taps[0][None, :] * padded[0:length].astype(f32)
        for k in range(1, conv):
            summed = summed + taps[k][None, :] * padded[k : k + length].astype(f32)
    return jax.nn.silu(summed).astype(bf16)


def local_ssd(x, dt, b_mat, c_mat, rates, backward):
    length, inner = x.shape
    heads = dt.shape[1]
    nb = length // GROUP
    xb = x.reshape(nb, GROUP, heads, HEAD_DIM)
    dtb = dt.reshape(nb, GROUP, heads)
    bb = b_mat.reshape(nb, GROUP, -1)
    cb = c_mat.reshape(nb, GROUP, -1)
    step = -dtb * rates[None, None, :]
    cum = lax.cumsum(step, axis=1, reverse=backward)
    last = cum[:, 0, :] if backward else cum[:, -1, :]
    scores = jnp.einsum("kin,kjn->kij", cb, bb, preferred_element_type=f32)
    rows = lax.broadcasted_iota(jnp.int32, (GROUP, GROUP), 0)
    cols = lax.broadcasted_iota(jnp.int32, (GROUP, GROUP), 1)
    mask = (rows <= cols) if backward else (rows >= cols)
    mask = mask[None, None]
    cum_t = cum.transpose(0, 2, 1)
    gap = jnp.where(mask, cum_t[:, :, :, None] - cum_t[:, :, None, :], 0.0)
    dt_t = dtb.transpose(0, 2, 1)
    weights = jnp.where(mask, scores[:, None] * jnp.exp(gap) * dt_t[:, :, None, :], 0.0).astype(bf16)
    intra = jnp.einsum("khij,kjhp->kihp", weights, xb, preferred_element_type=f32)
    tail = jnp.exp(last[:, None, :] - cum) * dtb
    operand = (tail.transpose(0, 2, 1)[:, :, :, None] * bb.astype(f32)[:, None]).astype(bf16)
    block_state = jnp.einsum("khjn,kjhp->khpn", operand, xb, preferred_element_type=f32)
    block_decay = jnp.exp(last)
    return dict(xb=xb, cb=cb, cum=cum, intra=intra, block_state=block_state, block_decay=block_decay)


def stretch_states(parts, backward):
    block_state, block_decay = parts["block_state"], parts["block_decay"]
    nb = block_state.shape[0]
    order = list(range(nb - 1, -1, -1)) if backward else list(range(nb))
    starts = [None] * nb
    prefix = [None] * nb
    run_state = jnp.zeros_like(block_state[0])
    run_decay = jnp.ones_like(block_decay[0])
    for k in order:
        starts[k] = run_state
        prefix[k] = run_decay
        run_state = block_decay[k][:, None, None] * run_state + block_state[k]
        run_decay = run_decay * block_decay[k]
    return jnp.stack(starts), jnp.stack(prefix), run_state, run_decay


def scan_over(axis, own_decay, own_state, backward):
    peers = lax.axis_size(axis)
    step = -1 if backward else 1
    ex_decay = jnp.ones_like(own_decay)
    ex_state = jnp.zeros_like(own_state)
    in_decay, in_state = own_decay, own_state
    distance = 1
    while distance < peers:
        got_decay, got_state = shifted((in_decay, in_state), axis, step * distance)
        ex_state = ex_decay[:, None, None] * got_state + ex_state
        ex_decay = ex_decay * got_decay
        if distance * 2 < peers:
            in_state = in_decay[:, None, None] * got_state + in_state
            in_decay = in_decay * got_decay
        distance *= 2
    return ex_state


def strand_output(parts, starts, prefix, carry, d_skip):
    start_states = starts + prefix[:, :, None, None] * carry[None]
    carried = jnp.einsum(
        "kin,khpn->kihp", parts["cb"].astype(f32), start_states, precision=exact_dot
    )
    xb = parts["xb"]
    y = (
        parts["intra"]
        + jnp.exp(parts["cum"])[:, :, :, None] * carried
        + d_skip[None, None, :, None] * xb.astype(f32)
    )
    nb, g, h, p = y.shape
    return y.reshape(nb * g, h * p)


def per_device(
    hidden,
    base_ids,
    embed,
    w_x,
    w_z,
    w_bc,
    w_dt,
    dt_bias,
    decay_rate,
    conv_x,
    conv_bc,
    d_skip,
    norm_gain,
    w_out,
):
    inner = w_x.shape[1]
    state = w_bc.shape[1] // 2
    conv = conv_x.shape[0]
    onehot = (base_ids[:, None] == jnp.arange(embed.shape[0], dtype=jnp.int32)[None, :]).astype(bf16)
    mixed_in = (hidden.astype(f32) + jnp.dot(onehot, embed, preferred_element_type=f32)).astype(bf16)
    u = gather_rows(mixed_in, "ch")
    length, width = u.shape
    flip = flip_matrix(width)
    u_flip = jnp.dot(u, flip, preferred_element_type=f32).astype(bf16)
    both = jnp.concatenate([u, u_flip], axis=0)
    x_raw = jnp.dot(both, w_x, preferred_element_type=f32).astype(bf16)
    z_all = jnp.dot(both, w_z, preferred_element_type=f32).astype(bf16)
    bc_raw = jnp.dot(both, w_bc, preferred_element_type=f32).astype(bf16)
    dt_all = jax.nn.softplus(jnp.dot(both, w_dt, preferred_element_type=f32) + dt_bias[None, :])

    outs = []
    sums = []
    for backward in (False, True):
        rows = slice(length, 2 * length) if backward else slice(0, length)
        xr, bcr = x_raw[rows], bc_raw[rows]
        if backward:
            rim_x = shifted(xr[: conv - 1], "ctx", -1)
            rim_bc = shifted(bcr[: conv - 1], "ctx", -1)
        else:
            rim_x = shifted(xr[length - conv + 1 :], "ctx", 1)
            rim_bc = shifted(bcr[length - conv + 1 :], "ctx", 1)
        x_c = conv_silu(xr, conv_x, rim_x, backward)
        bc_c = conv_silu(bcr, conv_bc, rim_bc, backward)
        parts = local_ssd(x_c, dt_all[rows], bc_c[:, :state], bc_c[:, state:], decay_rate, backward)
        starts, prefix, end_state, end_decay = stretch_states(parts, backward)
        carry = scan_over("ctx", end_decay, end_state, backward)
        y = strand_output(parts, starts, prefix, carry, d_skip)
        gated = (y * jax.nn.silu(z_all[rows].astype(f32))).astype(bf16).astype(f32)
        outs.append(gated)
        sums.append(jnp.sum(gated * gated, axis=1))
    total = lax.psum(jnp.stack(sums), "ch")
    full_inner = inner * lax.axis_size("ch")
    gain = norm_gain.astype(f32)[None, :]
    normed = [
        (g * lax.rsqrt(t / full_inner + norm_eps)[:, None] * gain).astype(bf16)
        for g, t in zip(outs, total)
    ]
    peers, me = lax.axis_size("ch"), lax.axis_index("ch")
    own_rows = length // peers

    def partial_for(target):
        nf = lax.dynamic_slice_in_dim(normed[0], target * own_rows, own_rows, axis=0)
        nb_ = lax.dynamic_slice_in_dim(normed[1], target * own_rows, own_rows, axis=0)
        out_f = jnp.dot(nf, w_out, preferred_element_type=f32)
        out_b = jnp.dot(nb_, w_out, preferred_element_type=f32)
        return out_f + flipped_columns(out_b, flip)

    received = []
    for d in range(1, peers):
        sent = partial_for((me + d) % peers)
        received.append(lax.ppermute(sent, "ch", [(i, (i + d) % peers) for i in range(peers)]))
    summed = partial_for(me)
    for r in received:
        summed = summed + r
    return summed.astype(bf16)


def solution(mesh):
    placed = (
        P(("ctx", "ch"), None),
        P(("ctx", "ch")),
        P(),
        P(None, "ch"),
        P(None, "ch"),
        P(),
        P(None, "ch"),
        P("ch"),
        P("ch"),
        P(None, "ch"),
        P(),
        P("ch"),
        P("ch"),
        P("ch", None),
    )
    return jax.shard_map(
        per_device, mesh=mesh, in_specs=placed, out_specs=P(("ctx", "ch"), None), check_vma=False
    )
```

```python
import jax
import jax.numpy as jnp
from jax import lax
from jax.sharding import PartitionSpec as P

HEAD_DIM = 64
GROUP = 128

exact_dot = lax.Precision.HIGHEST
norm_eps = 1e-05
f32 = jnp.float32
bf16 = jnp.bfloat16


def flip_matrix(n):
    rows = lax.broadcasted_iota(jnp.int32, (n, n), 0)
    cols = lax.broadcasted_iota(jnp.int32, (n, n), 1)
    return (rows + cols == n - 1).astype(bf16)


def shifted(block, axis, distance, parity=None):
    devices = range(lax.axis_size(axis))
    route = [
        (i, i + distance)
        for i in devices
        if i + distance in devices and (parity is None or i % 2 == parity)
    ]
    return lax.ppermute(block, axis, route)


def gather_rows(block, axis):
    peers, me = lax.axis_size(axis), lax.axis_index(axis)
    got = [block] + [
        lax.ppermute(block, axis, [(i, (i + d) % peers) for i in range(peers)])
        for d in range(peers - 1, 0, -1)
    ]
    stacked = jnp.stack(got)
    rolled = jnp.roll(stacked, me, axis=0)
    return rolled.reshape(peers * block.shape[0], *block.shape[1:])


def flipped_columns(part, flip):
    hi = part.astype(bf16)
    rest = part - hi.astype(f32)
    mid = rest.astype(bf16)
    lo = (rest - mid.astype(f32)).astype(bf16)
    rows = part.shape[0]
    pieces = jnp.dot(jnp.concatenate([hi, mid, lo], axis=0), flip, preferred_element_type=f32)
    return (pieces[:rows] + pieces[rows : 2 * rows]) + pieces[2 * rows :]


def conv_silu(raw, taps, rim, backward):
    conv = taps.shape[0]
    length = raw.shape[0]
    if backward:
        padded = jnp.concatenate([raw, rim], axis=0)
        summed = taps[0][None, :] * padded[conv - 1 : conv - 1 + length].astype(f32)
        for k in range(1, conv):
            start = conv - 1 - k
            summed = summed + taps[k][None, :] * padded[start : start + length].astype(f32)
    else:
        padded = jnp.concatenate([rim, raw], axis=0)
        summed = taps[0][None, :] * padded[0:length].astype(f32)
        for k in range(1, conv):
            summed = summed + taps[k][None, :] * padded[k : k + length].astype(f32)
    return jax.nn.silu(summed).astype(bf16)


def local_ssd(x, dt, b_mat, c_mat, rates, backward):
    length, inner = x.shape
    heads = dt.shape[1]
    nb = length // GROUP
    xb = x.reshape(nb, GROUP, heads, HEAD_DIM)
    dtb = dt.reshape(nb, GROUP, heads)
    bb = b_mat.reshape(nb, GROUP, -1)
    cb = c_mat.reshape(nb, GROUP, -1)
    step = -dtb * rates[None, None, :]
    cum = lax.cumsum(step, axis=1, reverse=backward)
    last = cum[:, 0, :] if backward else cum[:, -1, :]
    scores = jnp.einsum("kin,kjn->kij", cb, bb, preferred_element_type=f32)
    rows = lax.broadcasted_iota(jnp.int32, (GROUP, GROUP), 0)
    cols = lax.broadcasted_iota(jnp.int32, (GROUP, GROUP), 1)
    mask = (rows <= cols) if backward else (rows >= cols)
    mask = mask[None, None]
    cum_t = cum.transpose(0, 2, 1)
    gap = jnp.where(mask, cum_t[:, :, :, None] - cum_t[:, :, None, :], 0.0)
    dt_t = dtb.transpose(0, 2, 1)
    weights = jnp.where(mask, scores[:, None] * jnp.exp(gap) * dt_t[:, :, None, :], 0.0).astype(bf16)
    intra = jnp.einsum("khij,kjhp->kihp", weights, xb, preferred_element_type=f32)
    tail = jnp.exp(last[:, None, :] - cum) * dtb
    operand = (tail.transpose(0, 2, 1)[:, :, :, None] * bb.astype(f32)[:, None]).astype(bf16)
    block_state = jnp.einsum("khjn,kjhp->khpn", operand, xb, preferred_element_type=f32)
    block_decay = jnp.exp(last)
    return dict(xb=xb, cb=cb, cum=cum, intra=intra, block_state=block_state, block_decay=block_decay)


def stretch_states(parts, backward):
    block_state, block_decay = parts["block_state"], parts["block_decay"]
    nb = block_state.shape[0]
    order = list(range(nb - 1, -1, -1)) if backward else list(range(nb))
    starts = [None] * nb
    prefix = [None] * nb
    run_state = jnp.zeros_like(block_state[0])
    run_decay = jnp.ones_like(block_decay[0])
    for k in order:
        starts[k] = run_state
        prefix[k] = run_decay
        run_state = block_decay[k][:, None, None] * run_state + block_state[k]
        run_decay = run_decay * block_decay[k]
    return jnp.stack(starts), jnp.stack(prefix), run_state, run_decay


def pair_combine(earlier, later):
    (a0, s0), (a1, s1) = earlier, later
    return a1 * a0, a1[:, None, None] * s0 + s1


def scan_over(axis, own_decay, own_state, backward):
    peers = lax.axis_size(axis)
    step = -1 if backward else 1
    own = (own_decay, own_state)
    holder_parity = 0 if backward else 1
    first = shifted(own, axis, step, 1 - holder_parity)
    me = lax.axis_index(axis)
    holder = (me % 2 == 0) if backward else (me % 2 == 1)
    total = pair_combine(first, own)
    ex_decay = jnp.ones_like(own_decay)
    ex_state = jnp.zeros_like(own_state)
    in_decay, in_state = total
    distance = 2
    while distance < peers:
        got_decay, got_state = shifted((in_decay, in_state), axis, step * distance, holder_parity)
        ex_state = ex_decay[:, None, None] * got_state + ex_state
        ex_decay = ex_decay * got_decay
        if distance * 2 < peers:
            in_state = in_decay[:, None, None] * got_state + in_state
            in_decay = in_decay * got_decay
        distance *= 2
    handed = shifted(ex_state, axis, -step, holder_parity)
    mine = first[0][:, None, None] * ex_state + first[1]
    return jnp.where(holder, mine, handed)


def strand_output(parts, starts, prefix, carry, d_skip):
    start_states = starts + prefix[:, :, None, None] * carry[None]
    carried = jnp.einsum(
        "kin,khpn->kihp", parts["cb"].astype(f32), start_states, precision=exact_dot
    )
    xb = parts["xb"]
    y = (
        parts["intra"]
        + jnp.exp(parts["cum"])[:, :, :, None] * carried
        + d_skip[None, None, :, None] * xb.astype(f32)
    )
    nb, g, h, p = y.shape
    return y.reshape(nb * g, h * p)


def per_device(
    hidden,
    base_ids,
    embed,
    w_x,
    w_z,
    w_bc,
    w_dt,
    dt_bias,
    decay_rate,
    conv_x,
    conv_bc,
    d_skip,
    norm_gain,
    w_out,
):
    inner = w_x.shape[1]
    state = w_bc.shape[1] // 2
    conv = conv_x.shape[0]
    onehot = (base_ids[:, None] == jnp.arange(embed.shape[0], dtype=jnp.int32)[None, :]).astype(bf16)
    mixed_in = (hidden.astype(f32) + jnp.dot(onehot, embed, preferred_element_type=f32)).astype(bf16)
    u = gather_rows(mixed_in, "ch")
    length, width = u.shape
    flip = flip_matrix(width)
    u_flip = jnp.dot(u, flip, preferred_element_type=f32).astype(bf16)
    both = jnp.concatenate([u, u_flip], axis=0)
    x_raw = jnp.dot(both, w_x, preferred_element_type=f32).astype(bf16)
    z_all = jnp.dot(both, w_z, preferred_element_type=f32).astype(bf16)
    bc_raw = jnp.dot(both, w_bc, preferred_element_type=f32).astype(bf16)
    dt_all = jax.nn.softplus(jnp.dot(both, w_dt, preferred_element_type=f32) + dt_bias[None, :])

    outs = []
    sums = []
    for backward in (False, True):
        rows = slice(length, 2 * length) if backward else slice(0, length)
        xr, bcr = x_raw[rows], bc_raw[rows]
        if backward:
            rim_x = shifted(xr[: conv - 1], "ctx", -1)
            rim_bc = shifted(bcr[: conv - 1], "ctx", -1)
        else:
            rim_x = shifted(xr[length - conv + 1 :], "ctx", 1)
            rim_bc = shifted(bcr[length - conv + 1 :], "ctx", 1)
        x_c = conv_silu(xr, conv_x, rim_x, backward)
        bc_c = conv_silu(bcr, conv_bc, rim_bc, backward)
        parts = local_ssd(x_c, dt_all[rows], bc_c[:, :state], bc_c[:, state:], decay_rate, backward)
        starts, prefix, end_state, end_decay = stretch_states(parts, backward)
        carry = scan_over("ctx", end_decay, end_state, backward)
        y = strand_output(parts, starts, prefix, carry, d_skip)
        gated = (y * jax.nn.silu(z_all[rows].astype(f32))).astype(bf16).astype(f32)
        outs.append(gated)
        sums.append(jnp.sum(gated * gated, axis=1))
    total = lax.psum(jnp.stack(sums), "ch")
    full_inner = inner * lax.axis_size("ch")
    gain = norm_gain.astype(f32)[None, :]
    normed = [
        (g * lax.rsqrt(t / full_inner + norm_eps)[:, None] * gain).astype(bf16)
        for g, t in zip(outs, total)
    ]
    peers, me = lax.axis_size("ch"), lax.axis_index("ch")
    own_rows = length // peers

    def partial_for(target):
        nf = lax.dynamic_slice_in_dim(normed[0], target * own_rows, own_rows, axis=0)
        nb_ = lax.dynamic_slice_in_dim(normed[1], target * own_rows, own_rows, axis=0)
        out_f = jnp.dot(nf, w_out, preferred_element_type=f32)
        out_b = jnp.dot(nb_, w_out, preferred_element_type=f32)
        return out_f + flipped_columns(out_b, flip)

    received = []
    for d in range(1, peers):
        sent = partial_for((me + d) % peers)
        received.append(lax.ppermute(sent, "ch", [(i, (i + d) % peers) for i in range(peers)]))
    summed = partial_for(me)
    for r in received:
        summed = summed + r
    return summed.astype(bf16)


def solution(mesh):
    placed = (
        P(("ctx", "ch"), None),
        P(("ctx", "ch")),
        P(),
        P(None, "ch"),
        P(None, "ch"),
        P(),
        P(None, "ch"),
        P("ch"),
        P("ch"),
        P(None, "ch"),
        P(),
        P("ch"),
        P("ch"),
        P("ch", None),
    )
    return jax.shard_map(
        per_device, mesh=mesh, in_specs=placed, out_specs=P(("ctx", "ch"), None), check_vma=False
    )
```

```python
import jax
import jax.numpy as jnp
from jax import lax
from jax.sharding import PartitionSpec as P

HEAD_DIM = 64
GROUP = 128

exact_dot = lax.Precision.HIGHEST
norm_eps = 1e-05
f32 = jnp.float32
bf16 = jnp.bfloat16


def flip_matrix(n):
    rows = lax.broadcasted_iota(jnp.int32, (n, n), 0)
    cols = lax.broadcasted_iota(jnp.int32, (n, n), 1)
    return (rows + cols == n - 1).astype(bf16)


def shifted(block, axis, distance, parity=None):
    devices = range(lax.axis_size(axis))
    route = [
        (i, i + distance)
        for i in devices
        if i + distance in devices and (parity is None or i % 2 == parity)
    ]
    return lax.ppermute(block, axis, route)


def gather_rows(block, axis):
    peers, me = lax.axis_size(axis), lax.axis_index(axis)
    got = [block] + [
        lax.ppermute(block, axis, [(i, (i + d) % peers) for i in range(peers)])
        for d in range(peers - 1, 0, -1)
    ]
    stacked = jnp.stack(got)
    rolled = jnp.roll(stacked, me, axis=0)
    return rolled.reshape(peers * block.shape[0], *block.shape[1:])


def flipped_columns(part, flip):
    hi = part.astype(bf16)
    rest = part - hi.astype(f32)
    mid = rest.astype(bf16)
    lo = (rest - mid.astype(f32)).astype(bf16)
    rows = part.shape[0]
    pieces = jnp.dot(jnp.concatenate([hi, mid, lo], axis=0), flip, preferred_element_type=f32)
    return (pieces[:rows] + pieces[rows : 2 * rows]) + pieces[2 * rows :]


def conv_silu(raw, taps, rim, backward):
    conv = taps.shape[0]
    length = raw.shape[0]
    if backward:
        padded = jnp.concatenate([raw, rim], axis=0)
        summed = taps[0][None, :] * padded[conv - 1 : conv - 1 + length].astype(f32)
        for k in range(1, conv):
            start = conv - 1 - k
            summed = summed + taps[k][None, :] * padded[start : start + length].astype(f32)
    else:
        padded = jnp.concatenate([rim, raw], axis=0)
        summed = taps[0][None, :] * padded[0:length].astype(f32)
        for k in range(1, conv):
            summed = summed + taps[k][None, :] * padded[k : k + length].astype(f32)
    return jax.nn.silu(summed).astype(bf16)


def local_ssd(x, dt, b_mat, c_mat, rates, backward):
    length, inner = x.shape
    heads = dt.shape[1]
    nb = length // GROUP
    xb = x.reshape(nb, GROUP, heads, HEAD_DIM)
    dtb = dt.reshape(nb, GROUP, heads)
    bb = b_mat.reshape(nb, GROUP, -1)
    cb = c_mat.reshape(nb, GROUP, -1)
    step = -dtb * rates[None, None, :]
    cum = lax.cumsum(step, axis=1, reverse=backward)
    last = cum[:, 0, :] if backward else cum[:, -1, :]
    scores = jnp.einsum("kin,kjn->kij", cb, bb, preferred_element_type=f32)
    rows = lax.broadcasted_iota(jnp.int32, (GROUP, GROUP), 0)
    cols = lax.broadcasted_iota(jnp.int32, (GROUP, GROUP), 1)
    mask = (rows <= cols) if backward else (rows >= cols)
    mask = mask[None, None]
    cum_t = cum.transpose(0, 2, 1)
    gap = jnp.where(mask, cum_t[:, :, :, None] - cum_t[:, :, None, :], 0.0)
    dt_t = dtb.transpose(0, 2, 1)
    weights = jnp.where(mask, scores[:, None] * jnp.exp(gap) * dt_t[:, :, None, :], 0.0).astype(bf16)
    intra = jnp.einsum("khij,kjhp->kihp", weights, xb, preferred_element_type=f32)
    tail = jnp.exp(last[:, None, :] - cum) * dtb
    operand = (tail.transpose(0, 2, 1)[:, :, :, None] * bb.astype(f32)[:, None]).astype(bf16)
    block_state = jnp.einsum("khjn,kjhp->khpn", operand, xb, preferred_element_type=f32)
    block_decay = jnp.exp(last)
    return dict(xb=xb, cb=cb, cum=cum, intra=intra, block_state=block_state, block_decay=block_decay)


def stretch_states(parts, backward):
    block_state, block_decay = parts["block_state"], parts["block_decay"]
    nb = block_state.shape[0]
    order = list(range(nb - 1, -1, -1)) if backward else list(range(nb))
    starts = [None] * nb
    prefix = [None] * nb
    run_state = jnp.zeros_like(block_state[0])
    run_decay = jnp.ones_like(block_decay[0])
    for k in order:
        starts[k] = run_state
        prefix[k] = run_decay
        run_state = block_decay[k][:, None, None] * run_state + block_state[k]
        run_decay = run_decay * block_decay[k]
    return jnp.stack(starts), jnp.stack(prefix), run_state, run_decay


def pair_combine(earlier, later):
    (a0, s0), (a1, s1) = earlier, later
    return a1 * a0, a1[:, None, None] * s0 + s1


def scan_over(axis, own_decay, own_state, backward):
    peers = lax.axis_size(axis)
    step = -1 if backward else 1
    own = (own_decay, own_state)
    holder_parity = 0 if backward else 1
    first = shifted((own_decay, own_state.astype(bf16)), axis, step, 1 - holder_parity)
    first = (first[0], first[1].astype(f32))
    me = lax.axis_index(axis)
    holder = (me % 2 == 0) if backward else (me % 2 == 1)
    total = pair_combine(first, own)
    ex_decay = jnp.ones_like(own_decay)
    ex_state = jnp.zeros_like(own_state)
    in_decay, in_state = total
    distance = 2
    while distance < peers:
        got_decay, got_state = shifted(
            (in_decay, in_state.astype(bf16)), axis, step * distance, holder_parity
        )
        got_state = got_state.astype(f32)
        ex_state = ex_decay[:, None, None] * got_state + ex_state
        ex_decay = ex_decay * got_decay
        if distance * 2 < peers:
            in_state = in_decay[:, None, None] * got_state + in_state
            in_decay = in_decay * got_decay
        distance *= 2
    handed = shifted(ex_state.astype(bf16), axis, -step, holder_parity).astype(f32)
    mine = first[0][:, None, None] * ex_state + first[1]
    return jnp.where(holder, mine, handed)


def strand_output(parts, starts, prefix, carry, d_skip):
    start_states = starts + prefix[:, :, None, None] * carry[None]
    carried = jnp.einsum(
        "kin,khpn->kihp", parts["cb"].astype(f32), start_states, precision=exact_dot
    )
    xb = parts["xb"]
    y = (
        parts["intra"]
        + jnp.exp(parts["cum"])[:, :, :, None] * carried
        + d_skip[None, None, :, None] * xb.astype(f32)
    )
    nb, g, h, p = y.shape
    return y.reshape(nb * g, h * p)


def per_device(
    hidden,
    base_ids,
    embed,
    w_x,
    w_z,
    w_bc,
    w_dt,
    dt_bias,
    decay_rate,
    conv_x,
    conv_bc,
    d_skip,
    norm_gain,
    w_out,
):
    inner = w_x.shape[1]
    state = w_bc.shape[1] // 2
    conv = conv_x.shape[0]
    onehot = (base_ids[:, None] == jnp.arange(embed.shape[0], dtype=jnp.int32)[None, :]).astype(bf16)
    mixed_in = (hidden.astype(f32) + jnp.dot(onehot, embed, preferred_element_type=f32)).astype(bf16)
    u = gather_rows(mixed_in, "ch")
    length, width = u.shape
    flip = flip_matrix(width)
    u_flip = jnp.dot(u, flip, preferred_element_type=f32).astype(bf16)
    both = jnp.concatenate([u, u_flip], axis=0)
    x_raw = jnp.dot(both, w_x, preferred_element_type=f32).astype(bf16)
    z_all = jnp.dot(both, w_z, preferred_element_type=f32).astype(bf16)
    bc_raw = jnp.dot(both, w_bc, preferred_element_type=f32).astype(bf16)
    dt_all = jax.nn.softplus(jnp.dot(both, w_dt, preferred_element_type=f32) + dt_bias[None, :])

    outs = []
    sums = []
    for backward in (False, True):
        rows = slice(length, 2 * length) if backward else slice(0, length)
        xr, bcr = x_raw[rows], bc_raw[rows]
        if backward:
            rim_x = shifted(xr[: conv - 1], "ctx", -1)
            rim_bc = shifted(bcr[: conv - 1], "ctx", -1)
        else:
            rim_x = shifted(xr[length - conv + 1 :], "ctx", 1)
            rim_bc = shifted(bcr[length - conv + 1 :], "ctx", 1)
        x_c = conv_silu(xr, conv_x, rim_x, backward)
        bc_c = conv_silu(bcr, conv_bc, rim_bc, backward)
        parts = local_ssd(x_c, dt_all[rows], bc_c[:, :state], bc_c[:, state:], decay_rate, backward)
        starts, prefix, end_state, end_decay = stretch_states(parts, backward)
        carry = scan_over("ctx", end_decay, end_state, backward)
        y = strand_output(parts, starts, prefix, carry, d_skip)
        gated = (y * jax.nn.silu(z_all[rows].astype(f32))).astype(bf16).astype(f32)
        outs.append(gated)
        sums.append(jnp.sum(gated * gated, axis=1))
    total = lax.psum(jnp.stack(sums), "ch")
    full_inner = inner * lax.axis_size("ch")
    gain = norm_gain.astype(f32)[None, :]
    normed = [
        (g * lax.rsqrt(t / full_inner + norm_eps)[:, None] * gain).astype(bf16)
        for g, t in zip(outs, total)
    ]
    peers, me = lax.axis_size("ch"), lax.axis_index("ch")
    own_rows = length // peers

    def partial_for(target):
        nf = lax.dynamic_slice_in_dim(normed[0], target * own_rows, own_rows, axis=0)
        nb_ = lax.dynamic_slice_in_dim(normed[1], target * own_rows, own_rows, axis=0)
        out_f = jnp.dot(nf, w_out, preferred_element_type=f32)
        out_b = jnp.dot(nb_, w_out, preferred_element_type=f32)
        return out_f + flipped_columns(out_b, flip)

    received = []
    for d in range(1, peers):
        sent = partial_for((me + d) % peers)
        route = [(i, (i + d) % peers) for i in range(peers)]
        received.append(lax.ppermute(sent.astype(bf16), "ch", route))
    summed = partial_for(me)
    for r in received:
        summed = summed + r.astype(f32)
    return summed.astype(bf16)


def solution(mesh):
    placed = (
        P(("ctx", "ch"), None),
        P(("ctx", "ch")),
        P(),
        P(None, "ch"),
        P(None, "ch"),
        P(),
        P(None, "ch"),
        P("ch"),
        P("ch"),
        P(None, "ch"),
        P(),
        P("ch"),
        P("ch"),
        P("ch", None),
    )
    return jax.shard_map(
        per_device, mesh=mesh, in_specs=placed, out_specs=P(("ctx", "ch"), None), check_vma=False
    )
```

```python
import jax
import jax.numpy as jnp
from jax import lax
from jax.sharding import PartitionSpec as P

HEAD_DIM = 64
GROUP = 128

exact_dot = lax.Precision.HIGHEST
norm_eps = 1e-05
f32 = jnp.float32
bf16 = jnp.bfloat16


def flip_matrix(n):
    rows = lax.broadcasted_iota(jnp.int32, (n, n), 0)
    cols = lax.broadcasted_iota(jnp.int32, (n, n), 1)
    return (rows + cols == n - 1).astype(bf16)


def shifted(block, axis, distance, parity=None):
    devices = range(lax.axis_size(axis))
    route = [
        (i, i + distance)
        for i in devices
        if i + distance in devices and (parity is None or i % 2 == parity)
    ]
    return lax.ppermute(block, axis, route)


def gather_rows(block, axis):
    peers, me = lax.axis_size(axis), lax.axis_index(axis)
    got = [block] + [
        lax.ppermute(block, axis, [(i, (i + d) % peers) for i in range(peers)])
        for d in range(peers - 1, 0, -1)
    ]
    stacked = jnp.stack(got)
    rolled = jnp.roll(stacked, me, axis=0)
    return rolled.reshape(peers * block.shape[0], *block.shape[1:])


def flipped_columns(part, flip):
    hi = part.astype(bf16)
    rest = part - hi.astype(f32)
    mid = rest.astype(bf16)
    lo = (rest - mid.astype(f32)).astype(bf16)
    rows = part.shape[0]
    pieces = jnp.dot(jnp.concatenate([hi, mid, lo], axis=0), flip, preferred_element_type=f32)
    return (pieces[:rows] + pieces[rows : 2 * rows]) + pieces[2 * rows :]


def conv_silu(raw_ext, taps, rim, length, backward):
    conv = taps.shape[0]
    summed = None
    for k in range(conv):
        first = rim + conv - 1 - k if backward else rim - (conv - 1) + k
        term = taps[k][None, :] * raw_ext[first : first + length].astype(f32)
        summed = term if summed is None else summed + term
    return jax.nn.silu(summed).astype(bf16)


def local_ssd(x, dt, b_mat, c_mat, rates, backward):
    length, inner = x.shape
    heads = dt.shape[1]
    nb = length // GROUP
    xb = x.reshape(nb, GROUP, heads, HEAD_DIM)
    dtb = dt.reshape(nb, GROUP, heads)
    bb = b_mat.reshape(nb, GROUP, -1)
    cb = c_mat.reshape(nb, GROUP, -1)
    step = -dtb * rates[None, None, :]
    cum = lax.cumsum(step, axis=1, reverse=backward)
    last = cum[:, 0, :] if backward else cum[:, -1, :]
    scores = jnp.einsum("kin,kjn->kij", cb, bb, preferred_element_type=f32)
    rows = lax.broadcasted_iota(jnp.int32, (GROUP, GROUP), 0)
    cols = lax.broadcasted_iota(jnp.int32, (GROUP, GROUP), 1)
    mask = (rows <= cols) if backward else (rows >= cols)
    mask = mask[None, None]
    cum_t = cum.transpose(0, 2, 1)
    gap = jnp.where(mask, cum_t[:, :, :, None] - cum_t[:, :, None, :], 0.0)
    dt_t = dtb.transpose(0, 2, 1)
    weights = jnp.where(mask, scores[:, None] * jnp.exp(gap) * dt_t[:, :, None, :], 0.0).astype(bf16)
    intra = jnp.einsum("khij,kjhp->kihp", weights, xb, preferred_element_type=f32)
    tail = jnp.exp(last[:, None, :] - cum) * dtb
    operand = (tail.transpose(0, 2, 1)[:, :, :, None] * bb.astype(f32)[:, None]).astype(bf16)
    block_state = jnp.einsum("khjn,kjhp->khpn", operand, xb, preferred_element_type=f32)
    block_decay = jnp.exp(last)
    return dict(xb=xb, cb=cb, cum=cum, intra=intra, block_state=block_state, block_decay=block_decay)


def stretch_states(parts, backward):
    block_state, block_decay = parts["block_state"], parts["block_decay"]
    nb = block_state.shape[0]
    order = list(range(nb - 1, -1, -1)) if backward else list(range(nb))
    starts = [None] * nb
    prefix = [None] * nb
    run_state = jnp.zeros_like(block_state[0])
    run_decay = jnp.ones_like(block_decay[0])
    for k in order:
        starts[k] = run_state
        prefix[k] = run_decay
        run_state = block_decay[k][:, None, None] * run_state + block_state[k]
        run_decay = run_decay * block_decay[k]
    return jnp.stack(starts), jnp.stack(prefix), run_state, run_decay


def pair_combine(earlier, later):
    (a0, s0), (a1, s1) = earlier, later
    return a1 * a0, a1[:, None, None] * s0 + s1


def scan_over(axis, own_decay, own_state, backward):
    peers = lax.axis_size(axis)
    step = -1 if backward else 1
    own = (own_decay, own_state)
    holder_parity = 0 if backward else 1
    first = shifted((own_decay, own_state.astype(bf16)), axis, step, 1 - holder_parity)
    first = (first[0], first[1].astype(f32))
    me = lax.axis_index(axis)
    holder = (me % 2 == 0) if backward else (me % 2 == 1)
    total = pair_combine(first, own)
    ex_decay = jnp.ones_like(own_decay)
    ex_state = jnp.zeros_like(own_state)
    in_decay, in_state = total
    distance = 2
    while distance < peers:
        got_decay, got_state = shifted(
            (in_decay, in_state.astype(bf16)), axis, step * distance, holder_parity
        )
        got_state = got_state.astype(f32)
        ex_state = ex_decay[:, None, None] * got_state + ex_state
        ex_decay = ex_decay * got_decay
        if distance * 2 < peers:
            in_state = in_decay[:, None, None] * got_state + in_state
            in_decay = in_decay * got_decay
        distance *= 2
    handed = shifted(ex_state.astype(bf16), axis, -step, holder_parity).astype(f32)
    mine = first[0][:, None, None] * ex_state + first[1]
    return jnp.where(holder, mine, handed)


def strand_output(parts, starts, prefix, carry, d_skip):
    start_states = starts + prefix[:, :, None, None] * carry[None]
    carried = jnp.einsum(
        "kin,khpn->kihp", parts["cb"].astype(f32), start_states, precision=exact_dot
    )
    xb = parts["xb"]
    y = (
        parts["intra"]
        + jnp.exp(parts["cum"])[:, :, :, None] * carried
        + d_skip[None, None, :, None] * xb.astype(f32)
    )
    nb, g, h, p = y.shape
    return y.reshape(nb * g, h * p)


def per_device(
    hidden,
    base_ids,
    embed,
    w_x,
    w_z,
    w_bc,
    w_dt,
    dt_bias,
    decay_rate,
    conv_x,
    conv_bc,
    d_skip,
    norm_gain,
    w_out,
):
    inner = w_x.shape[1]
    state = w_bc.shape[1] // 2
    conv = conv_x.shape[0]
    onehot = (base_ids[:, None] == jnp.arange(embed.shape[0], dtype=jnp.int32)[None, :]).astype(bf16)
    mixed_in = (hidden.astype(f32) + jnp.dot(onehot, embed, preferred_element_type=f32)).astype(bf16)
    rim = 8
    peers = lax.axis_size("ch")
    both_axes = ("ctx", "ch")
    count = lax.axis_size(both_axes)
    before, after = [], []
    for h in range(peers):
        ahead = [(q, q + h + 1) for q in range(count) if q % peers == peers - 1 and q + h + 1 < count]
        behind = [(q, q - peers + h) for q in range(count) if q % peers == 0 and q - peers + h >= 0]
        before.append(lax.ppermute(mixed_in[-rim:], both_axes, ahead))
        after.append(lax.ppermute(mixed_in[:rim], both_axes, behind))
    me = lax.axis_index("ch")
    u = gather_rows(mixed_in, "ch")
    u_ext = jnp.concatenate(
        [
            jnp.stack(before)[me],
            u,
            jnp.stack(after)[me],
        ],
        axis=0,
    )
    length, width = u.shape
    flip = flip_matrix(width)
    u_ext_flip = jnp.dot(u_ext, flip, preferred_element_type=f32).astype(bf16)
    both_ext = jnp.concatenate([u_ext, u_ext_flip], axis=0)
    both = jnp.concatenate([u_ext[rim : rim + length], u_ext_flip[rim : rim + length]], axis=0)
    x_raw = jnp.dot(both_ext, w_x, preferred_element_type=f32).astype(bf16)
    bc_raw = jnp.dot(both_ext, w_bc, preferred_element_type=f32).astype(bf16)
    z_all = jnp.dot(both, w_z, preferred_element_type=f32).astype(bf16)
    dt_all = jax.nn.softplus(jnp.dot(both, w_dt, preferred_element_type=f32) + dt_bias[None, :])
    ext = length + 2 * rim

    outs = []
    sums = []
    for backward in (False, True):
        rows = slice(length, 2 * length) if backward else slice(0, length)
        ext_rows = slice(ext, 2 * ext) if backward else slice(0, ext)
        x_c = conv_silu(x_raw[ext_rows], conv_x, rim, length, backward)
        bc_c = conv_silu(bc_raw[ext_rows], conv_bc, rim, length, backward)
        parts = local_ssd(x_c, dt_all[rows], bc_c[:, :state], bc_c[:, state:], decay_rate, backward)
        starts, prefix, end_state, end_decay = stretch_states(parts, backward)
        carry = scan_over("ctx", end_decay, end_state, backward)
        y = strand_output(parts, starts, prefix, carry, d_skip)
        gated = (y * jax.nn.silu(z_all[rows].astype(f32))).astype(bf16).astype(f32)
        outs.append(gated)
        sums.append(jnp.sum(gated * gated, axis=1))
    total = lax.psum(jnp.stack(sums), "ch")
    full_inner = inner * lax.axis_size("ch")
    gain = norm_gain.astype(f32)[None, :]
    normed = [
        (g * lax.rsqrt(t / full_inner + norm_eps)[:, None] * gain).astype(bf16)
        for g, t in zip(outs, total)
    ]
    own_rows = length // peers

    def partial_for(target):
        nf = lax.dynamic_slice_in_dim(normed[0], target * own_rows, own_rows, axis=0)
        nb_ = lax.dynamic_slice_in_dim(normed[1], target * own_rows, own_rows, axis=0)
        out_f = jnp.dot(nf, w_out, preferred_element_type=f32)
        out_b = jnp.dot(nb_, w_out, preferred_element_type=f32)
        return out_f + flipped_columns(out_b, flip)

    received = []
    for d in range(1, peers):
        sent = partial_for((me + d) % peers)
        route = [(i, (i + d) % peers) for i in range(peers)]
        received.append(lax.ppermute(sent.astype(bf16), "ch", route))
    summed = partial_for(me)
    for r in received:
        summed = summed + r.astype(f32)
    return summed.astype(bf16)


def solution(mesh):
    placed = (
        P(("ctx", "ch"), None),
        P(("ctx", "ch")),
        P(),
        P(None, "ch"),
        P(None, "ch"),
        P(),
        P(None, "ch"),
        P("ch"),
        P("ch"),
        P(None, "ch"),
        P(),
        P("ch"),
        P("ch"),
        P("ch", None),
    )
    return jax.shard_map(
        per_device, mesh=mesh, in_specs=placed, out_specs=P(("ctx", "ch"), None), check_vma=False
    )
```

```python
import jax
import jax.numpy as jnp
from jax import lax
from jax.sharding import PartitionSpec as P

HEAD_DIM = 64
GROUP = 128

exact_dot = lax.Precision.HIGHEST
norm_eps = 1e-05
f32 = jnp.float32
bf16 = jnp.bfloat16


def flip_matrix(n):
    rows = lax.broadcasted_iota(jnp.int32, (n, n), 0)
    cols = lax.broadcasted_iota(jnp.int32, (n, n), 1)
    return (rows + cols == n - 1).astype(bf16)


def shifted(block, axis, distance, parity=None):
    devices = range(lax.axis_size(axis))
    route = [
        (i, i + distance)
        for i in devices
        if i + distance in devices and (parity is None or i % 2 == parity)
    ]
    return lax.ppermute(block, axis, route)


def gather_rows(block, axis):
    peers, me = lax.axis_size(axis), lax.axis_index(axis)
    got = [block] + [
        lax.ppermute(block, axis, [(i, (i + d) % peers) for i in range(peers)])
        for d in range(peers - 1, 0, -1)
    ]
    stacked = jnp.stack(got)
    rolled = jnp.roll(stacked, me, axis=0)
    return rolled.reshape(peers * block.shape[0], *block.shape[1:])


def flipped_columns(part, flip):
    hi = part.astype(bf16)
    rest = part - hi.astype(f32)
    mid = rest.astype(bf16)
    lo = (rest - mid.astype(f32)).astype(bf16)
    rows = part.shape[0]
    pieces = jnp.dot(jnp.concatenate([hi, mid, lo], axis=0), flip, preferred_element_type=f32)
    return (pieces[:rows] + pieces[rows : 2 * rows]) + pieces[2 * rows :]


def conv_silu(raw_ext, taps, rim, length, backward):
    conv = taps.shape[0]
    summed = None
    for k in range(conv):
        first = rim + conv - 1 - k if backward else rim - (conv - 1) + k
        term = taps[k][None, :] * raw_ext[first : first + length].astype(f32)
        summed = term if summed is None else summed + term
    return jax.nn.silu(summed).astype(bf16)


def head_spread(values, inner):
    heads = values.shape[-1]
    owner = lax.broadcasted_iota(jnp.int32, (heads, inner), 1) // HEAD_DIM
    spread = (owner == lax.broadcasted_iota(jnp.int32, (heads, inner), 0)).astype(f32)
    return jnp.dot(values, spread, precision=exact_dot)


def local_ssd(x, dt, b_mat, c_mat, rates, backward):
    length, inner = x.shape
    heads = dt.shape[1]
    nb = length // GROUP
    xb = x.reshape(nb, GROUP, heads, HEAD_DIM)
    dtb = dt.reshape(nb, GROUP, heads)
    bb = b_mat.reshape(nb, GROUP, -1)
    cb = c_mat.reshape(nb, GROUP, -1)
    step = -dtb * rates[None, None, :]
    cum = lax.cumsum(step, axis=1, reverse=backward)
    last = cum[:, 0, :] if backward else cum[:, -1, :]
    scores = jnp.einsum("kin,kjn->kij", cb, bb, preferred_element_type=f32)
    rows = lax.broadcasted_iota(jnp.int32, (GROUP, GROUP), 0)
    cols = lax.broadcasted_iota(jnp.int32, (GROUP, GROUP), 1)
    mask = (rows <= cols) if backward else (rows >= cols)
    mask = mask[None, None]
    cum_t = cum.transpose(0, 2, 1)
    gap = jnp.where(mask, cum_t[:, :, :, None] - cum_t[:, :, None, :], 0.0)
    dt_t = dtb.transpose(0, 2, 1)
    weights = jnp.where(mask, scores[:, None] * jnp.exp(gap) * dt_t[:, :, None, :], 0.0).astype(bf16)
    intra = jnp.einsum("khij,kjhp->kihp", weights, xb, preferred_element_type=f32)
    tail = jnp.exp(last[:, None, :] - cum) * dtb
    tail_wide = head_spread(tail.reshape(length, heads), inner).reshape(nb, GROUP, inner)
    scaled = x.reshape(nb, GROUP, inner).astype(f32) * tail_wide
    block_state = jnp.einsum("kjn,kjc->knc", bb.astype(f32), scaled, precision=exact_dot)
    block_decay = head_spread(jnp.exp(last), inner)
    cum_wide = head_spread(jnp.exp(cum).reshape(length, heads), inner)
    return dict(
        cb=cb,
        cum_wide=cum_wide,
        intra=intra.reshape(length, inner),
        block_state=block_state,
        block_decay=block_decay,
    )


def stretch_states(parts, backward):
    block_state, block_decay = parts["block_state"], parts["block_decay"]
    nb = block_state.shape[0]
    order = list(range(nb - 1, -1, -1)) if backward else list(range(nb))
    starts = [None] * nb
    prefix = [None] * nb
    run_state = jnp.zeros_like(block_state[0])
    run_decay = jnp.ones_like(block_decay[0])
    for k in order:
        starts[k] = run_state
        prefix[k] = run_decay
        run_state = block_decay[k][None, :] * run_state + block_state[k]
        run_decay = run_decay * block_decay[k]
    return jnp.stack(starts), jnp.stack(prefix), run_state, run_decay


def pair_combine(earlier, later):
    (a0, s0), (a1, s1) = earlier, later
    return a1 * a0, a1[None, :] * s0 + s1


def scan_over(axis, own_decay, own_state, backward):
    peers = lax.axis_size(axis)
    step = -1 if backward else 1
    own = (own_decay, own_state)
    holder_parity = 0 if backward else 1
    first = shifted((own_decay, own_state.astype(bf16)), axis, step, 1 - holder_parity)
    first = (first[0], first[1].astype(f32))
    me = lax.axis_index(axis)
    holder = (me % 2 == 0) if backward else (me % 2 == 1)
    total = pair_combine(first, own)
    ex_decay = jnp.ones_like(own_decay)
    ex_state = jnp.zeros_like(own_state)
    in_decay, in_state = total
    distance = 2
    while distance < peers:
        got_decay, got_state = shifted(
            (in_decay, in_state.astype(bf16)), axis, step * distance, holder_parity
        )
        got_state = got_state.astype(f32)
        ex_state = ex_decay[None, :] * got_state + ex_state
        ex_decay = ex_decay * got_decay
        if distance * 2 < peers:
            in_state = in_decay[None, :] * got_state + in_state
            in_decay = in_decay * got_decay
        distance *= 2
    handed = shifted(ex_state.astype(bf16), axis, -step, holder_parity).astype(f32)
    mine = first[0][None, :] * ex_state + first[1]
    return jnp.where(holder, mine, handed)


def strand_output(parts, starts, prefix, carry, x, d_wide):
    start_states = starts + prefix[:, None, :] * carry[None]
    carried = jnp.einsum(
        "kin,knc->kic", parts["cb"].astype(f32), start_states, precision=exact_dot
    )
    length, inner = x.shape
    carried = carried.reshape(length, inner)
    return parts["intra"] + parts["cum_wide"] * carried + d_wide[None, :] * x.astype(f32)


def per_device(
    hidden,
    base_ids,
    embed,
    w_x,
    w_z,
    w_bc,
    w_dt,
    dt_bias,
    decay_rate,
    conv_x,
    conv_bc,
    d_skip,
    norm_gain,
    w_out,
):
    inner = w_x.shape[1]
    state = w_bc.shape[1] // 2
    conv = conv_x.shape[0]
    onehot = (base_ids[:, None] == jnp.arange(embed.shape[0], dtype=jnp.int32)[None, :]).astype(bf16)
    mixed_in = (hidden.astype(f32) + jnp.dot(onehot, embed, preferred_element_type=f32)).astype(bf16)
    rim = 8
    peers = lax.axis_size("ch")
    both_axes = ("ctx", "ch")
    count = lax.axis_size(both_axes)
    before, after = [], []
    for h in range(peers):
        ahead = [(q, q + h + 1) for q in range(count) if q % peers == peers - 1 and q + h + 1 < count]
        behind = [(q, q - peers + h) for q in range(count) if q % peers == 0 and q - peers + h >= 0]
        before.append(lax.ppermute(mixed_in[-rim:], both_axes, ahead))
        after.append(lax.ppermute(mixed_in[:rim], both_axes, behind))
    me = lax.axis_index("ch")
    u = gather_rows(mixed_in, "ch")
    u_ext = jnp.concatenate(
        [
            jnp.stack(before)[me],
            u,
            jnp.stack(after)[me],
        ],
        axis=0,
    )
    length, width = u.shape
    flip = flip_matrix(width)
    u_ext_flip = jnp.dot(u_ext, flip, preferred_element_type=f32).astype(bf16)
    both_ext = jnp.concatenate([u_ext, u_ext_flip], axis=0)
    both = jnp.concatenate([u_ext[rim : rim + length], u_ext_flip[rim : rim + length]], axis=0)
    x_raw = jnp.dot(both_ext, w_x, preferred_element_type=f32).astype(bf16)
    bc_raw = jnp.dot(both_ext, w_bc, preferred_element_type=f32).astype(bf16)
    z_all = jnp.dot(both, w_z, preferred_element_type=f32).astype(bf16)
    dt_all = jax.nn.softplus(jnp.dot(both, w_dt, preferred_element_type=f32) + dt_bias[None, :])
    ext = length + 2 * rim
    d_wide = head_spread(d_skip[None, :], inner)[0]

    outs = []
    sums = []
    for backward in (False, True):
        rows = slice(length, 2 * length) if backward else slice(0, length)
        ext_rows = slice(ext, 2 * ext) if backward else slice(0, ext)
        x_c = conv_silu(x_raw[ext_rows], conv_x, rim, length, backward)
        bc_c = conv_silu(bc_raw[ext_rows], conv_bc, rim, length, backward)
        parts = local_ssd(x_c, dt_all[rows], bc_c[:, :state], bc_c[:, state:], decay_rate, backward)
        starts, prefix, end_state, end_decay = stretch_states(parts, backward)
        carry = scan_over("ctx", end_decay, end_state, backward)
        y = strand_output(parts, starts, prefix, carry, x_c, d_wide)
        gated = (y * jax.nn.silu(z_all[rows].astype(f32))).astype(bf16).astype(f32)
        outs.append(gated)
        sums.append(jnp.sum(gated * gated, axis=1))
    total = lax.psum(jnp.stack(sums), "ch")
    full_inner = inner * lax.axis_size("ch")
    gain = norm_gain.astype(f32)[None, :]
    normed = [
        (g * lax.rsqrt(t / full_inner + norm_eps)[:, None] * gain).astype(bf16)
        for g, t in zip(outs, total)
    ]
    own_rows = length // peers

    def partial_for(target):
        nf = lax.dynamic_slice_in_dim(normed[0], target * own_rows, own_rows, axis=0)
        nb_ = lax.dynamic_slice_in_dim(normed[1], target * own_rows, own_rows, axis=0)
        out_f = jnp.dot(nf, w_out, preferred_element_type=f32)
        out_b = jnp.dot(nb_, w_out, preferred_element_type=f32)
        return out_f + flipped_columns(out_b, flip)

    received = []
    for d in range(1, peers):
        sent = partial_for((me + d) % peers)
        route = [(i, (i + d) % peers) for i in range(peers)]
        received.append(lax.ppermute(sent.astype(bf16), "ch", route))
    summed = partial_for(me)
    for r in received:
        summed = summed + r.astype(f32)
    return summed.astype(bf16)


def solution(mesh):
    placed = (
        P(("ctx", "ch"), None),
        P(("ctx", "ch")),
        P(),
        P(None, "ch"),
        P(None, "ch"),
        P(),
        P(None, "ch"),
        P("ch"),
        P("ch"),
        P(None, "ch"),
        P(),
        P("ch"),
        P("ch"),
        P("ch", None),
    )
    return jax.shard_map(
        per_device, mesh=mesh, in_specs=placed, out_specs=P(("ctx", "ch"), None), check_vma=False
    )
```

```python
import jax
import jax.numpy as jnp
from jax import lax
from jax.experimental import pallas as pl
from jax.sharding import PartitionSpec as P

HEAD_DIM = 64
GROUP = 128

exact_dot = lax.Precision.HIGHEST
norm_eps = 1e-05
f32 = jnp.float32
bf16 = jnp.bfloat16


def flip_matrix(n):
    rows = lax.broadcasted_iota(jnp.int32, (n, n), 0)
    cols = lax.broadcasted_iota(jnp.int32, (n, n), 1)
    return (rows + cols == n - 1).astype(bf16)


def shifted(block, axis, distance, parity=None):
    devices = range(lax.axis_size(axis))
    route = [
        (i, i + distance)
        for i in devices
        if i + distance in devices and (parity is None or i % 2 == parity)
    ]
    return lax.ppermute(block, axis, route)


def gather_rows(block, axis):
    peers, me = lax.axis_size(axis), lax.axis_index(axis)
    got = [block] + [
        lax.ppermute(block, axis, [(i, (i + d) % peers) for i in range(peers)])
        for d in range(peers - 1, 0, -1)
    ]
    stacked = jnp.stack(got)
    rolled = jnp.roll(stacked, me, axis=0)
    return rolled.reshape(peers * block.shape[0], *block.shape[1:])


def flipped_columns(part, flip):
    hi = part.astype(bf16)
    rest = part - hi.astype(f32)
    mid = rest.astype(bf16)
    lo = (rest - mid.astype(f32)).astype(bf16)
    rows = part.shape[0]
    pieces = jnp.dot(jnp.concatenate([hi, mid, lo], axis=0), flip, preferred_element_type=f32)
    return (pieces[:rows] + pieces[rows : 2 * rows]) + pieces[2 * rows :]


def conv_silu(raw_ext, taps, rim, length, backward):
    conv = taps.shape[0]
    summed = None
    for k in range(conv):
        first = rim + conv - 1 - k if backward else rim - (conv - 1) + k
        term = taps[k][None, :] * raw_ext[first : first + length].astype(f32)
        summed = term if summed is None else summed + term
    return jax.nn.silu(summed).astype(bf16)


def intra_kernel(w_ref, x_ref, o_ref):
    lanes = 128
    per_tile = lanes // HEAD_DIM
    tiles = x_ref.shape[1] // lanes
    owner = lax.broadcasted_iota(jnp.int32, (x_ref.shape[0], lanes), 1) // HEAD_DIM

    def body(g, carry):
        cols = pl.ds(pl.multiple_of(g * lanes, lanes), lanes)
        tile = x_ref[:, cols]
        acc = jnp.zeros((x_ref.shape[0], lanes), f32)
        for t in range(per_tile):
            picked = jnp.where(owner == t, tile, jnp.zeros_like(tile))
            acc = acc + jnp.dot(w_ref[0, g * per_tile + t], picked, preferred_element_type=f32)
        o_ref[:, cols] = acc
        return carry

    lax.fori_loop(0, tiles, body, 0)


def intra_block(weights, x):
    nb, heads, group, _ = weights.shape
    length, inner = x.shape
    return pl.pallas_call(
        intra_kernel,
        out_shape=jax.ShapeDtypeStruct((length, inner), f32),
        grid=(nb,),
        in_specs=[
            pl.BlockSpec((1, heads, group, group), lambda k: (k, 0, 0, 0)),
            pl.BlockSpec((group, inner), lambda k: (k, 0)),
        ],
        out_specs=pl.BlockSpec((group, inner), lambda k: (k, 0)),
    )(weights, x)


def head_spread(values, inner):
    heads = values.shape[-1]
    owner = lax.broadcasted_iota(jnp.int32, (heads, inner), 1) // HEAD_DIM
    spread = (owner == lax.broadcasted_iota(jnp.int32, (heads, inner), 0)).astype(f32)
    return jnp.dot(values, spread, precision=exact_dot)


def local_ssd(x, dt, b_mat, c_mat, rates, backward):
    length, inner = x.shape
    heads = dt.shape[1]
    nb = length // GROUP
    xb = x.reshape(nb, GROUP, heads, HEAD_DIM)
    dtb = dt.reshape(nb, GROUP, heads)
    bb = b_mat.reshape(nb, GROUP, -1)
    cb = c_mat.reshape(nb, GROUP, -1)
    step = -dtb * rates[None, None, :]
    cum = lax.cumsum(step, axis=1, reverse=backward)
    last = cum[:, 0, :] if backward else cum[:, -1, :]
    scores = jnp.einsum("kin,kjn->kij", cb, bb, preferred_element_type=f32)
    rows = lax.broadcasted_iota(jnp.int32, (GROUP, GROUP), 0)
    cols = lax.broadcasted_iota(jnp.int32, (GROUP, GROUP), 1)
    mask = (rows <= cols) if backward else (rows >= cols)
    mask = mask[None, None]
    cum_t = cum.transpose(0, 2, 1)
    gap = jnp.where(mask, cum_t[:, :, :, None] - cum_t[:, :, None, :], 0.0)
    dt_t = dtb.transpose(0, 2, 1)
    weights = jnp.where(mask, scores[:, None] * jnp.exp(gap) * dt_t[:, :, None, :], 0.0).astype(bf16)
    intra = intra_block(weights, x)
    tail = jnp.exp(last[:, None, :] - cum) * dtb
    tail_wide = head_spread(tail.reshape(length, heads), inner).reshape(nb, GROUP, inner)
    scaled = x.reshape(nb, GROUP, inner).astype(f32) * tail_wide
    block_state = jnp.einsum("kjn,kjc->knc", bb.astype(f32), scaled, precision=exact_dot)
    block_decay = head_spread(jnp.exp(last), inner)
    cum_wide = head_spread(jnp.exp(cum).reshape(length, heads), inner)
    return dict(
        cb=cb,
        cum_wide=cum_wide,
        intra=intra,
        block_state=block_state,
        block_decay=block_decay,
    )


def stretch_states(parts, backward):
    block_state, block_decay = parts["block_state"], parts["block_decay"]
    nb = block_state.shape[0]
    order = list(range(nb - 1, -1, -1)) if backward else list(range(nb))
    starts = [None] * nb
    prefix = [None] * nb
    run_state = jnp.zeros_like(block_state[0])
    run_decay = jnp.ones_like(block_decay[0])
    for k in order:
        starts[k] = run_state
        prefix[k] = run_decay
        run_state = block_decay[k][None, :] * run_state + block_state[k]
        run_decay = run_decay * block_decay[k]
    return jnp.stack(starts), jnp.stack(prefix), run_state, run_decay


def pair_combine(earlier, later):
    (a0, s0), (a1, s1) = earlier, later
    return a1 * a0, a1[None, :] * s0 + s1


def scan_over(axis, own_decay, own_state, backward):
    peers = lax.axis_size(axis)
    step = -1 if backward else 1
    own = (own_decay, own_state)
    holder_parity = 0 if backward else 1
    first = shifted((own_decay, own_state.astype(bf16)), axis, step, 1 - holder_parity)
    first = (first[0], first[1].astype(f32))
    me = lax.axis_index(axis)
    holder = (me % 2 == 0) if backward else (me % 2 == 1)
    total = pair_combine(first, own)
    ex_decay = jnp.ones_like(own_decay)
    ex_state = jnp.zeros_like(own_state)
    in_decay, in_state = total
    distance = 2
    while distance < peers:
        got_decay, got_state = shifted(
            (in_decay, in_state.astype(bf16)), axis, step * distance, holder_parity
        )
        got_state = got_state.astype(f32)
        ex_state = ex_decay[None, :] * got_state + ex_state
        ex_decay = ex_decay * got_decay
        if distance * 2 < peers:
            in_state = in_decay[None, :] * got_state + in_state
            in_decay = in_decay * got_decay
        distance *= 2
    handed = shifted(ex_state.astype(bf16), axis, -step, holder_parity).astype(f32)
    mine = first[0][None, :] * ex_state + first[1]
    return jnp.where(holder, mine, handed)


def strand_output(parts, starts, prefix, carry, x, d_wide):
    start_states = starts + prefix[:, None, :] * carry[None]
    carried = jnp.einsum(
        "kin,knc->kic", parts["cb"].astype(f32), start_states, precision=exact_dot
    )
    length, inner = x.shape
    carried = carried.reshape(length, inner)
    return parts["intra"] + parts["cum_wide"] * carried + d_wide[None, :] * x.astype(f32)


def per_device(
    hidden,
    base_ids,
    embed,
    w_x,
    w_z,
    w_bc,
    w_dt,
    dt_bias,
    decay_rate,
    conv_x,
    conv_bc,
    d_skip,
    norm_gain,
    w_out,
):
    inner = w_x.shape[1]
    state = w_bc.shape[1] // 2
    conv = conv_x.shape[0]
    onehot = (base_ids[:, None] == jnp.arange(embed.shape[0], dtype=jnp.int32)[None, :]).astype(bf16)
    mixed_in = (hidden.astype(f32) + jnp.dot(onehot, embed, preferred_element_type=f32)).astype(bf16)
    rim = 8
    peers = lax.axis_size("ch")
    both_axes = ("ctx", "ch")
    count = lax.axis_size(both_axes)
    before, after = [], []
    for h in range(peers):
        ahead = [(q, q + h + 1) for q in range(count) if q % peers == peers - 1 and q + h + 1 < count]
        behind = [(q, q - peers + h) for q in range(count) if q % peers == 0 and q - peers + h >= 0]
        before.append(lax.ppermute(mixed_in[-rim:], both_axes, ahead))
        after.append(lax.ppermute(mixed_in[:rim], both_axes, behind))
    me = lax.axis_index("ch")
    u = gather_rows(mixed_in, "ch")
    u_ext = jnp.concatenate(
        [
            jnp.stack(before)[me],
            u,
            jnp.stack(after)[me],
        ],
        axis=0,
    )
    length, width = u.shape
    flip = flip_matrix(width)
    u_ext_flip = jnp.dot(u_ext, flip, preferred_element_type=f32).astype(bf16)
    both_ext = jnp.concatenate([u_ext, u_ext_flip], axis=0)
    both = jnp.concatenate([u_ext[rim : rim + length], u_ext_flip[rim : rim + length]], axis=0)
    x_raw = jnp.dot(both_ext, w_x, preferred_element_type=f32).astype(bf16)
    bc_raw = jnp.dot(both_ext, w_bc, preferred_element_type=f32).astype(bf16)
    z_all = jnp.dot(both, w_z, preferred_element_type=f32).astype(bf16)
    dt_all = jax.nn.softplus(jnp.dot(both, w_dt, preferred_element_type=f32) + dt_bias[None, :])
    ext = length + 2 * rim
    d_wide = head_spread(d_skip[None, :], inner)[0]

    outs = []
    sums = []
    for backward in (False, True):
        rows = slice(length, 2 * length) if backward else slice(0, length)
        ext_rows = slice(ext, 2 * ext) if backward else slice(0, ext)
        x_c = conv_silu(x_raw[ext_rows], conv_x, rim, length, backward)
        bc_c = conv_silu(bc_raw[ext_rows], conv_bc, rim, length, backward)
        parts = local_ssd(x_c, dt_all[rows], bc_c[:, :state], bc_c[:, state:], decay_rate, backward)
        starts, prefix, end_state, end_decay = stretch_states(parts, backward)
        carry = scan_over("ctx", end_decay, end_state, backward)
        y = strand_output(parts, starts, prefix, carry, x_c, d_wide)
        gated = (y * jax.nn.silu(z_all[rows].astype(f32))).astype(bf16).astype(f32)
        outs.append(gated)
        sums.append(jnp.sum(gated * gated, axis=1))
    total = lax.psum(jnp.stack(sums), "ch")
    full_inner = inner * lax.axis_size("ch")
    gain = norm_gain.astype(f32)[None, :]
    normed = [
        (g * lax.rsqrt(t / full_inner + norm_eps)[:, None] * gain).astype(bf16)
        for g, t in zip(outs, total)
    ]
    own_rows = length // peers

    def partial_for(target):
        nf = lax.dynamic_slice_in_dim(normed[0], target * own_rows, own_rows, axis=0)
        nb_ = lax.dynamic_slice_in_dim(normed[1], target * own_rows, own_rows, axis=0)
        out_f = jnp.dot(nf, w_out, preferred_element_type=f32)
        out_b = jnp.dot(nb_, w_out, preferred_element_type=f32)
        return out_f + flipped_columns(out_b, flip)

    received = []
    for d in range(1, peers):
        sent = partial_for((me + d) % peers)
        route = [(i, (i + d) % peers) for i in range(peers)]
        received.append(lax.ppermute(sent.astype(bf16), "ch", route))
    summed = partial_for(me)
    for r in received:
        summed = summed + r.astype(f32)
    return summed.astype(bf16)


def solution(mesh):
    placed = (
        P(("ctx", "ch"), None),
        P(("ctx", "ch")),
        P(),
        P(None, "ch"),
        P(None, "ch"),
        P(),
        P(None, "ch"),
        P("ch"),
        P("ch"),
        P(None, "ch"),
        P(),
        P("ch"),
        P("ch"),
        P("ch", None),
    )
    return jax.shard_map(
        per_device, mesh=mesh, in_specs=placed, out_specs=P(("ctx", "ch"), None), check_vma=False
    )
```

```python
import jax
import jax.numpy as jnp
from jax import lax
from jax.experimental import pallas as pl
from jax.sharding import PartitionSpec as P

HEAD_DIM = 64
GROUP = 128

exact_dot = lax.Precision.HIGHEST
norm_eps = 1e-05
f32 = jnp.float32
bf16 = jnp.bfloat16


def flip_matrix(n):
    rows = lax.broadcasted_iota(jnp.int32, (n, n), 0)
    cols = lax.broadcasted_iota(jnp.int32, (n, n), 1)
    return (rows + cols == n - 1).astype(bf16)


def shifted(block, axis, distance, parity=None):
    devices = range(lax.axis_size(axis))
    route = [
        (i, i + distance)
        for i in devices
        if i + distance in devices and (parity is None or i % 2 == parity)
    ]
    return lax.ppermute(block, axis, route)


def gather_rows(block, axis):
    peers, me = lax.axis_size(axis), lax.axis_index(axis)
    got = [block] + [
        lax.ppermute(block, axis, [(i, (i + d) % peers) for i in range(peers)])
        for d in range(peers - 1, 0, -1)
    ]
    stacked = jnp.stack(got)
    rolled = jnp.roll(stacked, me, axis=0)
    return rolled.reshape(peers * block.shape[0], *block.shape[1:])


def flipped_columns(part, flip):
    hi = part.astype(bf16)
    rest = part - hi.astype(f32)
    mid = rest.astype(bf16)
    lo = (rest - mid.astype(f32)).astype(bf16)
    rows = part.shape[0]
    pieces = jnp.dot(jnp.concatenate([hi, mid, lo], axis=0), flip, preferred_element_type=f32)
    return (pieces[:rows] + pieces[rows : 2 * rows]) + pieces[2 * rows :]


def conv_silu(raw_ext, taps, rim, length, backward):
    conv = taps.shape[0]
    summed = None
    for k in range(conv):
        first = rim + conv - 1 - k if backward else rim - (conv - 1) + k
        term = taps[k][None, :] * raw_ext[first : first + length].astype(f32)
        summed = term if summed is None else summed + term
    return jax.nn.silu(summed).astype(bf16)


def intra_kernel(w_ref, x_ref, o_ref):
    lanes = 128
    per_tile = lanes // HEAD_DIM
    rows = x_ref.shape[0]
    owner = lax.broadcasted_iota(jnp.int32, (rows, lanes), 1) // HEAD_DIM
    for g in range(x_ref.shape[1] // lanes):
        tile = x_ref[:, g * lanes : (g + 1) * lanes]
        zero = jnp.zeros_like(tile)
        stacked = jnp.concatenate([jnp.where(owner == t, tile, zero) for t in range(per_tile)], axis=0)
        wide = jnp.concatenate([w_ref[0, g * per_tile + t] for t in range(per_tile)], axis=1)
        o_ref[:, g * lanes : (g + 1) * lanes] = jnp.dot(wide, stacked, preferred_element_type=f32)


def intra_block(weights, x):
    nb, heads, group, _ = weights.shape
    length, inner = x.shape
    return pl.pallas_call(
        intra_kernel,
        out_shape=jax.ShapeDtypeStruct((length, inner), f32),
        grid=(nb,),
        in_specs=[
            pl.BlockSpec((1, heads, group, group), lambda k: (k, 0, 0, 0)),
            pl.BlockSpec((group, inner), lambda k: (k, 0)),
        ],
        out_specs=pl.BlockSpec((group, inner), lambda k: (k, 0)),
    )(weights, x)


def head_spread(values, inner):
    heads = values.shape[-1]
    owner = lax.broadcasted_iota(jnp.int32, (heads, inner), 1) // HEAD_DIM
    spread = (owner == lax.broadcasted_iota(jnp.int32, (heads, inner), 0)).astype(f32)
    return jnp.dot(values, spread, precision=exact_dot)


def local_ssd(x, dt, b_mat, c_mat, rates, backward):
    length, inner = x.shape
    heads = dt.shape[1]
    nb = length // GROUP
    xb = x.reshape(nb, GROUP, heads, HEAD_DIM)
    dtb = dt.reshape(nb, GROUP, heads)
    bb = b_mat.reshape(nb, GROUP, -1)
    cb = c_mat.reshape(nb, GROUP, -1)
    step = -dtb * rates[None, None, :]
    cum = lax.cumsum(step, axis=1, reverse=backward)
    last = cum[:, 0, :] if backward else cum[:, -1, :]
    scores = jnp.einsum("kin,kjn->kij", cb, bb, preferred_element_type=f32)
    rows = lax.broadcasted_iota(jnp.int32, (GROUP, GROUP), 0)
    cols = lax.broadcasted_iota(jnp.int32, (GROUP, GROUP), 1)
    mask = (rows <= cols) if backward else (rows >= cols)
    mask = mask[None, None]
    cum_t = cum.transpose(0, 2, 1)
    gap = jnp.where(mask, cum_t[:, :, :, None] - cum_t[:, :, None, :], 0.0)
    dt_t = dtb.transpose(0, 2, 1)
    weights = jnp.where(mask, scores[:, None] * jnp.exp(gap) * dt_t[:, :, None, :], 0.0).astype(bf16)
    intra = intra_block(weights, x)
    tail = jnp.exp(last[:, None, :] - cum) * dtb
    tail_wide = head_spread(tail.reshape(length, heads), inner).reshape(nb, GROUP, inner)
    scaled = x.reshape(nb, GROUP, inner).astype(f32) * tail_wide
    block_state = jnp.einsum("kjn,kjc->knc", bb.astype(f32), scaled, precision=exact_dot)
    block_decay = head_spread(jnp.exp(last), inner)
    cum_wide = head_spread(jnp.exp(cum).reshape(length, heads), inner)
    return dict(
        cb=cb,
        cum_wide=cum_wide,
        intra=intra,
        block_state=block_state,
        block_decay=block_decay,
    )


def stretch_states(parts, backward):
    block_state, block_decay = parts["block_state"], parts["block_decay"]
    nb = block_state.shape[0]
    order = list(range(nb - 1, -1, -1)) if backward else list(range(nb))
    starts = [None] * nb
    prefix = [None] * nb
    run_state = jnp.zeros_like(block_state[0])
    run_decay = jnp.ones_like(block_decay[0])
    for k in order:
        starts[k] = run_state
        prefix[k] = run_decay
        run_state = block_decay[k][None, :] * run_state + block_state[k]
        run_decay = run_decay * block_decay[k]
    return jnp.stack(starts), jnp.stack(prefix), run_state, run_decay


def pair_combine(earlier, later):
    (a0, s0), (a1, s1) = earlier, later
    return a1 * a0, a1[None, :] * s0 + s1


def scan_over(axis, own_decay, own_state, backward):
    peers = lax.axis_size(axis)
    step = -1 if backward else 1
    own = (own_decay, own_state)
    holder_parity = 0 if backward else 1
    first = shifted((own_decay, own_state.astype(bf16)), axis, step, 1 - holder_parity)
    first = (first[0], first[1].astype(f32))
    me = lax.axis_index(axis)
    holder = (me % 2 == 0) if backward else (me % 2 == 1)
    total = pair_combine(first, own)
    ex_decay = jnp.ones_like(own_decay)
    ex_state = jnp.zeros_like(own_state)
    in_decay, in_state = total
    distance = 2
    while distance < peers:
        got_decay, got_state = shifted(
            (in_decay, in_state.astype(bf16)), axis, step * distance, holder_parity
        )
        got_state = got_state.astype(f32)
        ex_state = ex_decay[None, :] * got_state + ex_state
        ex_decay = ex_decay * got_decay
        if distance * 2 < peers:
            in_state = in_decay[None, :] * got_state + in_state
            in_decay = in_decay * got_decay
        distance *= 2
    handed = shifted(ex_state.astype(bf16), axis, -step, holder_parity).astype(f32)
    mine = first[0][None, :] * ex_state + first[1]
    return jnp.where(holder, mine, handed)


def strand_output(parts, starts, prefix, carry, x, d_wide):
    start_states = starts + prefix[:, None, :] * carry[None]
    carried = jnp.einsum(
        "kin,knc->kic", parts["cb"].astype(f32), start_states, precision=exact_dot
    )
    length, inner = x.shape
    carried = carried.reshape(length, inner)
    return parts["intra"] + parts["cum_wide"] * carried + d_wide[None, :] * x.astype(f32)


def per_device(
    hidden,
    base_ids,
    embed,
    w_x,
    w_z,
    w_bc,
    w_dt,
    dt_bias,
    decay_rate,
    conv_x,
    conv_bc,
    d_skip,
    norm_gain,
    w_out,
):
    inner = w_x.shape[1]
    state = w_bc.shape[1] // 2
    conv = conv_x.shape[0]
    onehot = (base_ids[:, None] == jnp.arange(embed.shape[0], dtype=jnp.int32)[None, :]).astype(bf16)
    mixed_in = (hidden.astype(f32) + jnp.dot(onehot, embed, preferred_element_type=f32)).astype(bf16)
    rim = 8
    peers = lax.axis_size("ch")
    both_axes = ("ctx", "ch")
    count = lax.axis_size(both_axes)
    before, after = [], []
    for h in range(peers):
        ahead = [(q, q + h + 1) for q in range(count) if q % peers == peers - 1 and q + h + 1 < count]
        behind = [(q, q - peers + h) for q in range(count) if q % peers == 0 and q - peers + h >= 0]
        before.append(lax.ppermute(mixed_in[-rim:], both_axes, ahead))
        after.append(lax.ppermute(mixed_in[:rim], both_axes, behind))
    me = lax.axis_index("ch")
    u = gather_rows(mixed_in, "ch")
    u_ext = jnp.concatenate(
        [
            jnp.stack(before)[me],
            u,
            jnp.stack(after)[me],
        ],
        axis=0,
    )
    length, width = u.shape
    flip = flip_matrix(width)
    u_ext_flip = jnp.dot(u_ext, flip, preferred_element_type=f32).astype(bf16)
    both_ext = jnp.concatenate([u_ext, u_ext_flip], axis=0)
    both = jnp.concatenate([u_ext[rim : rim + length], u_ext_flip[rim : rim + length]], axis=0)
    x_raw = jnp.dot(both_ext, w_x, preferred_element_type=f32).astype(bf16)
    bc_raw = jnp.dot(both_ext, w_bc, preferred_element_type=f32).astype(bf16)
    z_all = jnp.dot(both, w_z, preferred_element_type=f32).astype(bf16)
    dt_all = jax.nn.softplus(jnp.dot(both, w_dt, preferred_element_type=f32) + dt_bias[None, :])
    ext = length + 2 * rim
    d_wide = head_spread(d_skip[None, :], inner)[0]

    outs = []
    sums = []
    for backward in (False, True):
        rows = slice(length, 2 * length) if backward else slice(0, length)
        ext_rows = slice(ext, 2 * ext) if backward else slice(0, ext)
        x_c = conv_silu(x_raw[ext_rows], conv_x, rim, length, backward)
        bc_c = conv_silu(bc_raw[ext_rows], conv_bc, rim, length, backward)
        parts = local_ssd(x_c, dt_all[rows], bc_c[:, :state], bc_c[:, state:], decay_rate, backward)
        starts, prefix, end_state, end_decay = stretch_states(parts, backward)
        carry = scan_over("ctx", end_decay, end_state, backward)
        y = strand_output(parts, starts, prefix, carry, x_c, d_wide)
        gated = (y * jax.nn.silu(z_all[rows].astype(f32))).astype(bf16).astype(f32)
        outs.append(gated)
        sums.append(jnp.sum(gated * gated, axis=1))
    total = lax.psum(jnp.stack(sums), "ch")
    full_inner = inner * lax.axis_size("ch")
    gain = norm_gain.astype(f32)[None, :]
    normed = [
        (g * lax.rsqrt(t / full_inner + norm_eps)[:, None] * gain).astype(bf16)
        for g, t in zip(outs, total)
    ]
    own_rows = length // peers

    def partial_for(target):
        nf = lax.dynamic_slice_in_dim(normed[0], target * own_rows, own_rows, axis=0)
        nb_ = lax.dynamic_slice_in_dim(normed[1], target * own_rows, own_rows, axis=0)
        out_f = jnp.dot(nf, w_out, preferred_element_type=f32)
        out_b = jnp.dot(nb_, w_out, preferred_element_type=f32)
        return out_f + flipped_columns(out_b, flip)

    received = []
    for d in range(1, peers):
        sent = partial_for((me + d) % peers)
        route = [(i, (i + d) % peers) for i in range(peers)]
        received.append(lax.ppermute(sent.astype(bf16), "ch", route))
    summed = partial_for(me)
    for r in received:
        summed = summed + r.astype(f32)
    return summed.astype(bf16)


def solution(mesh):
    placed = (
        P(("ctx", "ch"), None),
        P(("ctx", "ch")),
        P(),
        P(None, "ch"),
        P(None, "ch"),
        P(),
        P(None, "ch"),
        P("ch"),
        P("ch"),
        P(None, "ch"),
        P(),
        P("ch"),
        P("ch"),
        P("ch", None),
    )
    return jax.shard_map(
        per_device, mesh=mesh, in_specs=placed, out_specs=P(("ctx", "ch"), None), check_vma=False
    )
```

```python
import jax
import jax.numpy as jnp
from jax import lax
from jax.experimental import pallas as pl
from jax.sharding import PartitionSpec as P

HEAD_DIM = 64
GROUP = 128

exact_dot = lax.Precision.HIGHEST
norm_eps = 1e-05
f32 = jnp.float32
bf16 = jnp.bfloat16


def flip_matrix(n):
    rows = lax.broadcasted_iota(jnp.int32, (n, n), 0)
    cols = lax.broadcasted_iota(jnp.int32, (n, n), 1)
    return (rows + cols == n - 1).astype(bf16)


def shifted(block, axis, distance, parity=None):
    devices = range(lax.axis_size(axis))
    route = [
        (i, i + distance)
        for i in devices
        if i + distance in devices and (parity is None or i % 2 == parity)
    ]
    return lax.ppermute(block, axis, route)


def gather_rows(block, axis):
    peers, me = lax.axis_size(axis), lax.axis_index(axis)
    got = [block] + [
        lax.ppermute(block, axis, [(i, (i + d) % peers) for i in range(peers)])
        for d in range(peers - 1, 0, -1)
    ]
    stacked = jnp.stack(got)
    rolled = jnp.roll(stacked, me, axis=0)
    return rolled.reshape(peers * block.shape[0], *block.shape[1:])


def flipped_columns(part, flip):
    hi = part.astype(bf16)
    rest = part - hi.astype(f32)
    mid = rest.astype(bf16)
    lo = (rest - mid.astype(f32)).astype(bf16)
    rows = part.shape[0]
    pieces = jnp.dot(jnp.concatenate([hi, mid, lo], axis=0), flip, preferred_element_type=f32)
    return (pieces[:rows] + pieces[rows : 2 * rows]) + pieces[2 * rows :]


def conv_silu(raw_ext, taps, rim, length, backward):
    conv = taps.shape[0]
    summed = None
    for k in range(conv):
        first = rim + conv - 1 - k if backward else rim - (conv - 1) + k
        term = taps[k][None, :] * raw_ext[first : first + length].astype(f32)
        summed = term if summed is None else summed + term
    return jax.nn.silu(summed).astype(bf16)


def intra_kernel(w_ref, x_ref, o_ref):
    lanes = 128
    per_tile = lanes // HEAD_DIM
    rows = x_ref.shape[0]
    owner = lax.broadcasted_iota(jnp.int32, (rows, lanes), 1) // HEAD_DIM
    for g in range(x_ref.shape[1] // lanes):
        tile = x_ref[:, g * lanes : (g + 1) * lanes]
        zero = jnp.zeros_like(tile)
        stacked = jnp.concatenate([jnp.where(owner == t, tile, zero) for t in range(per_tile)], axis=0)
        wide = jnp.concatenate([w_ref[0, g * per_tile + t] for t in range(per_tile)], axis=1)
        o_ref[:, g * lanes : (g + 1) * lanes] = jnp.dot(wide, stacked, preferred_element_type=f32)


def intra_block(weights, x):
    nb, heads, group, _ = weights.shape
    length, inner = x.shape
    return pl.pallas_call(
        intra_kernel,
        out_shape=jax.ShapeDtypeStruct((length, inner), f32),
        grid=(nb,),
        in_specs=[
            pl.BlockSpec((1, heads, group, group), lambda k: (k, 0, 0, 0)),
            pl.BlockSpec((group, inner), lambda k: (k, 0)),
        ],
        out_specs=pl.BlockSpec((group, inner), lambda k: (k, 0)),
    )(weights, x)


def head_spread(values, inner):
    heads = values.shape[-1]
    owner = lax.broadcasted_iota(jnp.int32, (heads, inner), 1) // HEAD_DIM
    spread = (owner == lax.broadcasted_iota(jnp.int32, (heads, inner), 0)).astype(f32)
    return jnp.dot(values, spread, precision=exact_dot)


def local_ssd(x, dt, b_mat, c_mat, rates, backward):
    length, inner = x.shape
    heads = dt.shape[1]
    nb = length // GROUP
    xb = x.reshape(nb, GROUP, heads, HEAD_DIM)
    dtb = dt.reshape(nb, GROUP, heads)
    bb = b_mat.reshape(nb, GROUP, -1)
    cb = c_mat.reshape(nb, GROUP, -1)
    step = -dtb * rates[None, None, :]
    cum = lax.cumsum(step, axis=1, reverse=backward)
    last = cum[:, 0, :] if backward else cum[:, -1, :]
    scores = jnp.einsum("kin,kjn->kij", cb, bb, preferred_element_type=f32)
    rows = lax.broadcasted_iota(jnp.int32, (GROUP, GROUP), 0)
    cols = lax.broadcasted_iota(jnp.int32, (GROUP, GROUP), 1)
    mask = (rows <= cols) if backward else (rows >= cols)
    mask = mask[None, None]
    cum_t = cum.transpose(0, 2, 1)
    gap = jnp.where(mask, cum_t[:, :, :, None] - cum_t[:, :, None, :], 0.0)
    dt_t = dtb.transpose(0, 2, 1)
    weights = jnp.where(mask, scores[:, None] * jnp.exp(gap) * dt_t[:, :, None, :], 0.0).astype(bf16)
    intra = intra_block(weights, x)
    tail = jnp.exp(last[:, None, :] - cum) * dtb
    tail_wide = head_spread(tail.reshape(length, heads), inner).reshape(nb, GROUP, inner)
    scaled = x.reshape(nb, GROUP, inner).astype(f32) * tail_wide
    block_state = jnp.einsum("kjn,kjc->knc", bb.astype(f32), scaled, precision=exact_dot)
    block_decay = head_spread(jnp.exp(last), inner)
    cum_wide = head_spread(jnp.exp(cum).reshape(length, heads), inner)
    return dict(
        cb=cb,
        cum_wide=cum_wide,
        intra=intra,
        block_state=block_state,
        block_decay=block_decay,
    )


def stretch_states(parts, backward):
    block_state, block_decay = parts["block_state"], parts["block_decay"]
    nb = block_state.shape[0]
    order = list(range(nb - 1, -1, -1)) if backward else list(range(nb))
    starts = [None] * nb
    prefix = [None] * nb
    run_state = jnp.zeros_like(block_state[0])
    run_decay = jnp.ones_like(block_decay[0])
    for k in order:
        starts[k] = run_state
        prefix[k] = run_decay
        run_state = block_decay[k][None, :] * run_state + block_state[k]
        run_decay = run_decay * block_decay[k]
    return jnp.stack(starts), jnp.stack(prefix), run_state, run_decay


def pair_combine(earlier, later):
    (a0, s0), (a1, s1) = earlier, later
    return a1 * a0, a1[None, :] * s0 + s1


def scan_over(axis, own_decay, own_state, backward, extra):
    peers = lax.axis_size(axis)
    step = -1 if backward else 1
    own = (own_decay, own_state)
    holder_parity = 0 if backward else 1
    first = shifted((own_decay, own_state.astype(bf16)), axis, step, 1 - holder_parity)
    first = (first[0], first[1].astype(f32))
    me = lax.axis_index(axis)
    holder = (me % 2 == 0) if backward else (me % 2 == 1)
    total = pair_combine(first, own)
    ex_decay = jnp.ones_like(own_decay)
    ex_state = jnp.zeros_like(own_state)
    in_decay, in_state = total
    distance = 2
    while distance < peers:
        got_decay, got_state = shifted(
            (in_decay, in_state.astype(bf16)), axis, step * distance, holder_parity
        )
        got_state = got_state.astype(f32)
        if distance * 2 >= peers:
            got_state, extra = lax.optimization_barrier((got_state, extra))
        ex_state = ex_decay[None, :] * got_state + ex_state
        ex_decay = ex_decay * got_decay
        if distance * 2 < peers:
            in_state = in_decay[None, :] * got_state + in_state
            in_decay = in_decay * got_decay
        distance *= 2
    handed = shifted(ex_state.astype(bf16), axis, -step, holder_parity).astype(f32)
    mine = first[0][None, :] * ex_state + first[1]
    return jnp.where(holder, mine, handed), extra


def strand_output(parts, starts, prefix, carry, x, d_wide):
    start_states = starts + prefix[:, None, :] * carry[None]
    carried = jnp.einsum(
        "kin,knc->kic", parts["cb"].astype(f32), start_states, precision=exact_dot
    )
    length, inner = x.shape
    carried = carried.reshape(length, inner)
    return parts["intra"] + parts["cum_wide"] * carried + d_wide[None, :] * x.astype(f32)


def per_device(
    hidden,
    base_ids,
    embed,
    w_x,
    w_z,
    w_bc,
    w_dt,
    dt_bias,
    decay_rate,
    conv_x,
    conv_bc,
    d_skip,
    norm_gain,
    w_out,
):
    inner = w_x.shape[1]
    state = w_bc.shape[1] // 2
    conv = conv_x.shape[0]
    onehot = (base_ids[:, None] == jnp.arange(embed.shape[0], dtype=jnp.int32)[None, :]).astype(bf16)
    mixed_in = (hidden.astype(f32) + jnp.dot(onehot, embed, preferred_element_type=f32)).astype(bf16)
    rim = 8
    peers = lax.axis_size("ch")
    both_axes = ("ctx", "ch")
    count = lax.axis_size(both_axes)
    before, after = [], []
    for h in range(peers):
        ahead = [(q, q + h + 1) for q in range(count) if q % peers == peers - 1 and q + h + 1 < count]
        behind = [(q, q - peers + h) for q in range(count) if q % peers == 0 and q - peers + h >= 0]
        before.append(lax.ppermute(mixed_in[-rim:], both_axes, ahead))
        after.append(lax.ppermute(mixed_in[:rim], both_axes, behind))
    me = lax.axis_index("ch")
    u = gather_rows(mixed_in, "ch")
    u_ext = jnp.concatenate(
        [
            jnp.stack(before)[me],
            u,
            jnp.stack(after)[me],
        ],
        axis=0,
    )
    length, width = u.shape
    flip = flip_matrix(width)
    u_ext_flip = jnp.dot(u_ext, flip, preferred_element_type=f32).astype(bf16)
    both_ext = jnp.concatenate([u_ext, u_ext_flip], axis=0)
    both = jnp.concatenate([u_ext[rim : rim + length], u_ext_flip[rim : rim + length]], axis=0)
    x_raw = jnp.dot(both_ext, w_x, preferred_element_type=f32).astype(bf16)
    bc_raw = jnp.dot(both_ext, w_bc, preferred_element_type=f32).astype(bf16)
    z_all = jnp.dot(both, w_z, preferred_element_type=f32).astype(bf16)
    dt_all = jax.nn.softplus(jnp.dot(both, w_dt, preferred_element_type=f32) + dt_bias[None, :])
    ext = length + 2 * rim
    d_wide = head_spread(d_skip[None, :], inner)[0]

    outs = []
    sums = []
    for backward in (False, True):
        rows = slice(length, 2 * length) if backward else slice(0, length)
        ext_rows = slice(ext, 2 * ext) if backward else slice(0, ext)
        x_c = conv_silu(x_raw[ext_rows], conv_x, rim, length, backward)
        bc_c = conv_silu(bc_raw[ext_rows], conv_bc, rim, length, backward)
        parts = local_ssd(x_c, dt_all[rows], bc_c[:, :state], bc_c[:, state:], decay_rate, backward)
        starts, prefix, end_state, end_decay = stretch_states(parts, backward)
        carry, parts["intra"] = scan_over("ctx", end_decay, end_state, backward, parts["intra"])
        y = strand_output(parts, starts, prefix, carry, x_c, d_wide)
        gated = (y * jax.nn.silu(z_all[rows].astype(f32))).astype(bf16).astype(f32)
        outs.append(gated)
        sums.append(jnp.sum(gated * gated, axis=1))
    total = lax.psum(jnp.stack(sums), "ch")
    full_inner = inner * lax.axis_size("ch")
    gain = norm_gain.astype(f32)[None, :]
    normed = [
        (g * lax.rsqrt(t / full_inner + norm_eps)[:, None] * gain).astype(bf16)
        for g, t in zip(outs, total)
    ]
    own_rows = length // peers

    def partial_for(target):
        nf = lax.dynamic_slice_in_dim(normed[0], target * own_rows, own_rows, axis=0)
        nb_ = lax.dynamic_slice_in_dim(normed[1], target * own_rows, own_rows, axis=0)
        out_f = jnp.dot(nf, w_out, preferred_element_type=f32)
        out_b = jnp.dot(nb_, w_out, preferred_element_type=f32)
        return out_f + flipped_columns(out_b, flip)

    received = []
    for d in range(1, peers):
        sent = partial_for((me + d) % peers)
        route = [(i, (i + d) % peers) for i in range(peers)]
        received.append(lax.ppermute(sent.astype(bf16), "ch", route))
    summed = partial_for(me)
    for r in received:
        summed = summed + r.astype(f32)
    return summed.astype(bf16)


def solution(mesh):
    placed = (
        P(("ctx", "ch"), None),
        P(("ctx", "ch")),
        P(),
        P(None, "ch"),
        P(None, "ch"),
        P(),
        P(None, "ch"),
        P("ch"),
        P("ch"),
        P(None, "ch"),
        P(),
        P("ch"),
        P("ch"),
        P("ch", None),
    )
    return jax.shard_map(
        per_device, mesh=mesh, in_specs=placed, out_specs=P(("ctx", "ch"), None), check_vma=False
    )
```

```python
import jax
import jax.numpy as jnp
from jax import lax
from jax.experimental import pallas as pl
from jax.sharding import PartitionSpec as P

HEAD_DIM = 64
GROUP = 128

exact_dot = lax.Precision.HIGHEST
norm_eps = 1e-05
f32 = jnp.float32
bf16 = jnp.bfloat16


def flip_matrix(n):
    rows = lax.broadcasted_iota(jnp.int32, (n, n), 0)
    cols = lax.broadcasted_iota(jnp.int32, (n, n), 1)
    return (rows + cols == n - 1).astype(bf16)


def shifted(block, axis, distance, parity=None):
    devices = range(lax.axis_size(axis))
    route = [
        (i, i + distance)
        for i in devices
        if i + distance in devices and (parity is None or i % 2 == parity)
    ]
    return lax.ppermute(block, axis, route)


def gather_rows(block, axis):
    peers, me = lax.axis_size(axis), lax.axis_index(axis)
    got = [block] + [
        lax.ppermute(block, axis, [(i, (i + d) % peers) for i in range(peers)])
        for d in range(peers - 1, 0, -1)
    ]
    stacked = jnp.stack(got)
    rolled = jnp.roll(stacked, me, axis=0)
    return rolled.reshape(peers * block.shape[0], *block.shape[1:])


def flipped_columns(part, flip):
    hi = part.astype(bf16)
    rest = part - hi.astype(f32)
    mid = rest.astype(bf16)
    lo = (rest - mid.astype(f32)).astype(bf16)
    rows = part.shape[0]
    pieces = jnp.dot(jnp.concatenate([hi, mid, lo], axis=0), flip, preferred_element_type=f32)
    return (pieces[:rows] + pieces[rows : 2 * rows]) + pieces[2 * rows :]


def conv_silu(raw_ext, taps, rim, length, backward):
    conv = taps.shape[0]
    summed = None
    for k in range(conv):
        first = rim + conv - 1 - k if backward else rim - (conv - 1) + k
        term = taps[k][None, :] * raw_ext[first : first + length].astype(f32)
        summed = term if summed is None else summed + term
    return jax.nn.silu(summed).astype(bf16)


def intra_kernel(w_ref, x_ref, o_ref):
    lanes = 128
    per_tile = lanes // HEAD_DIM
    rows = x_ref.shape[0]
    owner = lax.broadcasted_iota(jnp.int32, (rows, lanes), 1) // HEAD_DIM
    for g in range(x_ref.shape[1] // lanes):
        tile = x_ref[:, g * lanes : (g + 1) * lanes]
        zero = jnp.zeros_like(tile)
        stacked = jnp.concatenate([jnp.where(owner == t, tile, zero) for t in range(per_tile)], axis=0)
        wide = jnp.concatenate([w_ref[0, g * per_tile + t] for t in range(per_tile)], axis=1)
        o_ref[:, g * lanes : (g + 1) * lanes] = jnp.dot(wide, stacked, preferred_element_type=f32)


def intra_block(weights, x):
    nb, heads, group, _ = weights.shape
    length, inner = x.shape
    return pl.pallas_call(
        intra_kernel,
        out_shape=jax.ShapeDtypeStruct((length, inner), f32),
        grid=(nb,),
        in_specs=[
            pl.BlockSpec((1, heads, group, group), lambda k: (k, 0, 0, 0)),
            pl.BlockSpec((group, inner), lambda k: (k, 0)),
        ],
        out_specs=pl.BlockSpec((group, inner), lambda k: (k, 0)),
    )(weights, x)


def head_spread(values, inner):
    heads = values.shape[-1]
    owner = lax.broadcasted_iota(jnp.int32, (heads, inner), 1) // HEAD_DIM
    spread = (owner == lax.broadcasted_iota(jnp.int32, (heads, inner), 0)).astype(f32)
    return jnp.dot(values, spread, precision=exact_dot)


def local_ssd(x, dt, b_mat, c_mat, rates, backward):
    length, inner = x.shape
    heads = dt.shape[1]
    nb = length // GROUP
    xb = x.reshape(nb, GROUP, heads, HEAD_DIM)
    dtb = dt.reshape(nb, GROUP, heads)
    bb = b_mat.reshape(nb, GROUP, -1)
    cb = c_mat.reshape(nb, GROUP, -1)
    step = -dtb * rates[None, None, :]
    cum = lax.cumsum(step, axis=1, reverse=backward)
    last = cum[:, 0, :] if backward else cum[:, -1, :]
    scores = jnp.einsum("kin,kjn->kij", cb, bb, preferred_element_type=f32)
    rows = lax.broadcasted_iota(jnp.int32, (GROUP, GROUP), 0)
    cols = lax.broadcasted_iota(jnp.int32, (GROUP, GROUP), 1)
    mask = (rows <= cols) if backward else (rows >= cols)
    mask = mask[None, None]
    cum_t = cum.transpose(0, 2, 1)
    gap = jnp.where(mask, cum_t[:, :, :, None] - cum_t[:, :, None, :], 0.0)
    dt_t = dtb.transpose(0, 2, 1)
    weights = jnp.where(mask, scores[:, None] * jnp.exp(gap) * dt_t[:, :, None, :], 0.0).astype(bf16)
    intra = intra_block(weights, x)
    tail = jnp.exp(last[:, None, :] - cum) * dtb
    tail_wide = head_spread(tail.reshape(length, heads), inner).reshape(nb, GROUP, inner)
    scaled = x.reshape(nb, GROUP, inner).astype(f32) * tail_wide
    block_state = jnp.einsum("kjn,kjc->knc", bb.astype(f32), scaled, precision=exact_dot)
    block_decay = head_spread(jnp.exp(last), inner)
    cum_wide = head_spread(jnp.exp(cum).reshape(length, heads), inner)
    return dict(
        cb=cb,
        cum_wide=cum_wide,
        intra=intra,
        block_state=block_state,
        block_decay=block_decay,
    )


def stretch_states(parts, backward):
    block_state, block_decay = parts["block_state"], parts["block_decay"]
    nb = block_state.shape[0]
    order = list(range(nb - 1, -1, -1)) if backward else list(range(nb))
    starts = [None] * nb
    prefix = [None] * nb
    run_state = jnp.zeros_like(block_state[0])
    run_decay = jnp.ones_like(block_decay[0])
    for k in order:
        starts[k] = run_state
        prefix[k] = run_decay
        run_state = block_decay[k][None, :] * run_state + block_state[k]
        run_decay = run_decay * block_decay[k]
    return jnp.stack(starts), jnp.stack(prefix), run_state, run_decay


def pair_combine(earlier, later):
    (a0, s0), (a1, s1) = earlier, later
    return a1 * a0, a1[None, :] * s0 + s1


def scan_over(axis, own_decay, own_state, backward):
    peers = lax.axis_size(axis)
    step = -1 if backward else 1
    own = (own_decay, own_state)
    holder_parity = 0 if backward else 1
    first = shifted((own_decay, own_state.astype(bf16)), axis, step, 1 - holder_parity)
    first = (first[0], first[1].astype(f32))
    me = lax.axis_index(axis)
    holder = (me % 2 == 0) if backward else (me % 2 == 1)
    total = pair_combine(first, own)
    ex_decay = jnp.ones_like(own_decay)
    ex_state = jnp.zeros_like(own_state)
    in_decay, in_state = total
    distance = 2
    while distance < peers:
        got_decay, got_state = shifted(
            (in_decay, in_state.astype(bf16)), axis, step * distance, holder_parity
        )
        got_state = got_state.astype(f32)
        ex_state = ex_decay[None, :] * got_state + ex_state
        ex_decay = ex_decay * got_decay
        if distance * 2 < peers:
            in_state = in_decay[None, :] * got_state + in_state
            in_decay = in_decay * got_decay
        distance *= 2
    handed = shifted(ex_state.astype(bf16), axis, -step, holder_parity).astype(f32)
    mine = first[0][None, :] * ex_state + first[1]
    return jnp.where(holder, mine, handed)


def strand_output(parts, starts, prefix, carry, x, d_wide):
    start_states = starts + prefix[:, None, :] * carry[None]
    carried = jnp.einsum(
        "kin,knc->kic", parts["cb"].astype(f32), start_states, precision=exact_dot
    )
    length, inner = x.shape
    carried = carried.reshape(length, inner)
    return parts["intra"] + parts["cum_wide"] * carried + d_wide[None, :] * x.astype(f32)


def per_device(
    hidden,
    base_ids,
    embed,
    w_x,
    w_z,
    w_bc,
    w_dt,
    dt_bias,
    decay_rate,
    conv_x,
    conv_bc,
    d_skip,
    norm_gain,
    w_out,
):
    inner = w_x.shape[1]
    state = w_bc.shape[1] // 2
    conv = conv_x.shape[0]
    onehot = (base_ids[:, None] == jnp.arange(embed.shape[0], dtype=jnp.int32)[None, :]).astype(bf16)
    mixed_in = (hidden.astype(f32) + jnp.dot(onehot, embed, preferred_element_type=f32)).astype(bf16)
    rim = 8
    peers = lax.axis_size("ch")
    both_axes = ("ctx", "ch")
    count = lax.axis_size(both_axes)
    before, after = [], []
    for h in range(peers):
        ahead = [(q, q + h + 1) for q in range(count) if q % peers == peers - 1 and q + h + 1 < count]
        behind = [(q, q - peers + h) for q in range(count) if q % peers == 0 and q - peers + h >= 0]
        before.append(lax.ppermute(mixed_in[-rim:], both_axes, ahead))
        after.append(lax.ppermute(mixed_in[:rim], both_axes, behind))
    me = lax.axis_index("ch")
    u = gather_rows(mixed_in, "ch")
    u_ext = jnp.concatenate(
        [
            jnp.stack(before)[me],
            u,
            jnp.stack(after)[me],
        ],
        axis=0,
    )
    length, width = u.shape
    flip = flip_matrix(width)
    u_ext_flip = jnp.dot(u_ext, flip, preferred_element_type=f32).astype(bf16)
    both = jnp.concatenate([u_ext[rim : rim + length], u_ext_flip[rim : rim + length]], axis=0)
    z_all = jnp.dot(both, w_z, preferred_element_type=f32).astype(bf16)
    ext = length + 2 * rim
    d_wide = head_spread(d_skip[None, :], inner)[0]

    outs = []
    sums = []
    for backward in (False, True):
        rows = slice(length, 2 * length) if backward else slice(0, length)
        source = u_ext_flip if backward else u_ext
        x_raw = jnp.dot(source, w_x, preferred_element_type=f32).astype(bf16)
        bc_raw = jnp.dot(source, w_bc, preferred_element_type=f32).astype(bf16)
        dt_raw = jnp.dot(source[rim : rim + length], w_dt, preferred_element_type=f32)
        dt_s = jax.nn.softplus(dt_raw + dt_bias[None, :])
        x_c = conv_silu(x_raw, conv_x, rim, length, backward)
        bc_c = conv_silu(bc_raw, conv_bc, rim, length, backward)
        parts = local_ssd(x_c, dt_s, bc_c[:, :state], bc_c[:, state:], decay_rate, backward)
        starts, prefix, end_state, end_decay = stretch_states(parts, backward)
        carry = scan_over("ctx", end_decay, end_state, backward)
        y = strand_output(parts, starts, prefix, carry, x_c, d_wide)
        gated = (y * jax.nn.silu(z_all[rows].astype(f32))).astype(bf16).astype(f32)
        outs.append(gated)
        sums.append(jnp.sum(gated * gated, axis=1))
    total = lax.psum(jnp.stack(sums), "ch")
    full_inner = inner * lax.axis_size("ch")
    gain = norm_gain.astype(f32)[None, :]
    normed = [
        (g * lax.rsqrt(t / full_inner + norm_eps)[:, None] * gain).astype(bf16)
        for g, t in zip(outs, total)
    ]
    own_rows = length // peers

    def partial_for(target):
        nf = lax.dynamic_slice_in_dim(normed[0], target * own_rows, own_rows, axis=0)
        nb_ = lax.dynamic_slice_in_dim(normed[1], target * own_rows, own_rows, axis=0)
        out_f = jnp.dot(nf, w_out, preferred_element_type=f32)
        out_b = jnp.dot(nb_, w_out, preferred_element_type=f32)
        return out_f + flipped_columns(out_b, flip)

    received = []
    for d in range(1, peers):
        sent = partial_for((me + d) % peers)
        route = [(i, (i + d) % peers) for i in range(peers)]
        received.append(lax.ppermute(sent.astype(bf16), "ch", route))
    summed = partial_for(me)
    for r in received:
        summed = summed + r.astype(f32)
    return summed.astype(bf16)


def solution(mesh):
    placed = (
        P(("ctx", "ch"), None),
        P(("ctx", "ch")),
        P(),
        P(None, "ch"),
        P(None, "ch"),
        P(),
        P(None, "ch"),
        P("ch"),
        P("ch"),
        P(None, "ch"),
        P(),
        P("ch"),
        P("ch"),
        P("ch", None),
    )
    return jax.shard_map(
        per_device, mesh=mesh, in_specs=placed, out_specs=P(("ctx", "ch"), None), check_vma=False
    )
```

```python
import jax
import jax.numpy as jnp
from jax import lax
from jax.experimental import pallas as pl
from jax.sharding import PartitionSpec as P

HEAD_DIM = 64
GROUP = 128

exact_dot = lax.Precision.HIGHEST
norm_eps = 1e-05
f32 = jnp.float32
bf16 = jnp.bfloat16


def flip_matrix(n):
    rows = lax.broadcasted_iota(jnp.int32, (n, n), 0)
    cols = lax.broadcasted_iota(jnp.int32, (n, n), 1)
    return (rows + cols == n - 1).astype(bf16)


def shifted(block, axis, distance, parity=None):
    devices = range(lax.axis_size(axis))
    route = [
        (i, i + distance)
        for i in devices
        if i + distance in devices and (parity is None or i % 2 == parity)
    ]
    return lax.ppermute(block, axis, route)


def gather_rows(block, axis):
    peers, me = lax.axis_size(axis), lax.axis_index(axis)
    got = [block] + [
        lax.ppermute(block, axis, [(i, (i + d) % peers) for i in range(peers)])
        for d in range(peers - 1, 0, -1)
    ]
    stacked = jnp.stack(got)
    rolled = jnp.roll(stacked, me, axis=0)
    return rolled.reshape(peers * block.shape[0], *block.shape[1:])


def flipped_columns(part, flip):
    hi = part.astype(bf16)
    rest = part - hi.astype(f32)
    mid = rest.astype(bf16)
    lo = (rest - mid.astype(f32)).astype(bf16)
    rows = part.shape[0]
    pieces = jnp.dot(jnp.concatenate([hi, mid, lo], axis=0), flip, preferred_element_type=f32)
    return (pieces[:rows] + pieces[rows : 2 * rows]) + pieces[2 * rows :]


def conv_silu(raw_ext, taps, rim, length, backward):
    conv = taps.shape[0]
    summed = None
    for k in range(conv):
        first = rim + conv - 1 - k if backward else rim - (conv - 1) + k
        term = taps[k][None, :] * raw_ext[first : first + length].astype(f32)
        summed = term if summed is None else summed + term
    return jax.nn.silu(summed).astype(bf16)


def intra_kernel(w_ref, x_ref, o_ref):
    lanes = 128
    per_tile = lanes // HEAD_DIM
    rows = x_ref.shape[0]
    owner = lax.broadcasted_iota(jnp.int32, (rows, lanes), 1) // HEAD_DIM
    for g in range(x_ref.shape[1] // lanes):
        tile = x_ref[:, g * lanes : (g + 1) * lanes]
        zero = jnp.zeros_like(tile)
        stacked = jnp.concatenate([jnp.where(owner == t, tile, zero) for t in range(per_tile)], axis=0)
        wide = jnp.concatenate([w_ref[0, g * per_tile + t] for t in range(per_tile)], axis=1)
        o_ref[:, g * lanes : (g + 1) * lanes] = jnp.dot(wide, stacked, preferred_element_type=f32)


def intra_block(weights, x):
    nb, heads, group, _ = weights.shape
    length, inner = x.shape
    return pl.pallas_call(
        intra_kernel,
        out_shape=jax.ShapeDtypeStruct((length, inner), f32),
        grid=(nb,),
        in_specs=[
            pl.BlockSpec((1, heads, group, group), lambda k: (k, 0, 0, 0)),
            pl.BlockSpec((group, inner), lambda k: (k, 0)),
        ],
        out_specs=pl.BlockSpec((group, inner), lambda k: (k, 0)),
    )(weights, x)


def head_spread(values, inner):
    heads = values.shape[-1]
    owner = lax.broadcasted_iota(jnp.int32, (heads, inner), 1) // HEAD_DIM
    spread = (owner == lax.broadcasted_iota(jnp.int32, (heads, inner), 0)).astype(f32)
    return jnp.dot(values, spread, precision=exact_dot)


def local_ssd(x, dt, b_mat, c_mat, rates, backward):
    length, inner = x.shape
    heads = dt.shape[1]
    nb = length // GROUP
    xb = x.reshape(nb, GROUP, heads, HEAD_DIM)
    dtb = dt.reshape(nb, GROUP, heads)
    bb = b_mat.reshape(nb, GROUP, -1)
    cb = c_mat.reshape(nb, GROUP, -1)
    step = -dtb * rates[None, None, :]
    cum = lax.cumsum(step, axis=1, reverse=backward)
    last = cum[:, 0, :] if backward else cum[:, -1, :]
    scores = jnp.einsum("kin,kjn->kij", cb, bb, preferred_element_type=f32)
    rows = lax.broadcasted_iota(jnp.int32, (GROUP, GROUP), 0)
    cols = lax.broadcasted_iota(jnp.int32, (GROUP, GROUP), 1)
    mask = (rows <= cols) if backward else (rows >= cols)
    mask = mask[None, None]
    cum_t = cum.transpose(0, 2, 1)
    gap = jnp.where(mask, cum_t[:, :, :, None] - cum_t[:, :, None, :], 0.0)
    dt_t = dtb.transpose(0, 2, 1)
    weights = jnp.where(mask, scores[:, None] * jnp.exp(gap) * dt_t[:, :, None, :], 0.0).astype(bf16)
    intra = intra_block(weights, x)
    tail = jnp.exp(last[:, None, :] - cum) * dtb
    tail_wide = head_spread(tail.reshape(length, heads), inner).reshape(nb, GROUP, inner)
    scaled = x.reshape(nb, GROUP, inner).astype(f32) * tail_wide
    block_state = jnp.einsum("kjn,kjc->knc", bb.astype(f32), scaled, precision=exact_dot)
    block_decay = head_spread(jnp.exp(last), inner)
    cum_wide = head_spread(jnp.exp(cum).reshape(length, heads), inner)
    return dict(
        cb=cb,
        cum_wide=cum_wide,
        intra=intra,
        block_state=block_state,
        block_decay=block_decay,
    )


def stretch_states(parts, backward):
    block_state, block_decay = parts["block_state"], parts["block_decay"]
    nb = block_state.shape[0]
    order = list(range(nb - 1, -1, -1)) if backward else list(range(nb))
    starts = [None] * nb
    prefix = [None] * nb
    run_state = jnp.zeros_like(block_state[0])
    run_decay = jnp.ones_like(block_decay[0])
    for k in order:
        starts[k] = run_state
        prefix[k] = run_decay
        run_state = block_decay[k][None, :] * run_state + block_state[k]
        run_decay = run_decay * block_decay[k]
    return jnp.stack(starts), jnp.stack(prefix), run_state, run_decay


def packed(decay, state):
    hi = decay.astype(bf16)
    rest = decay - hi.astype(f32)
    mid = rest.astype(bf16)
    lo = (rest - mid.astype(f32)).astype(bf16)
    return jnp.concatenate([state.astype(bf16), jnp.stack([hi, mid, lo])], axis=0)


def unpacked(message):
    rows = message.shape[0] - 3
    tail = message[rows:].astype(f32)
    return (tail[0] + tail[1]) + tail[2], message[:rows].astype(f32)


def pair_combine(earlier, later):
    (a0, s0), (a1, s1) = earlier, later
    return a1 * a0, a1[None, :] * s0 + s1


def scan_over(axis, own_decay, own_state, backward):
    peers = lax.axis_size(axis)
    step = -1 if backward else 1
    own = (own_decay, own_state)
    holder_parity = 0 if backward else 1
    first = unpacked(shifted(packed(own_decay, own_state), axis, step, 1 - holder_parity))
    me = lax.axis_index(axis)
    holder = (me % 2 == 0) if backward else (me % 2 == 1)
    total = pair_combine(first, own)
    ex_decay = jnp.ones_like(own_decay)
    ex_state = jnp.zeros_like(own_state)
    in_decay, in_state = total
    distance = 2
    while distance < peers:
        got_decay, got_state = unpacked(
            shifted(packed(in_decay, in_state), axis, step * distance, holder_parity)
        )
        ex_state = ex_decay[None, :] * got_state + ex_state
        ex_decay = ex_decay * got_decay
        if distance * 2 < peers:
            in_state = in_decay[None, :] * got_state + in_state
            in_decay = in_decay * got_decay
        distance *= 2
    handed = shifted(ex_state.astype(bf16), axis, -step, holder_parity).astype(f32)
    mine = first[0][None, :] * ex_state + first[1]
    return jnp.where(holder, mine, handed)


def strand_output(parts, starts, prefix, carry, x, d_wide):
    start_states = starts + prefix[:, None, :] * carry[None]
    carried = jnp.einsum(
        "kin,knc->kic", parts["cb"].astype(f32), start_states, precision=exact_dot
    )
    length, inner = x.shape
    carried = carried.reshape(length, inner)
    return parts["intra"] + parts["cum_wide"] * carried + d_wide[None, :] * x.astype(f32)


def per_device(
    hidden,
    base_ids,
    embed,
    w_x,
    w_z,
    w_bc,
    w_dt,
    dt_bias,
    decay_rate,
    conv_x,
    conv_bc,
    d_skip,
    norm_gain,
    w_out,
):
    inner = w_x.shape[1]
    state = w_bc.shape[1] // 2
    conv = conv_x.shape[0]
    onehot = (base_ids[:, None] == jnp.arange(embed.shape[0], dtype=jnp.int32)[None, :]).astype(bf16)
    mixed_in = (hidden.astype(f32) + jnp.dot(onehot, embed, preferred_element_type=f32)).astype(bf16)
    rim = 8
    peers = lax.axis_size("ch")
    both_axes = ("ctx", "ch")
    count = lax.axis_size(both_axes)
    before, after = [], []
    for h in range(peers):
        ahead = [(q, q + h + 1) for q in range(count) if q % peers == peers - 1 and q + h + 1 < count]
        behind = [(q, q - peers + h) for q in range(count) if q % peers == 0 and q - peers + h >= 0]
        before.append(lax.ppermute(mixed_in[-rim:], both_axes, ahead))
        after.append(lax.ppermute(mixed_in[:rim], both_axes, behind))
    me = lax.axis_index("ch")
    u = gather_rows(mixed_in, "ch")
    u_ext = jnp.concatenate(
        [
            jnp.stack(before)[me],
            u,
            jnp.stack(after)[me],
        ],
        axis=0,
    )
    length, width = u.shape
    flip = flip_matrix(width)
    u_ext_flip = jnp.dot(u_ext, flip, preferred_element_type=f32).astype(bf16)
    both_ext = jnp.concatenate([u_ext, u_ext_flip], axis=0)
    both = jnp.concatenate([u_ext[rim : rim + length], u_ext_flip[rim : rim + length]], axis=0)
    x_raw = jnp.dot(both_ext, w_x, preferred_element_type=f32).astype(bf16)
    bc_raw = jnp.dot(both_ext, w_bc, preferred_element_type=f32).astype(bf16)
    z_all = jnp.dot(both, w_z, preferred_element_type=f32).astype(bf16)
    dt_all = jax.nn.softplus(jnp.dot(both, w_dt, preferred_element_type=f32) + dt_bias[None, :])
    ext = length + 2 * rim
    d_wide = head_spread(d_skip[None, :], inner)[0]

    outs = []
    sums = []
    for backward in (False, True):
        rows = slice(length, 2 * length) if backward else slice(0, length)
        ext_rows = slice(ext, 2 * ext) if backward else slice(0, ext)
        x_c = conv_silu(x_raw[ext_rows], conv_x, rim, length, backward)
        bc_c = conv_silu(bc_raw[ext_rows], conv_bc, rim, length, backward)
        parts = local_ssd(x_c, dt_all[rows], bc_c[:, :state], bc_c[:, state:], decay_rate, backward)
        starts, prefix, end_state, end_decay = stretch_states(parts, backward)
        carry = scan_over("ctx", end_decay, end_state, backward)
        y = strand_output(parts, starts, prefix, carry, x_c, d_wide)
        gated = (y * jax.nn.silu(z_all[rows].astype(f32))).astype(bf16).astype(f32)
        outs.append(gated)
        sums.append(jnp.sum(gated * gated, axis=1))
    total = lax.psum(jnp.stack(sums), "ch")
    full_inner = inner * lax.axis_size("ch")
    gain = norm_gain.astype(f32)[None, :]
    normed = [
        (g * lax.rsqrt(t / full_inner + norm_eps)[:, None] * gain).astype(bf16)
        for g, t in zip(outs, total)
    ]
    own_rows = length // peers

    def partial_for(target):
        nf = lax.dynamic_slice_in_dim(normed[0], target * own_rows, own_rows, axis=0)
        nb_ = lax.dynamic_slice_in_dim(normed[1], target * own_rows, own_rows, axis=0)
        out_f = jnp.dot(nf, w_out, preferred_element_type=f32)
        out_b = jnp.dot(nb_, w_out, preferred_element_type=f32)
        return out_f + flipped_columns(out_b, flip)

    received = []
    for d in range(1, peers):
        sent = partial_for((me + d) % peers)
        route = [(i, (i + d) % peers) for i in range(peers)]
        received.append(lax.ppermute(sent.astype(bf16), "ch", route))
    summed = partial_for(me)
    for r in received:
        summed = summed + r.astype(f32)
    return summed.astype(bf16)


def solution(mesh):
    placed = (
        P(("ctx", "ch"), None),
        P(("ctx", "ch")),
        P(),
        P(None, "ch"),
        P(None, "ch"),
        P(),
        P(None, "ch"),
        P("ch"),
        P("ch"),
        P(None, "ch"),
        P(),
        P("ch"),
        P("ch"),
        P("ch", None),
    )
    return jax.shard_map(
        per_device, mesh=mesh, in_specs=placed, out_specs=P(("ctx", "ch"), None), check_vma=False
    )
```

```python
import jax
import jax.numpy as jnp
from jax import lax
from jax.experimental import pallas as pl
from jax.sharding import PartitionSpec as P

HEAD_DIM = 64
GROUP = 128

exact_dot = lax.Precision.HIGHEST
norm_eps = 1e-05
f32 = jnp.float32
bf16 = jnp.bfloat16


def flip_matrix(n):
    rows = lax.broadcasted_iota(jnp.int32, (n, n), 0)
    cols = lax.broadcasted_iota(jnp.int32, (n, n), 1)
    return (rows + cols == n - 1).astype(bf16)


def shifted(block, axis, distance, parity=None):
    devices = range(lax.axis_size(axis))
    route = [
        (i, i + distance)
        for i in devices
        if i + distance in devices and (parity is None or i % 2 == parity)
    ]
    return lax.ppermute(block, axis, route)


def gather_rows(block, axis):
    peers, me = lax.axis_size(axis), lax.axis_index(axis)
    got = [block] + [
        lax.ppermute(block, axis, [(i, (i + d) % peers) for i in range(peers)])
        for d in range(peers - 1, 0, -1)
    ]
    stacked = jnp.stack(got)
    rolled = jnp.roll(stacked, me, axis=0)
    return rolled.reshape(peers * block.shape[0], *block.shape[1:])


def bf16_part(values):
    return lax.reduce_precision(values, exponent_bits=8, mantissa_bits=7)


def flipped_columns(part, flip):
    hi = bf16_part(part)
    rest = part - hi
    mid = bf16_part(rest)
    lo = rest - mid
    rows = part.shape[0]
    split = jnp.concatenate([hi, mid, lo], axis=0).astype(bf16)
    pieces = jnp.dot(split, flip, preferred_element_type=f32)
    return (pieces[:rows] + pieces[rows : 2 * rows]) + pieces[2 * rows :]


def conv_silu(raw_ext, taps, rim, length, backward):
    conv = taps.shape[0]
    summed = None
    for k in range(conv):
        first = rim + conv - 1 - k if backward else rim - (conv - 1) + k
        term = taps[k][None, :] * raw_ext[first : first + length].astype(f32)
        summed = term if summed is None else summed + term
    return jax.nn.silu(summed).astype(bf16)


def intra_kernel(w_ref, x_ref, o_ref):
    lanes = 128
    per_tile = lanes // HEAD_DIM
    rows = x_ref.shape[0]
    owner = lax.broadcasted_iota(jnp.int32, (rows, lanes), 1) // HEAD_DIM
    for g in range(x_ref.shape[1] // lanes):
        tile = x_ref[:, g * lanes : (g + 1) * lanes]
        zero = jnp.zeros_like(tile)
        stacked = jnp.concatenate([jnp.where(owner == t, tile, zero) for t in range(per_tile)], axis=0)
        wide = jnp.concatenate([w_ref[0, g * per_tile + t] for t in range(per_tile)], axis=1)
        o_ref[:, g * lanes : (g + 1) * lanes] = jnp.dot(wide, stacked, preferred_element_type=f32)


def intra_block(weights, x):
    nb, heads, group, _ = weights.shape
    length, inner = x.shape
    return pl.pallas_call(
        intra_kernel,
        out_shape=jax.ShapeDtypeStruct((length, inner), f32),
        grid=(nb,),
        in_specs=[
            pl.BlockSpec((1, heads, group, group), lambda k: (k, 0, 0, 0)),
            pl.BlockSpec((group, inner), lambda k: (k, 0)),
        ],
        out_specs=pl.BlockSpec((group, inner), lambda k: (k, 0)),
    )(weights, x)


def head_spread(values, inner):
    heads = values.shape[-1]
    owner = lax.broadcasted_iota(jnp.int32, (heads, inner), 1) // HEAD_DIM
    spread = (owner == lax.broadcasted_iota(jnp.int32, (heads, inner), 0)).astype(f32)
    return jnp.dot(values, spread, precision=exact_dot)


def local_ssd(x, dt, b_mat, c_mat, rates, backward):
    length, inner = x.shape
    heads = dt.shape[1]
    nb = length // GROUP
    xb = x.reshape(nb, GROUP, heads, HEAD_DIM)
    dtb = dt.reshape(nb, GROUP, heads)
    bb = b_mat.reshape(nb, GROUP, -1)
    cb = c_mat.reshape(nb, GROUP, -1)
    step = -dtb * rates[None, None, :]
    cum = lax.cumsum(step, axis=1, reverse=backward)
    last = cum[:, 0, :] if backward else cum[:, -1, :]
    scores = jnp.einsum("kin,kjn->kij", cb, bb, preferred_element_type=f32)
    rows = lax.broadcasted_iota(jnp.int32, (GROUP, GROUP), 0)
    cols = lax.broadcasted_iota(jnp.int32, (GROUP, GROUP), 1)
    mask = (rows <= cols) if backward else (rows >= cols)
    mask = mask[None, None]
    cum_t = cum.transpose(0, 2, 1)
    gap = jnp.where(mask, cum_t[:, :, :, None] - cum_t[:, :, None, :], 0.0)
    dt_t = dtb.transpose(0, 2, 1)
    weights = jnp.where(mask, scores[:, None] * jnp.exp(gap) * dt_t[:, :, None, :], 0.0).astype(bf16)
    intra = intra_block(weights, x)
    tail = jnp.exp(last[:, None, :] - cum) * dtb
    tail_wide = head_spread(tail.reshape(length, heads), inner).reshape(nb, GROUP, inner)
    scaled = x.reshape(nb, GROUP, inner).astype(f32) * tail_wide
    block_state = jnp.einsum("kjn,kjc->knc", bb.astype(f32), scaled, precision=exact_dot)
    block_decay = head_spread(jnp.exp(last), inner)
    cum_wide = head_spread(jnp.exp(cum).reshape(length, heads), inner)
    return dict(
        cb=cb,
        cum_wide=cum_wide,
        intra=intra,
        block_state=block_state,
        block_decay=block_decay,
    )


def stretch_states(parts, backward):
    block_state, block_decay = parts["block_state"], parts["block_decay"]
    nb = block_state.shape[0]
    order = list(range(nb - 1, -1, -1)) if backward else list(range(nb))
    starts = [None] * nb
    prefix = [None] * nb
    run_state = jnp.zeros_like(block_state[0])
    run_decay = jnp.ones_like(block_decay[0])
    for k in order:
        starts[k] = run_state
        prefix[k] = run_decay
        run_state = block_decay[k][None, :] * run_state + block_state[k]
        run_decay = run_decay * block_decay[k]
    return jnp.stack(starts), jnp.stack(prefix), run_state, run_decay


def pair_combine(earlier, later):
    (a0, s0), (a1, s1) = earlier, later
    return a1 * a0, a1[None, :] * s0 + s1


def scan_over(axis, own_decay, own_state, backward):
    peers = lax.axis_size(axis)
    step = -1 if backward else 1
    own = (own_decay, own_state)
    holder_parity = 0 if backward else 1
    first = shifted((own_decay, own_state.astype(bf16)), axis, step, 1 - holder_parity)
    first = (first[0], first[1].astype(f32))
    me = lax.axis_index(axis)
    holder = (me % 2 == 0) if backward else (me % 2 == 1)
    total = pair_combine(first, own)
    ex_decay = jnp.ones_like(own_decay)
    ex_state = jnp.zeros_like(own_state)
    in_decay, in_state = total
    distance = 2
    while distance < peers:
        got_decay, got_state = shifted(
            (in_decay, in_state.astype(bf16)), axis, step * distance, holder_parity
        )
        got_state = got_state.astype(f32)
        ex_state = ex_decay[None, :] * got_state + ex_state
        ex_decay = ex_decay * got_decay
        if distance * 2 < peers:
            in_state = in_decay[None, :] * got_state + in_state
            in_decay = in_decay * got_decay
        distance *= 2
    handed = shifted(ex_state.astype(bf16), axis, -step, holder_parity).astype(f32)
    mine = first[0][None, :] * ex_state + first[1]
    return jnp.where(holder, mine, handed)


def strand_output(parts, starts, prefix, carry, x, d_wide):
    start_states = starts + prefix[:, None, :] * carry[None]
    carried = jnp.einsum(
        "kin,knc->kic", parts["cb"].astype(f32), start_states, precision=exact_dot
    )
    length, inner = x.shape
    carried = carried.reshape(length, inner)
    return parts["intra"] + parts["cum_wide"] * carried + d_wide[None, :] * x.astype(f32)


def per_device(
    hidden,
    base_ids,
    embed,
    w_x,
    w_z,
    w_bc,
    w_dt,
    dt_bias,
    decay_rate,
    conv_x,
    conv_bc,
    d_skip,
    norm_gain,
    w_out,
):
    inner = w_x.shape[1]
    state = w_bc.shape[1] // 2
    conv = conv_x.shape[0]
    onehot = (base_ids[:, None] == jnp.arange(embed.shape[0], dtype=jnp.int32)[None, :]).astype(bf16)
    mixed_in = (hidden.astype(f32) + jnp.dot(onehot, embed, preferred_element_type=f32)).astype(bf16)
    rim = 8
    peers = lax.axis_size("ch")
    both_axes = ("ctx", "ch")
    count = lax.axis_size(both_axes)
    before, after = [], []
    for h in range(peers):
        ahead = [(q, q + h + 1) for q in range(count) if q % peers == peers - 1 and q + h + 1 < count]
        behind = [(q, q - peers + h) for q in range(count) if q % peers == 0 and q - peers + h >= 0]
        before.append(lax.ppermute(mixed_in[-rim:], both_axes, ahead))
        after.append(lax.ppermute(mixed_in[:rim], both_axes, behind))
    me = lax.axis_index("ch")
    u = gather_rows(mixed_in, "ch")
    u_ext = jnp.concatenate(
        [
            jnp.stack(before)[me],
            u,
            jnp.stack(after)[me],
        ],
        axis=0,
    )
    length, width = u.shape
    flip = flip_matrix(width)
    u_ext_flip = jnp.dot(u_ext, flip, preferred_element_type=f32).astype(bf16)
    both_ext = jnp.concatenate([u_ext, u_ext_flip], axis=0)
    both = jnp.concatenate([u_ext[rim : rim + length], u_ext_flip[rim : rim + length]], axis=0)
    x_raw = jnp.dot(both_ext, w_x, preferred_element_type=f32).astype(bf16)
    bc_raw = jnp.dot(both_ext, w_bc, preferred_element_type=f32).astype(bf16)
    z_all = jnp.dot(both, w_z, preferred_element_type=f32).astype(bf16)
    dt_all = jax.nn.softplus(jnp.dot(both, w_dt, preferred_element_type=f32) + dt_bias[None, :])
    ext = length + 2 * rim
    d_wide = head_spread(d_skip[None, :], inner)[0]

    outs = []
    sums = []
    for backward in (False, True):
        rows = slice(length, 2 * length) if backward else slice(0, length)
        ext_rows = slice(ext, 2 * ext) if backward else slice(0, ext)
        x_c = conv_silu(x_raw[ext_rows], conv_x, rim, length, backward)
        bc_c = conv_silu(bc_raw[ext_rows], conv_bc, rim, length, backward)
        parts = local_ssd(x_c, dt_all[rows], bc_c[:, :state], bc_c[:, state:], decay_rate, backward)
        starts, prefix, end_state, end_decay = stretch_states(parts, backward)
        carry = scan_over("ctx", end_decay, end_state, backward)
        y = strand_output(parts, starts, prefix, carry, x_c, d_wide)
        gated = (y * jax.nn.silu(z_all[rows].astype(f32))).astype(bf16).astype(f32)
        outs.append(gated)
        sums.append(jnp.sum(gated * gated, axis=1))
    total = lax.psum(jnp.stack(sums), "ch")
    full_inner = inner * lax.axis_size("ch")
    gain = norm_gain.astype(f32)[None, :]
    normed = [
        (g * lax.rsqrt(t / full_inner + norm_eps)[:, None] * gain).astype(bf16)
        for g, t in zip(outs, total)
    ]
    own_rows = length // peers

    def partial_for(target):
        nf = lax.dynamic_slice_in_dim(normed[0], target * own_rows, own_rows, axis=0)
        nb_ = lax.dynamic_slice_in_dim(normed[1], target * own_rows, own_rows, axis=0)
        out_f = jnp.dot(nf, w_out, preferred_element_type=f32)
        out_b = jnp.dot(nb_, w_out, preferred_element_type=f32)
        return out_f + flipped_columns(out_b, flip)

    received = []
    for d in range(1, peers):
        sent = partial_for((me + d) % peers)
        route = [(i, (i + d) % peers) for i in range(peers)]
        received.append(lax.ppermute(sent.astype(bf16), "ch", route))
    summed = partial_for(me)
    for r in received:
        summed = summed + r.astype(f32)
    return summed.astype(bf16)


def solution(mesh):
    placed = (
        P(("ctx", "ch"), None),
        P(("ctx", "ch")),
        P(),
        P(None, "ch"),
        P(None, "ch"),
        P(),
        P(None, "ch"),
        P("ch"),
        P("ch"),
        P(None, "ch"),
        P(),
        P("ch"),
        P("ch"),
        P("ch", None),
    )
    return jax.shard_map(
        per_device, mesh=mesh, in_specs=placed, out_specs=P(("ctx", "ch"), None), check_vma=False
    )
```

```python
import jax
import jax.numpy as jnp
from jax import lax
from jax.experimental import pallas as pl
from jax.sharding import PartitionSpec as P

HEAD_DIM = 64
GROUP = 128

exact_dot = lax.Precision.HIGHEST
norm_eps = 1e-05
f32 = jnp.float32
bf16 = jnp.bfloat16


def flip_matrix(n):
    rows = lax.broadcasted_iota(jnp.int32, (n, n), 0)
    cols = lax.broadcasted_iota(jnp.int32, (n, n), 1)
    return (rows + cols == n - 1).astype(bf16)


def shifted(block, axis, distance, parity=None):
    devices = range(lax.axis_size(axis))
    route = [
        (i, i + distance)
        for i in devices
        if i + distance in devices and (parity is None or i % 2 == parity)
    ]
    return lax.ppermute(block, axis, route)


def gather_rows(block, axis):
    peers, me = lax.axis_size(axis), lax.axis_index(axis)
    got = [block] + [
        lax.ppermute(block, axis, [(i, (i + d) % peers) for i in range(peers)])
        for d in range(peers - 1, 0, -1)
    ]
    stacked = jnp.stack(got)
    rolled = jnp.roll(stacked, me, axis=0)
    return rolled.reshape(peers * block.shape[0], *block.shape[1:])


def bf16_part(values):
    return lax.reduce_precision(values, exponent_bits=8, mantissa_bits=7)


def flipped_columns(part, flip):
    hi = bf16_part(part)
    rest = part - hi
    mid = bf16_part(rest)
    lo = rest - mid
    rows = part.shape[0]
    split = jnp.concatenate([hi, mid, lo], axis=0).astype(bf16)
    pieces = jnp.dot(split, flip, preferred_element_type=f32)
    return (pieces[:rows] + pieces[rows : 2 * rows]) + pieces[2 * rows :]


def conv_silu(raw_ext, taps, rim, length, backward):
    conv = taps.shape[0]
    summed = None
    for k in range(conv):
        first = rim + conv - 1 - k if backward else rim - (conv - 1) + k
        term = taps[k][None, :] * raw_ext[first : first + length].astype(f32)
        summed = term if summed is None else summed + term
    return jax.nn.silu(summed).astype(bf16)


def intra_kernel(w_ref, x_ref, o_ref):
    lanes = 128
    per_tile = lanes // HEAD_DIM
    rows = x_ref.shape[0]
    owner = lax.broadcasted_iota(jnp.int32, (rows, lanes), 1) // HEAD_DIM
    for g in range(x_ref.shape[1] // lanes):
        tile = x_ref[:, g * lanes : (g + 1) * lanes]
        zero = jnp.zeros_like(tile)
        stacked = jnp.concatenate([jnp.where(owner == t, tile, zero) for t in range(per_tile)], axis=0)
        wide = jnp.concatenate([w_ref[0, g * per_tile + t] for t in range(per_tile)], axis=1)
        o_ref[:, g * lanes : (g + 1) * lanes] = jnp.dot(wide, stacked, preferred_element_type=f32)


def intra_block(weights, x):
    nb, heads, group, _ = weights.shape
    length, inner = x.shape
    return pl.pallas_call(
        intra_kernel,
        out_shape=jax.ShapeDtypeStruct((length, inner), f32),
        grid=(nb,),
        in_specs=[
            pl.BlockSpec((1, heads, group, group), lambda k: (k, 0, 0, 0)),
            pl.BlockSpec((group, inner), lambda k: (k, 0)),
        ],
        out_specs=pl.BlockSpec((group, inner), lambda k: (k, 0)),
    )(weights, x)


def head_spread(values, inner):
    heads = values.shape[-1]
    owner = lax.broadcasted_iota(jnp.int32, (heads, inner), 1) // HEAD_DIM
    spread = (owner == lax.broadcasted_iota(jnp.int32, (heads, inner), 0)).astype(f32)
    return jnp.dot(values, spread, precision=exact_dot)


def local_ssd(x, dt, b_mat, c_mat, rates, backward):
    length, inner = x.shape
    heads = dt.shape[1]
    nb = length // GROUP
    xb = x.reshape(nb, GROUP, heads, HEAD_DIM)
    dtb = dt.reshape(nb, GROUP, heads)
    bb = b_mat.reshape(nb, GROUP, -1)
    cb = c_mat.reshape(nb, GROUP, -1)
    step = -dtb * rates[None, None, :]
    cum = lax.cumsum(step, axis=1, reverse=backward)
    last = cum[:, 0, :] if backward else cum[:, -1, :]
    scores = jnp.einsum("kin,kjn->kij", cb, bb, preferred_element_type=f32)
    rows = lax.broadcasted_iota(jnp.int32, (GROUP, GROUP), 0)
    cols = lax.broadcasted_iota(jnp.int32, (GROUP, GROUP), 1)
    mask = (rows <= cols) if backward else (rows >= cols)
    mask = mask[None, None]
    cum_t = cum.transpose(0, 2, 1)
    gap = jnp.where(mask, cum_t[:, :, :, None] - cum_t[:, :, None, :], 0.0)
    dt_t = dtb.transpose(0, 2, 1)
    weights = jnp.where(mask, scores[:, None] * jnp.exp(gap) * dt_t[:, :, None, :], 0.0).astype(bf16)
    intra = intra_block(weights, x)
    tail = jnp.exp(last[:, None, :] - cum) * dtb
    tail_wide = head_spread(tail.reshape(length, heads), inner).reshape(nb, GROUP, inner)
    scaled = x.reshape(nb, GROUP, inner).astype(f32) * tail_wide
    block_state = jnp.einsum("kjn,kjc->knc", bb.astype(f32), scaled, precision=exact_dot)
    block_decay = head_spread(jnp.exp(last), inner)
    cum_wide = head_spread(jnp.exp(cum).reshape(length, heads), inner)
    return dict(
        cb=cb,
        cum_wide=cum_wide,
        intra=intra,
        block_state=block_state,
        block_decay=block_decay,
    )


def stretch_states(parts, backward):
    block_state, block_decay = parts["block_state"], parts["block_decay"]
    nb = block_state.shape[0]
    order = list(range(nb - 1, -1, -1)) if backward else list(range(nb))
    starts = [None] * nb
    prefix = [None] * nb
    run_state = jnp.zeros_like(block_state[0])
    run_decay = jnp.ones_like(block_decay[0])
    for k in order:
        starts[k] = run_state
        prefix[k] = run_decay
        run_state = block_decay[k][None, :] * run_state + block_state[k]
        run_decay = run_decay * block_decay[k]
    return jnp.stack(starts), jnp.stack(prefix), run_state, run_decay


def pair_combine(earlier, later):
    (a0, s0), (a1, s1) = earlier, later
    return a1 * a0, a1[None, :] * s0 + s1


def scan_over(axis, own_decay, own_state, backward):
    peers = lax.axis_size(axis)
    step = -1 if backward else 1
    own = (own_decay, own_state)
    holder_parity = 0 if backward else 1
    first = shifted((own_decay, own_state.astype(bf16)), axis, step, 1 - holder_parity)
    first = (first[0], first[1].astype(f32))
    me = lax.axis_index(axis)
    holder = (me % 2 == 0) if backward else (me % 2 == 1)
    total = pair_combine(first, own)
    ex_decay = jnp.ones_like(own_decay)
    ex_state = jnp.zeros_like(own_state)
    in_decay, in_state = total
    distance = 2
    while distance < peers:
        got_decay, got_state = shifted(
            (in_decay, in_state.astype(bf16)), axis, step * distance, holder_parity
        )
        got_state = got_state.astype(f32)
        ex_state = ex_decay[None, :] * got_state + ex_state
        ex_decay = ex_decay * got_decay
        if distance * 2 < peers:
            in_state = in_decay[None, :] * got_state + in_state
            in_decay = in_decay * got_decay
        distance *= 2
    handed = shifted(ex_state.astype(bf16), axis, -step, holder_parity).astype(f32)
    mine = first[0][None, :] * ex_state + first[1]
    return jnp.where(holder, mine, handed)


def strand_output(parts, starts, prefix, carry, x, d_wide):
    start_states = starts + prefix[:, None, :] * carry[None]
    carried = jnp.einsum(
        "kin,knc->kic", parts["cb"].astype(f32), start_states, precision=exact_dot
    )
    length, inner = x.shape
    carried = carried.reshape(length, inner)
    return parts["intra"] + parts["cum_wide"] * carried + d_wide[None, :] * x.astype(f32)


def per_device(
    hidden,
    base_ids,
    embed,
    w_x,
    w_z,
    w_bc,
    w_dt,
    dt_bias,
    decay_rate,
    conv_x,
    conv_bc,
    d_skip,
    norm_gain,
    w_out,
):
    inner = w_x.shape[1]
    state = w_bc.shape[1] // 2
    conv = conv_x.shape[0]
    onehot = (base_ids[:, None] == jnp.arange(embed.shape[0], dtype=jnp.int32)[None, :]).astype(bf16)
    mixed_in = (hidden.astype(f32) + jnp.dot(onehot, embed, preferred_element_type=f32)).astype(bf16)
    rim = 8
    peers = lax.axis_size("ch")
    both_axes = ("ctx", "ch")
    count = lax.axis_size(both_axes)
    before, after = [], []
    for h in range(peers):
        ahead = [(q, q + h + 1) for q in range(count) if q % peers == peers - 1 and q + h + 1 < count]
        behind = [(q, q - peers + h) for q in range(count) if q % peers == 0 and q - peers + h >= 0]
        before.append(lax.ppermute(mixed_in[-rim:], both_axes, ahead))
        after.append(lax.ppermute(mixed_in[:rim], both_axes, behind))
    me = lax.axis_index("ch")
    u = gather_rows(mixed_in, "ch")
    u_ext = jnp.concatenate(
        [
            jnp.stack(before)[me],
            u,
            jnp.stack(after)[me],
        ],
        axis=0,
    )
    length, width = u.shape
    flip = flip_matrix(width)
    u_ext_flip = jnp.dot(u_ext, flip, preferred_element_type=f32).astype(bf16)
    both_ext = jnp.concatenate([u_ext, u_ext_flip], axis=0)
    both = jnp.concatenate([u_ext[rim : rim + length], u_ext_flip[rim : rim + length]], axis=0)
    x_raw = jnp.dot(both_ext, w_x, preferred_element_type=f32).astype(bf16)
    bc_raw = jnp.dot(both_ext, w_bc, preferred_element_type=f32).astype(bf16)
    z_all = jnp.dot(both, w_z, preferred_element_type=f32).astype(bf16)
    dt_all = jax.nn.softplus(jnp.dot(both, w_dt, preferred_element_type=f32) + dt_bias[None, :])
    ext = length + 2 * rim
    d_wide = head_spread(d_skip[None, :], inner)[0]

    outs = []
    sums = []
    for backward in (False, True):
        rows = slice(length, 2 * length) if backward else slice(0, length)
        ext_rows = slice(ext, 2 * ext) if backward else slice(0, ext)
        x_c = conv_silu(x_raw[ext_rows], conv_x, rim, length, backward)
        bc_c = conv_silu(bc_raw[ext_rows], conv_bc, rim, length, backward)
        parts = local_ssd(x_c, dt_all[rows], bc_c[:, :state], bc_c[:, state:], decay_rate, backward)
        starts, prefix, end_state, end_decay = stretch_states(parts, backward)
        carry = scan_over("ctx", end_decay, end_state, backward)
        y = strand_output(parts, starts, prefix, carry, x_c, d_wide)
        gated = (y * jax.nn.silu(z_all[rows].astype(f32))).astype(bf16).astype(f32)
        outs.append(gated)
        sums.append(jnp.sum(gated * gated, axis=1))
    total = lax.psum(jnp.stack(sums), "ch")
    full_inner = inner * lax.axis_size("ch")
    gain = norm_gain.astype(f32)[None, :]
    normed = [
        (g * lax.rsqrt(t / full_inner + norm_eps)[:, None] * gain).astype(bf16)
        for g, t in zip(outs, total)
    ]
    own_rows = length // peers

    def partial_for(normed_pair, target):
        nf = lax.dynamic_slice_in_dim(normed_pair[0], target * own_rows, own_rows, axis=0)
        nb_ = lax.dynamic_slice_in_dim(normed_pair[1], target * own_rows, own_rows, axis=0)
        out_f = jnp.dot(nf, w_out, preferred_element_type=f32)
        out_b = jnp.dot(nb_, w_out, preferred_element_type=f32)
        return out_f + flipped_columns(out_b, flip)

    received = []
    sent_all = []
    for d in range(1, peers):
        sent = partial_for(normed, (me + d) % peers).astype(bf16)
        sent_all.append(sent)
        route = [(i, (i + d) % peers) for i in range(peers)]
        received.append(lax.ppermute(sent, "ch", route))
    _, normed_later = lax.optimization_barrier((sent_all, normed))
    summed = partial_for(normed_later, me)
    for r in received:
        summed = summed + r.astype(f32)
    return summed.astype(bf16)


def solution(mesh):
    placed = (
        P(("ctx", "ch"), None),
        P(("ctx", "ch")),
        P(),
        P(None, "ch"),
        P(None, "ch"),
        P(),
        P(None, "ch"),
        P("ch"),
        P("ch"),
        P(None, "ch"),
        P(),
        P("ch"),
        P("ch"),
        P("ch", None),
    )
    return jax.shard_map(
        per_device, mesh=mesh, in_specs=placed, out_specs=P(("ctx", "ch"), None), check_vma=False
    )
```

```python
import jax
import jax.numpy as jnp
from jax import lax
from jax.experimental import pallas as pl
from jax.sharding import PartitionSpec as P

HEAD_DIM = 64
GROUP = 128

exact_dot = lax.Precision.HIGHEST
norm_eps = 1e-05
f32 = jnp.float32
bf16 = jnp.bfloat16


def flip_matrix(n):
    rows = lax.broadcasted_iota(jnp.int32, (n, n), 0)
    cols = lax.broadcasted_iota(jnp.int32, (n, n), 1)
    return (rows + cols == n - 1).astype(bf16)


def shifted(block, axis, distance, parity=None):
    devices = range(lax.axis_size(axis))
    route = [
        (i, i + distance)
        for i in devices
        if i + distance in devices and (parity is None or i % 2 == parity)
    ]
    return lax.ppermute(block, axis, route)


def gather_rows(block, axis):
    peers, me = lax.axis_size(axis), lax.axis_index(axis)
    got = [block] + [
        lax.ppermute(block, axis, [(i, (i + d) % peers) for i in range(peers)])
        for d in range(peers - 1, 0, -1)
    ]
    stacked = jnp.stack(got)
    rolled = jnp.roll(stacked, me, axis=0)
    return rolled.reshape(peers * block.shape[0], *block.shape[1:])


def bf16_part(values):
    return lax.reduce_precision(values, exponent_bits=8, mantissa_bits=7)


def flipped_columns(part, flip):
    hi = bf16_part(part)
    rest = part - hi
    mid = bf16_part(rest)
    lo = rest - mid
    rows = part.shape[0]
    split = jnp.concatenate([hi, mid, lo], axis=0).astype(bf16)
    pieces = jnp.dot(split, flip, preferred_element_type=f32)
    return (pieces[:rows] + pieces[rows : 2 * rows]) + pieces[2 * rows :]


def conv_silu(raw_ext, taps, rim, length, backward):
    conv = taps.shape[0]
    summed = None
    for k in range(conv):
        first = rim + conv - 1 - k if backward else rim - (conv - 1) + k
        term = taps[k][None, :] * raw_ext[first : first + length].astype(f32)
        summed = term if summed is None else summed + term
    return jax.nn.silu(summed).astype(bf16)


def intra_kernel(w_ref, x_ref, o_ref):
    lanes = 128
    per_tile = lanes // HEAD_DIM
    rows = x_ref.shape[0]
    owner = lax.broadcasted_iota(jnp.int32, (rows, lanes), 1) // HEAD_DIM
    for g in range(x_ref.shape[1] // lanes):
        tile = x_ref[:, g * lanes : (g + 1) * lanes]
        zero = jnp.zeros_like(tile)
        stacked = jnp.concatenate([jnp.where(owner == t, tile, zero) for t in range(per_tile)], axis=0)
        wide = jnp.concatenate([w_ref[0, g * per_tile + t] for t in range(per_tile)], axis=1)
        o_ref[:, g * lanes : (g + 1) * lanes] = jnp.dot(wide, stacked, preferred_element_type=f32)


def intra_block(weights, x):
    nb, heads, group, _ = weights.shape
    length, inner = x.shape
    return pl.pallas_call(
        intra_kernel,
        out_shape=jax.ShapeDtypeStruct((length, inner), f32),
        grid=(nb,),
        in_specs=[
            pl.BlockSpec((1, heads, group, group), lambda k: (k, 0, 0, 0)),
            pl.BlockSpec((group, inner), lambda k: (k, 0)),
        ],
        out_specs=pl.BlockSpec((group, inner), lambda k: (k, 0)),
    )(weights, x)


def head_spread(values, inner):
    heads = values.shape[-1]
    owner = lax.broadcasted_iota(jnp.int32, (heads, inner), 1) // HEAD_DIM
    spread = (owner == lax.broadcasted_iota(jnp.int32, (heads, inner), 0)).astype(f32)
    return jnp.dot(values, spread, precision=exact_dot)


def local_ssd(x, dt, b_mat, c_mat, rates, backward):
    length, inner = x.shape
    heads = dt.shape[1]
    nb = length // GROUP
    xb = x.reshape(nb, GROUP, heads, HEAD_DIM)
    dtb = dt.reshape(nb, GROUP, heads)
    bb = b_mat.reshape(nb, GROUP, -1)
    cb = c_mat.reshape(nb, GROUP, -1)
    step = -dtb * rates[None, None, :]
    cum = lax.cumsum(step, axis=1, reverse=backward)
    last = cum[:, 0, :] if backward else cum[:, -1, :]
    scores = jnp.einsum("kin,kjn->kij", cb, bb, preferred_element_type=f32)
    rows = lax.broadcasted_iota(jnp.int32, (GROUP, GROUP), 0)
    cols = lax.broadcasted_iota(jnp.int32, (GROUP, GROUP), 1)
    mask = (rows <= cols) if backward else (rows >= cols)
    mask = mask[None, None]
    cum_t = cum.transpose(0, 2, 1)
    gap = jnp.where(mask, cum_t[:, :, :, None] - cum_t[:, :, None, :], 0.0)
    dt_t = dtb.transpose(0, 2, 1)
    weights = jnp.where(mask, scores[:, None] * jnp.exp(gap) * dt_t[:, :, None, :], 0.0).astype(bf16)
    intra = intra_block(weights, x)
    tail = jnp.exp(last[:, None, :] - cum) * dtb
    tail_wide = head_spread(tail.reshape(length, heads), inner).reshape(nb, GROUP, inner)
    scaled = x.reshape(nb, GROUP, inner).astype(f32) * tail_wide
    block_state = jnp.einsum("kjn,kjc->knc", bb.astype(f32), scaled, precision=exact_dot)
    block_decay = head_spread(jnp.exp(last), inner)
    cum_wide = head_spread(jnp.exp(cum).reshape(length, heads), inner)
    return dict(
        cb=cb,
        cum_wide=cum_wide,
        intra=intra,
        block_state=block_state,
        block_decay=block_decay,
    )


def stretch_states(parts, backward):
    block_state, block_decay = parts["block_state"], parts["block_decay"]
    nb = block_state.shape[0]
    order = list(range(nb - 1, -1, -1)) if backward else list(range(nb))
    starts = [None] * nb
    prefix = [None] * nb
    run_state = jnp.zeros_like(block_state[0])
    run_decay = jnp.ones_like(block_decay[0])
    for k in order:
        starts[k] = run_state
        prefix[k] = run_decay
        run_state = block_decay[k][None, :] * run_state + block_state[k]
        run_decay = run_decay * block_decay[k]
    return jnp.stack(starts), jnp.stack(prefix), run_state, run_decay


def pair_combine(earlier, later):
    (a0, s0), (a1, s1) = earlier, later
    return a1 * a0, a1[None, :] * s0 + s1


def scan_over(axis, own_decay, own_state, backward):
    peers = lax.axis_size(axis)
    step = -1 if backward else 1
    own = (own_decay, own_state)
    holder_parity = 0 if backward else 1
    first = shifted((own_decay, own_state.astype(bf16)), axis, step, 1 - holder_parity)
    first = (first[0], first[1].astype(f32))
    me = lax.axis_index(axis)
    holder = (me % 2 == 0) if backward else (me % 2 == 1)
    total = pair_combine(first, own)
    ex_decay = jnp.ones_like(own_decay)
    ex_state = jnp.zeros_like(own_state)
    in_decay, in_state = total
    distance = 2
    while distance < peers:
        got_decay, got_state = shifted(
            (in_decay, in_state.astype(bf16)), axis, step * distance, holder_parity
        )
        got_state = got_state.astype(f32)
        ex_state = ex_decay[None, :] * got_state + ex_state
        ex_decay = ex_decay * got_decay
        if distance * 2 < peers:
            in_state = in_decay[None, :] * got_state + in_state
            in_decay = in_decay * got_decay
        distance *= 2
    handed = shifted(ex_state.astype(bf16), axis, -step, holder_parity).astype(f32)
    mine = first[0][None, :] * ex_state + first[1]
    return jnp.where(holder, mine, handed)


def strand_output(parts, starts, prefix, carry, x, d_wide):
    start_states = starts + prefix[:, None, :] * carry[None]
    carried = jnp.einsum(
        "kin,knc->kic", parts["cb"].astype(f32), start_states, precision=exact_dot
    )
    length, inner = x.shape
    carried = carried.reshape(length, inner)
    return parts["intra"] + parts["cum_wide"] * carried + d_wide[None, :] * x.astype(f32)


def per_device(
    hidden,
    base_ids,
    embed,
    w_x,
    w_z,
    w_bc,
    w_dt,
    dt_bias,
    decay_rate,
    conv_x,
    conv_bc,
    d_skip,
    norm_gain,
    w_out,
):
    inner = w_x.shape[1]
    state = w_bc.shape[1] // 2
    conv = conv_x.shape[0]
    onehot = (base_ids[:, None] == jnp.arange(embed.shape[0], dtype=jnp.int32)[None, :]).astype(bf16)
    mixed_in = (hidden.astype(f32) + jnp.dot(onehot, embed, preferred_element_type=f32)).astype(bf16)
    rim = 8
    peers = lax.axis_size("ch")
    both_axes = ("ctx", "ch")
    count = lax.axis_size(both_axes)
    before, after = [], []
    for h in range(peers):
        ahead = [(q, q + h + 1) for q in range(count) if q % peers == peers - 1 and q + h + 1 < count]
        behind = [(q, q - peers + h) for q in range(count) if q % peers == 0 and q - peers + h >= 0]
        before.append(lax.ppermute(mixed_in[-rim:], both_axes, ahead))
        after.append(lax.ppermute(mixed_in[:rim], both_axes, behind))
    me = lax.axis_index("ch")
    u = gather_rows(mixed_in, "ch")
    u_ext = jnp.concatenate(
        [
            jnp.stack(before)[me],
            u,
            jnp.stack(after)[me],
        ],
        axis=0,
    )
    length, width = u.shape
    flip = flip_matrix(width)
    u_ext_flip = jnp.dot(u_ext, flip, preferred_element_type=f32).astype(bf16)
    both_ext = jnp.concatenate([u_ext, u_ext_flip], axis=0)
    both = jnp.concatenate([u_ext[rim : rim + length], u_ext_flip[rim : rim + length]], axis=0)
    x_raw = jnp.dot(both_ext, w_x, preferred_element_type=f32).astype(bf16)
    bc_raw = jnp.dot(both_ext, w_bc, preferred_element_type=f32).astype(bf16)
    z_all = jnp.dot(both, w_z, preferred_element_type=f32).astype(bf16)
    dt_all = jax.nn.softplus(jnp.dot(both, w_dt, preferred_element_type=f32) + dt_bias[None, :])
    ext = length + 2 * rim
    d_wide = head_spread(d_skip[None, :], inner)[0]

    outs = []
    sums = []
    for backward in (False, True):
        rows = slice(length, 2 * length) if backward else slice(0, length)
        ext_rows = slice(ext, 2 * ext) if backward else slice(0, ext)
        x_c = conv_silu(x_raw[ext_rows], conv_x, rim, length, backward)
        bc_c = conv_silu(bc_raw[ext_rows], conv_bc, rim, length, backward)
        parts = local_ssd(x_c, dt_all[rows], bc_c[:, :state], bc_c[:, state:], decay_rate, backward)
        starts, prefix, end_state, end_decay = stretch_states(parts, backward)
        carry = scan_over("ctx", end_decay, end_state, backward)
        y = strand_output(parts, starts, prefix, carry, x_c, d_wide)
        gated = (y * jax.nn.silu(z_all[rows].astype(f32))).astype(bf16).astype(f32)
        outs.append(gated)
        sums.append(jnp.sum(gated * gated, axis=1))
    local_sums = jnp.stack(sums)
    total = local_sums
    for d in range(1, peers):
        route = [(i, (i + d) % peers) for i in range(peers)]
        total = total + lax.ppermute(local_sums, "ch", route)
    full_inner = inner * lax.axis_size("ch")
    gain = norm_gain.astype(f32)[None, :]
    normed = [
        (g * lax.rsqrt(t / full_inner + norm_eps)[:, None] * gain).astype(bf16)
        for g, t in zip(outs, total)
    ]
    own_rows = length // peers

    def partial_for(normed_pair, target):
        nf = lax.dynamic_slice_in_dim(normed_pair[0], target * own_rows, own_rows, axis=0)
        nb_ = lax.dynamic_slice_in_dim(normed_pair[1], target * own_rows, own_rows, axis=0)
        out_f = jnp.dot(nf, w_out, preferred_element_type=f32)
        out_b = jnp.dot(nb_, w_out, preferred_element_type=f32)
        return out_f + flipped_columns(out_b, flip)

    received = []
    sent_all = []
    for d in range(1, peers):
        sent = partial_for(normed, (me + d) % peers).astype(bf16)
        sent_all.append(sent)
        route = [(i, (i + d) % peers) for i in range(peers)]
        received.append(lax.ppermute(sent, "ch", route))
    _, normed_later = lax.optimization_barrier((sent_all, normed))
    summed = partial_for(normed_later, me)
    for r in received:
        summed = summed + r.astype(f32)
    return summed.astype(bf16)


def solution(mesh):
    placed = (
        P(("ctx", "ch"), None),
        P(("ctx", "ch")),
        P(),
        P(None, "ch"),
        P(None, "ch"),
        P(),
        P(None, "ch"),
        P("ch"),
        P("ch"),
        P(None, "ch"),
        P(),
        P("ch"),
        P("ch"),
        P("ch", None),
    )
    return jax.shard_map(
        per_device, mesh=mesh, in_specs=placed, out_specs=P(("ctx", "ch"), None), check_vma=False
    )
```

```python
import jax
import jax.numpy as jnp
from jax import lax
from jax.experimental import pallas as pl
from jax.sharding import PartitionSpec as P

HEAD_DIM = 64
GROUP = 128

exact_dot = lax.Precision.HIGHEST
norm_eps = 1e-05
f32 = jnp.float32
bf16 = jnp.bfloat16


def flip_matrix(n):
    rows = lax.broadcasted_iota(jnp.int32, (n, n), 0)
    cols = lax.broadcasted_iota(jnp.int32, (n, n), 1)
    return (rows + cols == n - 1).astype(bf16)


def shifted(block, axis, distance, parity=None):
    devices = range(lax.axis_size(axis))
    route = [
        (i, i + distance)
        for i in devices
        if i + distance in devices and (parity is None or i % 2 == parity)
    ]
    return lax.ppermute(block, axis, route)


def gather_rows(block, axis):
    peers, me = lax.axis_size(axis), lax.axis_index(axis)
    got = [block] + [
        lax.ppermute(block, axis, [(i, (i + d) % peers) for i in range(peers)])
        for d in range(peers - 1, 0, -1)
    ]
    stacked = jnp.stack(got)
    rolled = jnp.roll(stacked, me, axis=0)
    return rolled.reshape(peers * block.shape[0], *block.shape[1:])


def bf16_part(values):
    return lax.reduce_precision(values, exponent_bits=8, mantissa_bits=7)


def flipped_columns(part, flip):
    hi = bf16_part(part)
    rest = part - hi
    mid = bf16_part(rest)
    lo = rest - mid
    rows = part.shape[0]
    split = jnp.concatenate([hi, mid, lo], axis=0).astype(bf16)
    pieces = jnp.dot(split, flip, preferred_element_type=f32)
    return (pieces[:rows] + pieces[rows : 2 * rows]) + pieces[2 * rows :]


def conv_silu(raw_ext, taps, rim, length, backward):
    conv = taps.shape[0]
    summed = None
    for k in range(conv):
        first = rim + conv - 1 - k if backward else rim - (conv - 1) + k
        term = taps[k][None, :] * raw_ext[first : first + length].astype(f32)
        summed = term if summed is None else summed + term
    return jax.nn.silu(summed).astype(bf16)


def intra_kernel(w_ref, x_ref, o_ref):
    lanes = 128
    per_tile = lanes // HEAD_DIM
    rows = x_ref.shape[0]
    owner = lax.broadcasted_iota(jnp.int32, (rows, lanes), 1) // HEAD_DIM
    for g in range(x_ref.shape[1] // lanes):
        tile = x_ref[:, g * lanes : (g + 1) * lanes]
        zero = jnp.zeros_like(tile)
        stacked = jnp.concatenate([jnp.where(owner == t, tile, zero) for t in range(per_tile)], axis=0)
        wide = jnp.concatenate([w_ref[0, g * per_tile + t] for t in range(per_tile)], axis=1)
        o_ref[:, g * lanes : (g + 1) * lanes] = jnp.dot(wide, stacked, preferred_element_type=f32)


def intra_block(weights, x):
    nb, heads, group, _ = weights.shape
    length, inner = x.shape
    return pl.pallas_call(
        intra_kernel,
        out_shape=jax.ShapeDtypeStruct((length, inner), f32),
        grid=(nb,),
        in_specs=[
            pl.BlockSpec((1, heads, group, group), lambda k: (k, 0, 0, 0)),
            pl.BlockSpec((group, inner), lambda k: (k, 0)),
        ],
        out_specs=pl.BlockSpec((group, inner), lambda k: (k, 0)),
    )(weights, x)


def head_spread(values, inner):
    heads = values.shape[-1]
    owner = lax.broadcasted_iota(jnp.int32, (heads, inner), 1) // HEAD_DIM
    spread = (owner == lax.broadcasted_iota(jnp.int32, (heads, inner), 0)).astype(f32)
    return jnp.dot(values, spread, precision=exact_dot)


def local_ssd(x, dt, b_mat, c_mat, rates, backward):
    length, inner = x.shape
    heads = dt.shape[1]
    nb = length // GROUP
    xb = x.reshape(nb, GROUP, heads, HEAD_DIM)
    dtb = dt.reshape(nb, GROUP, heads)
    bb = b_mat.reshape(nb, GROUP, -1)
    cb = c_mat.reshape(nb, GROUP, -1)
    step = -dtb * rates[None, None, :]
    cum = lax.cumsum(step, axis=1, reverse=backward)
    last = cum[:, 0, :] if backward else cum[:, -1, :]
    scores = jnp.einsum("kin,kjn->kij", cb, bb, preferred_element_type=f32)
    rows = lax.broadcasted_iota(jnp.int32, (GROUP, GROUP), 0)
    cols = lax.broadcasted_iota(jnp.int32, (GROUP, GROUP), 1)
    mask = (rows <= cols) if backward else (rows >= cols)
    mask = mask[None, None]
    cum_t = cum.transpose(0, 2, 1)
    gap = jnp.where(mask, cum_t[:, :, :, None] - cum_t[:, :, None, :], 0.0)
    dt_t = dtb.transpose(0, 2, 1)
    weights = jnp.where(mask, scores[:, None] * jnp.exp(gap) * dt_t[:, :, None, :], 0.0).astype(bf16)
    intra = intra_block(weights, x)
    tail = jnp.exp(last[:, None, :] - cum) * dtb
    tail_wide = head_spread(tail.reshape(length, heads), inner).reshape(nb, GROUP, inner)
    scaled = x.reshape(nb, GROUP, inner).astype(f32) * tail_wide
    block_state = jnp.einsum("kjn,kjc->knc", bb.astype(f32), scaled, precision=exact_dot)
    intra, block_state = lax.optimization_barrier((intra, block_state))
    block_decay = head_spread(jnp.exp(last), inner)
    cum_wide = head_spread(jnp.exp(cum).reshape(length, heads), inner)
    return dict(
        cb=cb,
        cum_wide=cum_wide,
        intra=intra,
        block_state=block_state,
        block_decay=block_decay,
    )


def stretch_states(parts, backward):
    block_state, block_decay = parts["block_state"], parts["block_decay"]
    nb = block_state.shape[0]
    order = list(range(nb - 1, -1, -1)) if backward else list(range(nb))
    starts = [None] * nb
    prefix = [None] * nb
    run_state = jnp.zeros_like(block_state[0])
    run_decay = jnp.ones_like(block_decay[0])
    for k in order:
        starts[k] = run_state
        prefix[k] = run_decay
        run_state = block_decay[k][None, :] * run_state + block_state[k]
        run_decay = run_decay * block_decay[k]
    return jnp.stack(starts), jnp.stack(prefix), run_state, run_decay


def pair_combine(earlier, later):
    (a0, s0), (a1, s1) = earlier, later
    return a1 * a0, a1[None, :] * s0 + s1


def scan_over(axis, own_decay, own_state, backward):
    peers = lax.axis_size(axis)
    step = -1 if backward else 1
    own = (own_decay, own_state)
    holder_parity = 0 if backward else 1
    first = shifted((own_decay, own_state.astype(bf16)), axis, step, 1 - holder_parity)
    first = (first[0], first[1].astype(f32))
    me = lax.axis_index(axis)
    holder = (me % 2 == 0) if backward else (me % 2 == 1)
    total = pair_combine(first, own)
    ex_decay = jnp.ones_like(own_decay)
    ex_state = jnp.zeros_like(own_state)
    in_decay, in_state = total
    distance = 2
    while distance < peers:
        got_decay, got_state = shifted(
            (in_decay, in_state.astype(bf16)), axis, step * distance, holder_parity
        )
        got_state = got_state.astype(f32)
        ex_state = ex_decay[None, :] * got_state + ex_state
        ex_decay = ex_decay * got_decay
        if distance * 2 < peers:
            in_state = in_decay[None, :] * got_state + in_state
            in_decay = in_decay * got_decay
        distance *= 2
    handed = shifted(ex_state.astype(bf16), axis, -step, holder_parity).astype(f32)
    mine = first[0][None, :] * ex_state + first[1]
    return jnp.where(holder, mine, handed)


def strand_output(parts, starts, prefix, carry, x, d_wide):
    start_states = starts + prefix[:, None, :] * carry[None]
    carried = jnp.einsum(
        "kin,knc->kic", parts["cb"].astype(f32), start_states, precision=exact_dot
    )
    length, inner = x.shape
    carried = carried.reshape(length, inner)
    return parts["intra"] + parts["cum_wide"] * carried + d_wide[None, :] * x.astype(f32)


def per_device(
    hidden,
    base_ids,
    embed,
    w_x,
    w_z,
    w_bc,
    w_dt,
    dt_bias,
    decay_rate,
    conv_x,
    conv_bc,
    d_skip,
    norm_gain,
    w_out,
):
    inner = w_x.shape[1]
    state = w_bc.shape[1] // 2
    conv = conv_x.shape[0]
    onehot = (base_ids[:, None] == jnp.arange(embed.shape[0], dtype=jnp.int32)[None, :]).astype(bf16)
    mixed_in = (hidden.astype(f32) + jnp.dot(onehot, embed, preferred_element_type=f32)).astype(bf16)
    rim = 8
    peers = lax.axis_size("ch")
    both_axes = ("ctx", "ch")
    count = lax.axis_size(both_axes)
    before, after = [], []
    for h in range(peers):
        ahead = [(q, q + h + 1) for q in range(count) if q % peers == peers - 1 and q + h + 1 < count]
        behind = [(q, q - peers + h) for q in range(count) if q % peers == 0 and q - peers + h >= 0]
        before.append(lax.ppermute(mixed_in[-rim:], both_axes, ahead))
        after.append(lax.ppermute(mixed_in[:rim], both_axes, behind))
    me = lax.axis_index("ch")
    u = gather_rows(mixed_in, "ch")
    u_ext = jnp.concatenate(
        [
            jnp.stack(before)[me],
            u,
            jnp.stack(after)[me],
        ],
        axis=0,
    )
    length, width = u.shape
    flip = flip_matrix(width)
    u_ext_flip = jnp.dot(u_ext, flip, preferred_element_type=f32).astype(bf16)
    both_ext = jnp.concatenate([u_ext, u_ext_flip], axis=0)
    both = jnp.concatenate([u_ext[rim : rim + length], u_ext_flip[rim : rim + length]], axis=0)
    x_raw = jnp.dot(both_ext, w_x, preferred_element_type=f32).astype(bf16)
    bc_raw = jnp.dot(both_ext, w_bc, preferred_element_type=f32).astype(bf16)
    z_all = jnp.dot(both, w_z, preferred_element_type=f32).astype(bf16)
    dt_all = jax.nn.softplus(jnp.dot(both, w_dt, preferred_element_type=f32) + dt_bias[None, :])
    ext = length + 2 * rim
    d_wide = head_spread(d_skip[None, :], inner)[0]

    outs = []
    sums = []
    for backward in (False, True):
        rows = slice(length, 2 * length) if backward else slice(0, length)
        ext_rows = slice(ext, 2 * ext) if backward else slice(0, ext)
        x_c = conv_silu(x_raw[ext_rows], conv_x, rim, length, backward)
        bc_c = conv_silu(bc_raw[ext_rows], conv_bc, rim, length, backward)
        parts = local_ssd(x_c, dt_all[rows], bc_c[:, :state], bc_c[:, state:], decay_rate, backward)
        starts, prefix, end_state, end_decay = stretch_states(parts, backward)
        carry = scan_over("ctx", end_decay, end_state, backward)
        y = strand_output(parts, starts, prefix, carry, x_c, d_wide)
        gated = (y * jax.nn.silu(z_all[rows].astype(f32))).astype(bf16).astype(f32)
        outs.append(gated)
        sums.append(jnp.sum(gated * gated, axis=1))
    total = lax.psum(jnp.stack(sums), "ch")
    full_inner = inner * lax.axis_size("ch")
    gain = norm_gain.astype(f32)[None, :]
    normed = [
        (g * lax.rsqrt(t / full_inner + norm_eps)[:, None] * gain).astype(bf16)
        for g, t in zip(outs, total)
    ]
    own_rows = length // peers

    def partial_for(normed_pair, target):
        nf = lax.dynamic_slice_in_dim(normed_pair[0], target * own_rows, own_rows, axis=0)
        nb_ = lax.dynamic_slice_in_dim(normed_pair[1], target * own_rows, own_rows, axis=0)
        out_f = jnp.dot(nf, w_out, preferred_element_type=f32)
        out_b = jnp.dot(nb_, w_out, preferred_element_type=f32)
        return out_f + flipped_columns(out_b, flip)

    received = []
    sent_all = []
    for d in range(1, peers):
        sent = partial_for(normed, (me + d) % peers).astype(bf16)
        sent_all.append(sent)
        route = [(i, (i + d) % peers) for i in range(peers)]
        received.append(lax.ppermute(sent, "ch", route))
    _, normed_later = lax.optimization_barrier((sent_all, normed))
    summed = partial_for(normed_later, me)
    for r in received:
        summed = summed + r.astype(f32)
    return summed.astype(bf16)


def solution(mesh):
    placed = (
        P(("ctx", "ch"), None),
        P(("ctx", "ch")),
        P(),
        P(None, "ch"),
        P(None, "ch"),
        P(),
        P(None, "ch"),
        P("ch"),
        P("ch"),
        P(None, "ch"),
        P(),
        P("ch"),
        P("ch"),
        P("ch", None),
    )
    return jax.shard_map(
        per_device, mesh=mesh, in_specs=placed, out_specs=P(("ctx", "ch"), None), check_vma=False
    )
```

```python
import jax
import jax.numpy as jnp
from jax import lax
from jax.experimental import pallas as pl
from jax.sharding import PartitionSpec as P

HEAD_DIM = 64
GROUP = 128

exact_dot = lax.Precision.HIGHEST
norm_eps = 1e-05
f32 = jnp.float32
bf16 = jnp.bfloat16


def flip_matrix(n):
    rows = lax.broadcasted_iota(jnp.int32, (n, n), 0)
    cols = lax.broadcasted_iota(jnp.int32, (n, n), 1)
    return (rows + cols == n - 1).astype(bf16)


def shifted(block, axis, distance, parity=None):
    devices = range(lax.axis_size(axis))
    route = [
        (i, i + distance)
        for i in devices
        if i + distance in devices and (parity is None or i % 2 == parity)
    ]
    return lax.ppermute(block, axis, route)


def gather_rows(block, axis):
    peers, me = lax.axis_size(axis), lax.axis_index(axis)
    got = [block] + [
        lax.ppermute(block, axis, [(i, (i + d) % peers) for i in range(peers)])
        for d in range(peers - 1, 0, -1)
    ]
    stacked = jnp.stack(got)
    rolled = jnp.roll(stacked, me, axis=0)
    return rolled.reshape(peers * block.shape[0], *block.shape[1:])


def bf16_part(values):
    return lax.reduce_precision(values, exponent_bits=8, mantissa_bits=7)


def flipped_columns(part, flip):
    hi = bf16_part(part)
    rest = part - hi
    mid = bf16_part(rest)
    lo = rest - mid
    rows = part.shape[0]
    split = jnp.concatenate([hi, mid, lo], axis=0).astype(bf16)
    pieces = jnp.dot(split, flip, preferred_element_type=f32)
    return (pieces[:rows] + pieces[rows : 2 * rows]) + pieces[2 * rows :]


def conv_silu(raw_ext, taps, rim, length, backward):
    conv = taps.shape[0]
    summed = None
    for k in range(conv):
        first = rim + conv - 1 - k if backward else rim - (conv - 1) + k
        term = taps[k][None, :] * raw_ext[first : first + length].astype(f32)
        summed = term if summed is None else summed + term
    return jax.nn.silu(summed).astype(bf16)


def intra_kernel(w_ref, x_ref, o_ref):
    lanes = 128
    per_tile = lanes // HEAD_DIM
    rows = x_ref.shape[0]
    owner = lax.broadcasted_iota(jnp.int32, (rows, lanes), 1) // HEAD_DIM
    for g in range(x_ref.shape[1] // lanes):
        tile = x_ref[:, g * lanes : (g + 1) * lanes]
        zero = jnp.zeros_like(tile)
        stacked = jnp.concatenate([jnp.where(owner == t, tile, zero) for t in range(per_tile)], axis=0)
        wide = jnp.concatenate([w_ref[0, g * per_tile + t] for t in range(per_tile)], axis=1)
        o_ref[:, g * lanes : (g + 1) * lanes] = jnp.dot(wide, stacked, preferred_element_type=f32)


def intra_block(weights, x):
    nb, heads, group, _ = weights.shape
    length, inner = x.shape
    return pl.pallas_call(
        intra_kernel,
        out_shape=jax.ShapeDtypeStruct((length, inner), f32),
        grid=(nb,),
        in_specs=[
            pl.BlockSpec((1, heads, group, group), lambda k: (k, 0, 0, 0)),
            pl.BlockSpec((group, inner), lambda k: (k, 0)),
        ],
        out_specs=pl.BlockSpec((group, inner), lambda k: (k, 0)),
    )(weights, x)


def head_spread(values, inner):
    heads = values.shape[-1]
    owner = lax.broadcasted_iota(jnp.int32, (heads, inner), 1) // HEAD_DIM
    spread = (owner == lax.broadcasted_iota(jnp.int32, (heads, inner), 0)).astype(f32)
    return jnp.dot(values, spread, precision=exact_dot)


def local_ssd(x, dt, b_mat, c_mat, rates, backward):
    length, inner = x.shape
    heads = dt.shape[1]
    nb = length // GROUP
    xb = x.reshape(nb, GROUP, heads, HEAD_DIM)
    dtb = dt.reshape(nb, GROUP, heads)
    bb = b_mat.reshape(nb, GROUP, -1)
    cb = c_mat.reshape(nb, GROUP, -1)
    step = -dtb * rates[None, None, :]
    cum = lax.cumsum(step, axis=1, reverse=backward)
    last = cum[:, 0, :] if backward else cum[:, -1, :]
    scores = jnp.einsum("kin,kjn->kij", cb, bb, preferred_element_type=f32)
    rows = lax.broadcasted_iota(jnp.int32, (GROUP, GROUP), 0)
    cols = lax.broadcasted_iota(jnp.int32, (GROUP, GROUP), 1)
    mask = (rows <= cols) if backward else (rows >= cols)
    mask = mask[None, None]
    cum_t = cum.transpose(0, 2, 1)
    gap = jnp.where(mask, cum_t[:, :, :, None] - cum_t[:, :, None, :], 0.0)
    dt_t = dtb.transpose(0, 2, 1)
    weights = jnp.where(mask, scores[:, None] * jnp.exp(gap) * dt_t[:, :, None, :], 0.0).astype(bf16)
    intra = intra_block(weights, x)
    tail = jnp.exp(last[:, None, :] - cum) * dtb
    tail_wide = head_spread(tail.reshape(length, heads), inner).reshape(nb, GROUP, inner)
    scaled = x.reshape(nb, GROUP, inner).astype(f32) * tail_wide
    block_state = jnp.einsum("kjn,kjc->knc", bb.astype(f32), scaled, precision=exact_dot)
    block_decay = head_spread(jnp.exp(last), inner)
    cum_wide = head_spread(jnp.exp(cum).reshape(length, heads), inner)
    return dict(
        cb=cb,
        cum_wide=cum_wide,
        intra=intra,
        block_state=block_state,
        block_decay=block_decay,
    )


def stretch_states(parts, backward):
    block_state, block_decay = parts["block_state"], parts["block_decay"]
    nb = block_state.shape[0]
    order = list(range(nb - 1, -1, -1)) if backward else list(range(nb))
    starts = [None] * nb
    prefix = [None] * nb
    run_state = jnp.zeros_like(block_state[0])
    run_decay = jnp.ones_like(block_decay[0])
    for k in order:
        starts[k] = run_state
        prefix[k] = run_decay
        run_state = block_decay[k][None, :] * run_state + block_state[k]
        run_decay = run_decay * block_decay[k]
    return jnp.stack(starts), jnp.stack(prefix), run_state, run_decay


def pair_combine(earlier, later):
    (a0, s0), (a1, s1) = earlier, later
    return a1 * a0, a1[None, :] * s0 + s1


def scan_over(axis, own_decay, own_state, backward):
    peers = lax.axis_size(axis)
    step = -1 if backward else 1
    own = (own_decay, own_state)
    holder_parity = 0 if backward else 1
    first = shifted((own_decay, own_state.astype(bf16)), axis, step, 1 - holder_parity)
    first = (first[0], first[1].astype(f32))
    me = lax.axis_index(axis)
    holder = (me % 2 == 0) if backward else (me % 2 == 1)
    total = pair_combine(first, own)
    ex_decay = jnp.ones_like(own_decay)
    ex_state = jnp.zeros_like(own_state)
    in_decay, in_state = total
    distance = 2
    while distance < peers:
        got_decay, got_state = shifted(
            (in_decay, in_state.astype(bf16)), axis, step * distance, holder_parity
        )
        got_state = got_state.astype(f32)
        ex_state = ex_decay[None, :] * got_state + ex_state
        ex_decay = ex_decay * got_decay
        if distance * 2 < peers:
            in_state = in_decay[None, :] * got_state + in_state
            in_decay = in_decay * got_decay
        distance *= 2
    handed = shifted(ex_state.astype(bf16), axis, -step, holder_parity).astype(f32)
    mine = first[0][None, :] * ex_state + first[1]
    return jnp.where(holder, mine, handed)


def strand_output(parts, starts, prefix, carry, x, d_wide):
    start_states = starts + prefix[:, None, :] * carry[None]
    carried = jnp.einsum(
        "kin,knc->kic", parts["cb"].astype(f32), start_states, precision=exact_dot
    )
    length, inner = x.shape
    carried = carried.reshape(length, inner)
    return parts["intra"] + parts["cum_wide"] * carried + d_wide[None, :] * x.astype(f32)


def per_device(
    hidden,
    base_ids,
    embed,
    w_x,
    w_z,
    w_bc,
    w_dt,
    dt_bias,
    decay_rate,
    conv_x,
    conv_bc,
    d_skip,
    norm_gain,
    w_out,
):
    inner = w_x.shape[1]
    state = w_bc.shape[1] // 2
    conv = conv_x.shape[0]
    onehot = (base_ids[:, None] == jnp.arange(embed.shape[0], dtype=jnp.int32)[None, :]).astype(bf16)
    mixed_in = (hidden.astype(f32) + jnp.dot(onehot, embed, preferred_element_type=f32)).astype(bf16)
    rim = 8
    peers = lax.axis_size("ch")
    both_axes = ("ctx", "ch")
    count = lax.axis_size(both_axes)
    before, after = [], []
    for h in range(peers):
        ahead = [(q, q + h + 1) for q in range(count) if q % peers == peers - 1 and q + h + 1 < count]
        behind = [(q, q - peers + h) for q in range(count) if q % peers == 0 and q - peers + h >= 0]
        before.append(lax.ppermute(mixed_in[-rim:], both_axes, ahead))
        after.append(lax.ppermute(mixed_in[:rim], both_axes, behind))
    me = lax.axis_index("ch")
    u = gather_rows(mixed_in, "ch")
    u_ext = jnp.concatenate(
        [
            jnp.stack(before)[me],
            u,
            jnp.stack(after)[me],
        ],
        axis=0,
    )
    length, width = u.shape
    flip = flip_matrix(width)
    u_ext_flip = jnp.dot(u_ext, flip, preferred_element_type=f32).astype(bf16)
    both_ext = jnp.concatenate([u_ext, u_ext_flip], axis=0)
    both = jnp.concatenate([u_ext[rim : rim + length], u_ext_flip[rim : rim + length]], axis=0)
    x_raw = jnp.dot(both_ext, w_x, preferred_element_type=f32).astype(bf16)
    bc_raw = jnp.dot(both_ext, w_bc, preferred_element_type=f32).astype(bf16)
    z_all = jnp.dot(both, w_z, preferred_element_type=f32).astype(bf16)
    dt_all = jax.nn.softplus(jnp.dot(both, w_dt, preferred_element_type=f32) + dt_bias[None, :])
    ext = length + 2 * rim
    d_wide = head_spread(d_skip[None, :], inner)[0]

    outs = []
    sums = []
    for backward in (False, True):
        rows = slice(length, 2 * length) if backward else slice(0, length)
        ext_rows = slice(ext, 2 * ext) if backward else slice(0, ext)
        x_c = conv_silu(x_raw[ext_rows], conv_x, rim, length, backward)
        bc_c = conv_silu(bc_raw[ext_rows], conv_bc, rim, length, backward)
        parts = local_ssd(x_c, dt_all[rows], bc_c[:, :state], bc_c[:, state:], decay_rate, backward)
        starts, prefix, end_state, end_decay = stretch_states(parts, backward)
        carry = scan_over("ctx", end_decay, end_state, backward)
        y = strand_output(parts, starts, prefix, carry, x_c, d_wide)
        gated = (y * jax.nn.silu(z_all[rows].astype(f32))).astype(bf16).astype(f32)
        outs.append(gated)
        sums.append(jnp.sum(gated * gated, axis=1))
    total = lax.psum(jnp.stack(sums), "ch")
    full_inner = inner * lax.axis_size("ch")
    gain = norm_gain.astype(f32)[None, :]
    normed = [
        (g * lax.rsqrt(t / full_inner + norm_eps)[:, None] * gain).astype(bf16)
        for g, t in zip(outs, total)
    ]
    own_rows = length // peers

    def partial_for(normed_pair, target):
        nf = lax.dynamic_slice_in_dim(normed_pair[0], target * own_rows, own_rows, axis=0)
        nb_ = lax.dynamic_slice_in_dim(normed_pair[1], target * own_rows, own_rows, axis=0)
        out_f = jnp.dot(nf, w_out, preferred_element_type=f32)
        out_b = jnp.dot(nb_, w_out, preferred_element_type=f32)
        return out_f + flipped_columns(out_b, flip)

    half = own_rows // 2

    def partial_rows(normed_pair, first, count):
        nf = lax.dynamic_slice_in_dim(normed_pair[0], first, count, axis=0)
        nb_ = lax.dynamic_slice_in_dim(normed_pair[1], first, count, axis=0)
        out_f = jnp.dot(nf, w_out, preferred_element_type=f32)
        out_b = jnp.dot(nb_, w_out, preferred_element_type=f32)
        return out_f + flipped_columns(out_b, flip)

    received = []
    sent_all = []
    state = normed
    for d in range(1, peers):
        route = [(i, (i + d) % peers) for i in range(peers)]
        target = (me + d) % peers
        for piece in range(2):
            sent = partial_rows(state, target * own_rows + piece * half, half).astype(bf16)
            sent_all.append(sent)
            received.append(lax.ppermute(sent, "ch", route))
            _, state = lax.optimization_barrier((sent, state))
    summed = partial_for(state, me)
    pieces = len(received) // 2
    for d in range(pieces):
        summed = summed + jnp.concatenate([received[2 * d], received[2 * d + 1]], axis=0).astype(f32)
    return summed.astype(bf16)


def solution(mesh):
    placed = (
        P(("ctx", "ch"), None),
        P(("ctx", "ch")),
        P(),
        P(None, "ch"),
        P(None, "ch"),
        P(),
        P(None, "ch"),
        P("ch"),
        P("ch"),
        P(None, "ch"),
        P(),
        P("ch"),
        P("ch"),
        P("ch", None),
    )
    return jax.shard_map(
        per_device, mesh=mesh, in_specs=placed, out_specs=P(("ctx", "ch"), None), check_vma=False
    )
```

```python
import jax
import jax.numpy as jnp
from jax import lax
from jax.experimental import pallas as pl
from jax.sharding import PartitionSpec as P

HEAD_DIM = 64
GROUP = 128

exact_dot = lax.Precision.HIGHEST
norm_eps = 1e-05
f32 = jnp.float32
bf16 = jnp.bfloat16


def flip_matrix(n):
    rows = lax.broadcasted_iota(jnp.int32, (n, n), 0)
    cols = lax.broadcasted_iota(jnp.int32, (n, n), 1)
    return (rows + cols == n - 1).astype(bf16)


def shifted(block, axis, distance, parity=None):
    devices = range(lax.axis_size(axis))
    route = [
        (i, i + distance)
        for i in devices
        if i + distance in devices and (parity is None or i % 2 == parity)
    ]
    return lax.ppermute(block, axis, route)


def gather_rows(block, axis):
    peers, me = lax.axis_size(axis), lax.axis_index(axis)
    got = [block] + [
        lax.ppermute(block, axis, [(i, (i + d) % peers) for i in range(peers)])
        for d in range(peers - 1, 0, -1)
    ]
    stacked = jnp.stack(got)
    rolled = jnp.roll(stacked, me, axis=0)
    return rolled.reshape(peers * block.shape[0], *block.shape[1:])


def bf16_part(values):
    return lax.reduce_precision(values, exponent_bits=8, mantissa_bits=7)


def flipped_columns(part, flip):
    hi = bf16_part(part)
    lo = part - hi
    rows = part.shape[0]
    split = jnp.concatenate([hi, lo], axis=0).astype(bf16)
    pieces = jnp.dot(split, flip, preferred_element_type=f32)
    return pieces[:rows] + pieces[rows:]


def conv_silu(raw_ext, taps, rim, length, backward):
    conv = taps.shape[0]
    summed = None
    for k in range(conv):
        first = rim + conv - 1 - k if backward else rim - (conv - 1) + k
        term = taps[k][None, :] * raw_ext[first : first + length].astype(f32)
        summed = term if summed is None else summed + term
    return jax.nn.silu(summed).astype(bf16)


def intra_kernel(w_ref, x_ref, o_ref):
    lanes = 128
    per_tile = lanes // HEAD_DIM
    rows = x_ref.shape[0]
    owner = lax.broadcasted_iota(jnp.int32, (rows, lanes), 1) // HEAD_DIM
    for g in range(x_ref.shape[1] // lanes):
        tile = x_ref[:, g * lanes : (g + 1) * lanes]
        zero = jnp.zeros_like(tile)
        stacked = jnp.concatenate([jnp.where(owner == t, tile, zero) for t in range(per_tile)], axis=0)
        wide = jnp.concatenate([w_ref[0, g * per_tile + t] for t in range(per_tile)], axis=1)
        o_ref[:, g * lanes : (g + 1) * lanes] = jnp.dot(wide, stacked, preferred_element_type=f32)


def intra_block(weights, x):
    nb, heads, group, _ = weights.shape
    length, inner = x.shape
    return pl.pallas_call(
        intra_kernel,
        out_shape=jax.ShapeDtypeStruct((length, inner), f32),
        grid=(nb,),
        in_specs=[
            pl.BlockSpec((1, heads, group, group), lambda k: (k, 0, 0, 0)),
            pl.BlockSpec((group, inner), lambda k: (k, 0)),
        ],
        out_specs=pl.BlockSpec((group, inner), lambda k: (k, 0)),
    )(weights, x)


def head_spread(values, inner):
    heads = values.shape[-1]
    owner = lax.broadcasted_iota(jnp.int32, (heads, inner), 1) // HEAD_DIM
    spread = (owner == lax.broadcasted_iota(jnp.int32, (heads, inner), 0)).astype(f32)
    return jnp.dot(values, spread, precision=exact_dot)


def local_ssd(x, dt, b_mat, c_mat, rates, backward):
    length, inner = x.shape
    heads = dt.shape[1]
    nb = length // GROUP
    xb = x.reshape(nb, GROUP, heads, HEAD_DIM)
    dtb = dt.reshape(nb, GROUP, heads)
    bb = b_mat.reshape(nb, GROUP, -1)
    cb = c_mat.reshape(nb, GROUP, -1)
    step = -dtb * rates[None, None, :]
    cum = lax.cumsum(step, axis=1, reverse=backward)
    last = cum[:, 0, :] if backward else cum[:, -1, :]
    scores = jnp.einsum("kin,kjn->kij", cb, bb, preferred_element_type=f32)
    rows = lax.broadcasted_iota(jnp.int32, (GROUP, GROUP), 0)
    cols = lax.broadcasted_iota(jnp.int32, (GROUP, GROUP), 1)
    mask = (rows <= cols) if backward else (rows >= cols)
    mask = mask[None, None]
    cum_t = cum.transpose(0, 2, 1)
    gap = jnp.where(mask, cum_t[:, :, :, None] - cum_t[:, :, None, :], 0.0)
    dt_t = dtb.transpose(0, 2, 1)
    weights = jnp.where(mask, scores[:, None] * jnp.exp(gap) * dt_t[:, :, None, :], 0.0).astype(bf16)
    intra = intra_block(weights, x)
    tail = jnp.exp(last[:, None, :] - cum) * dtb
    tail_wide = head_spread(tail.reshape(length, heads), inner).reshape(nb, GROUP, inner)
    scaled = x.reshape(nb, GROUP, inner).astype(f32) * tail_wide
    block_state = jnp.einsum("kjn,kjc->knc", bb.astype(f32), scaled, precision=exact_dot)
    block_decay = head_spread(jnp.exp(last), inner)
    cum_wide = head_spread(jnp.exp(cum).reshape(length, heads), inner)
    return dict(
        cb=cb,
        cum_wide=cum_wide,
        intra=intra,
        block_state=block_state,
        block_decay=block_decay,
    )


def stretch_states(parts, backward):
    block_state, block_decay = parts["block_state"], parts["block_decay"]
    nb = block_state.shape[0]
    order = list(range(nb - 1, -1, -1)) if backward else list(range(nb))
    starts = [None] * nb
    prefix = [None] * nb
    run_state = jnp.zeros_like(block_state[0])
    run_decay = jnp.ones_like(block_decay[0])
    for k in order:
        starts[k] = run_state
        prefix[k] = run_decay
        run_state = block_decay[k][None, :] * run_state + block_state[k]
        run_decay = run_decay * block_decay[k]
    return jnp.stack(starts), jnp.stack(prefix), run_state, run_decay


def pair_combine(earlier, later):
    (a0, s0), (a1, s1) = earlier, later
    return a1 * a0, a1[None, :] * s0 + s1


def scan_over(axis, own_decay, own_state, backward):
    peers = lax.axis_size(axis)
    step = -1 if backward else 1
    own = (own_decay, own_state)
    holder_parity = 0 if backward else 1
    first = shifted((own_decay, own_state.astype(bf16)), axis, step, 1 - holder_parity)
    first = (first[0], first[1].astype(f32))
    me = lax.axis_index(axis)
    holder = (me % 2 == 0) if backward else (me % 2 == 1)
    total = pair_combine(first, own)
    ex_decay = jnp.ones_like(own_decay)
    ex_state = jnp.zeros_like(own_state)
    in_decay, in_state = total
    distance = 2
    while distance < peers:
        got_decay, got_state = shifted(
            (in_decay, in_state.astype(bf16)), axis, step * distance, holder_parity
        )
        got_state = got_state.astype(f32)
        ex_state = ex_decay[None, :] * got_state + ex_state
        ex_decay = ex_decay * got_decay
        if distance * 2 < peers:
            in_state = in_decay[None, :] * got_state + in_state
            in_decay = in_decay * got_decay
        distance *= 2
    handed = shifted(ex_state.astype(bf16), axis, -step, holder_parity).astype(f32)
    mine = first[0][None, :] * ex_state + first[1]
    return jnp.where(holder, mine, handed)


def strand_output(parts, starts, prefix, carry, x, d_wide):
    start_states = starts + prefix[:, None, :] * carry[None]
    carried = jnp.einsum(
        "kin,knc->kic", parts["cb"].astype(f32), start_states, precision=exact_dot
    )
    length, inner = x.shape
    carried = carried.reshape(length, inner)
    return parts["intra"] + parts["cum_wide"] * carried + d_wide[None, :] * x.astype(f32)


def per_device(
    hidden,
    base_ids,
    embed,
    w_x,
    w_z,
    w_bc,
    w_dt,
    dt_bias,
    decay_rate,
    conv_x,
    conv_bc,
    d_skip,
    norm_gain,
    w_out,
):
    inner = w_x.shape[1]
    state = w_bc.shape[1] // 2
    conv = conv_x.shape[0]
    onehot = (base_ids[:, None] == jnp.arange(embed.shape[0], dtype=jnp.int32)[None, :]).astype(bf16)
    mixed_in = (hidden.astype(f32) + jnp.dot(onehot, embed, preferred_element_type=f32)).astype(bf16)
    rim = 8
    peers = lax.axis_size("ch")
    both_axes = ("ctx", "ch")
    count = lax.axis_size(both_axes)
    before, after = [], []
    for h in range(peers):
        ahead = [(q, q + h + 1) for q in range(count) if q % peers == peers - 1 and q + h + 1 < count]
        behind = [(q, q - peers + h) for q in range(count) if q % peers == 0 and q - peers + h >= 0]
        before.append(lax.ppermute(mixed_in[-rim:], both_axes, ahead))
        after.append(lax.ppermute(mixed_in[:rim], both_axes, behind))
    me = lax.axis_index("ch")
    u = gather_rows(mixed_in, "ch")
    u_ext = jnp.concatenate(
        [
            jnp.stack(before)[me],
            u,
            jnp.stack(after)[me],
        ],
        axis=0,
    )
    length, width = u.shape
    flip = flip_matrix(width)
    u_ext_flip = jnp.dot(u_ext, flip, preferred_element_type=f32).astype(bf16)
    both_ext = jnp.concatenate([u_ext, u_ext_flip], axis=0)
    both = jnp.concatenate([u_ext[rim : rim + length], u_ext_flip[rim : rim + length]], axis=0)
    x_raw = jnp.dot(both_ext, w_x, preferred_element_type=f32).astype(bf16)
    bc_raw = jnp.dot(both_ext, w_bc, preferred_element_type=f32).astype(bf16)
    z_all = jnp.dot(both, w_z, preferred_element_type=f32).astype(bf16)
    dt_all = jax.nn.softplus(jnp.dot(both, w_dt, preferred_element_type=f32) + dt_bias[None, :])
    ext = length + 2 * rim
    d_wide = head_spread(d_skip[None, :], inner)[0]

    outs = []
    sums = []
    for backward in (False, True):
        rows = slice(length, 2 * length) if backward else slice(0, length)
        ext_rows = slice(ext, 2 * ext) if backward else slice(0, ext)
        x_c = conv_silu(x_raw[ext_rows], conv_x, rim, length, backward)
        bc_c = conv_silu(bc_raw[ext_rows], conv_bc, rim, length, backward)
        parts = local_ssd(x_c, dt_all[rows], bc_c[:, :state], bc_c[:, state:], decay_rate, backward)
        starts, prefix, end_state, end_decay = stretch_states(parts, backward)
        carry = scan_over("ctx", end_decay, end_state, backward)
        y = strand_output(parts, starts, prefix, carry, x_c, d_wide)
        gated = (y * jax.nn.silu(z_all[rows].astype(f32))).astype(bf16).astype(f32)
        outs.append(gated)
        sums.append(jnp.sum(gated * gated, axis=1))
    total = lax.psum(jnp.stack(sums), "ch")
    full_inner = inner * lax.axis_size("ch")
    gain = norm_gain.astype(f32)[None, :]
    normed = [
        (g * lax.rsqrt(t / full_inner + norm_eps)[:, None] * gain).astype(bf16)
        for g, t in zip(outs, total)
    ]
    own_rows = length // peers

    def partial_for(normed_pair, target):
        nf = lax.dynamic_slice_in_dim(normed_pair[0], target * own_rows, own_rows, axis=0)
        nb_ = lax.dynamic_slice_in_dim(normed_pair[1], target * own_rows, own_rows, axis=0)
        out_f = jnp.dot(nf, w_out, preferred_element_type=f32)
        out_b = jnp.dot(nb_, w_out, preferred_element_type=f32)
        return out_f + flipped_columns(out_b, flip)

    received = []
    sent_all = []
    for d in range(1, peers):
        sent = partial_for(normed, (me + d) % peers).astype(bf16)
        sent_all.append(sent)
        route = [(i, (i + d) % peers) for i in range(peers)]
        received.append(lax.ppermute(sent, "ch", route))
    _, normed_later = lax.optimization_barrier((sent_all, normed))
    summed = partial_for(normed_later, me)
    for r in received:
        summed = summed + r.astype(f32)
    return summed.astype(bf16)


def solution(mesh):
    placed = (
        P(("ctx", "ch"), None),
        P(("ctx", "ch")),
        P(),
        P(None, "ch"),
        P(None, "ch"),
        P(),
        P(None, "ch"),
        P("ch"),
        P("ch"),
        P(None, "ch"),
        P(),
        P("ch"),
        P("ch"),
        P("ch", None),
    )
    return jax.shard_map(
        per_device, mesh=mesh, in_specs=placed, out_specs=P(("ctx", "ch"), None), check_vma=False
    )
```

```python
import jax
import jax.numpy as jnp
from jax import lax
from jax.experimental import pallas as pl
from jax.sharding import PartitionSpec as P

HEAD_DIM = 64
GROUP = 128

exact_dot = lax.Precision.HIGHEST
norm_eps = 1e-05
f32 = jnp.float32
bf16 = jnp.bfloat16


def flip_matrix(n):
    rows = lax.broadcasted_iota(jnp.int32, (n, n), 0)
    cols = lax.broadcasted_iota(jnp.int32, (n, n), 1)
    return (rows + cols == n - 1).astype(bf16)


def shifted(block, axis, distance, parity=None):
    devices = range(lax.axis_size(axis))
    route = [
        (i, i + distance)
        for i in devices
        if i + distance in devices and (parity is None or i % 2 == parity)
    ]
    return lax.ppermute(block, axis, route)


def gather_rows(block, axis):
    peers, me = lax.axis_size(axis), lax.axis_index(axis)
    got = [block] + [
        lax.ppermute(block, axis, [(i, (i + d) % peers) for i in range(peers)])
        for d in range(peers - 1, 0, -1)
    ]
    stacked = jnp.stack(got)
    rolled = jnp.roll(stacked, me, axis=0)
    return rolled.reshape(peers * block.shape[0], *block.shape[1:])


def bf16_part(values):
    return lax.reduce_precision(values, exponent_bits=8, mantissa_bits=7)


def flipped_columns(part, flip):
    hi = bf16_part(part)
    lo = part - hi
    rows = part.shape[0]
    split = jnp.concatenate([hi, lo], axis=0).astype(bf16)
    pieces = jnp.dot(split, flip, preferred_element_type=f32)
    return pieces[:rows] + pieces[rows:]


def conv_silu(raw_ext, taps, rim, length, backward):
    conv = taps.shape[0]
    summed = None
    for k in range(conv):
        first = rim + conv - 1 - k if backward else rim - (conv - 1) + k
        term = taps[k][None, :] * raw_ext[first : first + length].astype(f32)
        summed = term if summed is None else summed + term
    return jax.nn.silu(summed).astype(bf16)


def intra_kernel(w_ref, x_ref, o_ref):
    lanes = 128
    per_tile = lanes // HEAD_DIM
    rows = x_ref.shape[0]
    owner = lax.broadcasted_iota(jnp.int32, (rows, lanes), 1) // HEAD_DIM
    for g in range(x_ref.shape[1] // lanes):
        tile = x_ref[:, g * lanes : (g + 1) * lanes]
        zero = jnp.zeros_like(tile)
        stacked = jnp.concatenate([jnp.where(owner == t, tile, zero) for t in range(per_tile)], axis=0)
        wide = jnp.concatenate([w_ref[0, g * per_tile + t] for t in range(per_tile)], axis=1)
        o_ref[:, g * lanes : (g + 1) * lanes] = jnp.dot(wide, stacked, preferred_element_type=f32)


def intra_block(weights, x):
    nb, heads, group, _ = weights.shape
    length, inner = x.shape
    return pl.pallas_call(
        intra_kernel,
        out_shape=jax.ShapeDtypeStruct((length, inner), f32),
        grid=(nb,),
        in_specs=[
            pl.BlockSpec((1, heads, group, group), lambda k: (k, 0, 0, 0)),
            pl.BlockSpec((group, inner), lambda k: (k, 0)),
        ],
        out_specs=pl.BlockSpec((group, inner), lambda k: (k, 0)),
    )(weights, x)


def head_spread(values, inner):
    heads = values.shape[-1]
    owner = lax.broadcasted_iota(jnp.int32, (heads, inner), 1) // HEAD_DIM
    spread = (owner == lax.broadcasted_iota(jnp.int32, (heads, inner), 0)).astype(f32)
    return jnp.dot(values, spread, precision=exact_dot)


def local_ssd(x, dt, b_mat, c_mat, rates, backward):
    length, inner = x.shape
    heads = dt.shape[1]
    nb = length // GROUP
    xb = x.reshape(nb, GROUP, heads, HEAD_DIM)
    dtb = dt.reshape(nb, GROUP, heads)
    bb = b_mat.reshape(nb, GROUP, -1)
    cb = c_mat.reshape(nb, GROUP, -1)
    step = -dtb * rates[None, None, :]
    cum = lax.cumsum(step, axis=1, reverse=backward)
    last = cum[:, 0, :] if backward else cum[:, -1, :]
    scores = jnp.einsum("kin,kjn->kij", cb, bb, preferred_element_type=f32)
    rows = lax.broadcasted_iota(jnp.int32, (GROUP, GROUP), 0)
    cols = lax.broadcasted_iota(jnp.int32, (GROUP, GROUP), 1)
    mask = (rows <= cols) if backward else (rows >= cols)
    mask = mask[None, None]
    cum_t = cum.transpose(0, 2, 1)
    gap = jnp.where(mask, cum_t[:, :, :, None] - cum_t[:, :, None, :], 0.0)
    dt_t = dtb.transpose(0, 2, 1)
    weights = jnp.where(mask, scores[:, None] * jnp.exp(gap) * dt_t[:, :, None, :], 0.0).astype(bf16)
    intra = intra_block(weights, x)
    tail = jnp.exp(last[:, None, :] - cum) * dtb
    tail_wide = head_spread(tail.reshape(length, heads), inner).reshape(nb, GROUP, inner)
    scaled = x.reshape(nb, GROUP, inner).astype(f32) * tail_wide
    block_state = jnp.einsum("kjn,kjc->knc", bb.astype(f32), scaled, precision=lax.Precision.HIGH)
    block_decay = head_spread(jnp.exp(last), inner)
    cum_wide = head_spread(jnp.exp(cum).reshape(length, heads), inner)
    return dict(
        cb=cb,
        cum_wide=cum_wide,
        intra=intra,
        block_state=block_state,
        block_decay=block_decay,
    )


def stretch_states(parts, backward):
    block_state, block_decay = parts["block_state"], parts["block_decay"]
    nb = block_state.shape[0]
    order = list(range(nb - 1, -1, -1)) if backward else list(range(nb))
    starts = [None] * nb
    prefix = [None] * nb
    run_state = jnp.zeros_like(block_state[0])
    run_decay = jnp.ones_like(block_decay[0])
    for k in order:
        starts[k] = run_state
        prefix[k] = run_decay
        run_state = block_decay[k][None, :] * run_state + block_state[k]
        run_decay = run_decay * block_decay[k]
    return jnp.stack(starts), jnp.stack(prefix), run_state, run_decay


def pair_combine(earlier, later):
    (a0, s0), (a1, s1) = earlier, later
    return a1 * a0, a1[None, :] * s0 + s1


def scan_over(axis, own_decay, own_state, backward):
    peers = lax.axis_size(axis)
    step = -1 if backward else 1
    own = (own_decay, own_state)
    holder_parity = 0 if backward else 1
    first = shifted((own_decay, own_state.astype(bf16)), axis, step, 1 - holder_parity)
    first = (first[0], first[1].astype(f32))
    me = lax.axis_index(axis)
    holder = (me % 2 == 0) if backward else (me % 2 == 1)
    total = pair_combine(first, own)
    ex_decay = jnp.ones_like(own_decay)
    ex_state = jnp.zeros_like(own_state)
    in_decay, in_state = total
    distance = 2
    while distance < peers:
        got_decay, got_state = shifted(
            (in_decay, in_state.astype(bf16)), axis, step * distance, holder_parity
        )
        got_state = got_state.astype(f32)
        ex_state = ex_decay[None, :] * got_state + ex_state
        ex_decay = ex_decay * got_decay
        if distance * 2 < peers:
            in_state = in_decay[None, :] * got_state + in_state
            in_decay = in_decay * got_decay
        distance *= 2
    handed = shifted(ex_state.astype(bf16), axis, -step, holder_parity).astype(f32)
    mine = first[0][None, :] * ex_state + first[1]
    return jnp.where(holder, mine, handed)


def strand_output(parts, starts, prefix, carry, x, d_wide):
    start_states = starts + prefix[:, None, :] * carry[None]
    carried = jnp.einsum(
        "kin,knc->kic", parts["cb"].astype(f32), start_states, precision=lax.Precision.HIGH
    )
    length, inner = x.shape
    carried = carried.reshape(length, inner)
    return parts["intra"] + parts["cum_wide"] * carried + d_wide[None, :] * x.astype(f32)


def per_device(
    hidden,
    base_ids,
    embed,
    w_x,
    w_z,
    w_bc,
    w_dt,
    dt_bias,
    decay_rate,
    conv_x,
    conv_bc,
    d_skip,
    norm_gain,
    w_out,
):
    inner = w_x.shape[1]
    state = w_bc.shape[1] // 2
    conv = conv_x.shape[0]
    onehot = (base_ids[:, None] == jnp.arange(embed.shape[0], dtype=jnp.int32)[None, :]).astype(bf16)
    mixed_in = (hidden.astype(f32) + jnp.dot(onehot, embed, preferred_element_type=f32)).astype(bf16)
    rim = 8
    peers = lax.axis_size("ch")
    both_axes = ("ctx", "ch")
    count = lax.axis_size(both_axes)
    before, after = [], []
    for h in range(peers):
        ahead = [(q, q + h + 1) for q in range(count) if q % peers == peers - 1 and q + h + 1 < count]
        behind = [(q, q - peers + h) for q in range(count) if q % peers == 0 and q - peers + h >= 0]
        before.append(lax.ppermute(mixed_in[-rim:], both_axes, ahead))
        after.append(lax.ppermute(mixed_in[:rim], both_axes, behind))
    me = lax.axis_index("ch")
    u = gather_rows(mixed_in, "ch")
    u_ext = jnp.concatenate(
        [
            jnp.stack(before)[me],
            u,
            jnp.stack(after)[me],
        ],
        axis=0,
    )
    length, width = u.shape
    flip = flip_matrix(width)
    u_ext_flip = jnp.dot(u_ext, flip, preferred_element_type=f32).astype(bf16)
    both_ext = jnp.concatenate([u_ext, u_ext_flip], axis=0)
    both = jnp.concatenate([u_ext[rim : rim + length], u_ext_flip[rim : rim + length]], axis=0)
    x_raw = jnp.dot(both_ext, w_x, preferred_element_type=f32).astype(bf16)
    bc_raw = jnp.dot(both_ext, w_bc, preferred_element_type=f32).astype(bf16)
    z_all = jnp.dot(both, w_z, preferred_element_type=f32).astype(bf16)
    dt_all = jax.nn.softplus(jnp.dot(both, w_dt, preferred_element_type=f32) + dt_bias[None, :])
    ext = length + 2 * rim
    d_wide = head_spread(d_skip[None, :], inner)[0]

    outs = []
    sums = []
    for backward in (False, True):
        rows = slice(length, 2 * length) if backward else slice(0, length)
        ext_rows = slice(ext, 2 * ext) if backward else slice(0, ext)
        x_c = conv_silu(x_raw[ext_rows], conv_x, rim, length, backward)
        bc_c = conv_silu(bc_raw[ext_rows], conv_bc, rim, length, backward)
        parts = local_ssd(x_c, dt_all[rows], bc_c[:, :state], bc_c[:, state:], decay_rate, backward)
        starts, prefix, end_state, end_decay = stretch_states(parts, backward)
        carry = scan_over("ctx", end_decay, end_state, backward)
        y = strand_output(parts, starts, prefix, carry, x_c, d_wide)
        gated = (y * jax.nn.silu(z_all[rows].astype(f32))).astype(bf16).astype(f32)
        outs.append(gated)
        sums.append(jnp.sum(gated * gated, axis=1))
    total = lax.psum(jnp.stack(sums), "ch")
    full_inner = inner * lax.axis_size("ch")
    gain = norm_gain.astype(f32)[None, :]
    normed = [
        (g * lax.rsqrt(t / full_inner + norm_eps)[:, None] * gain).astype(bf16)
        for g, t in zip(outs, total)
    ]
    own_rows = length // peers

    def partial_for(normed_pair, target):
        nf = lax.dynamic_slice_in_dim(normed_pair[0], target * own_rows, own_rows, axis=0)
        nb_ = lax.dynamic_slice_in_dim(normed_pair[1], target * own_rows, own_rows, axis=0)
        out_f = jnp.dot(nf, w_out, preferred_element_type=f32)
        out_b = jnp.dot(nb_, w_out, preferred_element_type=f32)
        return out_f + flipped_columns(out_b, flip)

    received = []
    sent_all = []
    for d in range(1, peers):
        sent = partial_for(normed, (me + d) % peers).astype(bf16)
        sent_all.append(sent)
        route = [(i, (i + d) % peers) for i in range(peers)]
        received.append(lax.ppermute(sent, "ch", route))
    _, normed_later = lax.optimization_barrier((sent_all, normed))
    summed = partial_for(normed_later, me)
    for r in received:
        summed = summed + r.astype(f32)
    return summed.astype(bf16)


def solution(mesh):
    placed = (
        P(("ctx", "ch"), None),
        P(("ctx", "ch")),
        P(),
        P(None, "ch"),
        P(None, "ch"),
        P(),
        P(None, "ch"),
        P("ch"),
        P("ch"),
        P(None, "ch"),
        P(),
        P("ch"),
        P("ch"),
        P("ch", None),
    )
    return jax.shard_map(
        per_device, mesh=mesh, in_specs=placed, out_specs=P(("ctx", "ch"), None), check_vma=False
    )
```

```python
import jax
import jax.numpy as jnp
from jax import lax
from jax.experimental import pallas as pl
from jax.sharding import PartitionSpec as P

HEAD_DIM = 64
GROUP = 128

exact_dot = lax.Precision.HIGHEST
norm_eps = 1e-05
f32 = jnp.float32
bf16 = jnp.bfloat16


def flip_matrix(n):
    rows = lax.broadcasted_iota(jnp.int32, (n, n), 0)
    cols = lax.broadcasted_iota(jnp.int32, (n, n), 1)
    return (rows + cols == n - 1).astype(bf16)


def shifted(block, axis, distance, parity=None):
    devices = range(lax.axis_size(axis))
    route = [
        (i, i + distance)
        for i in devices
        if i + distance in devices and (parity is None or i % 2 == parity)
    ]
    return lax.ppermute(block, axis, route)


def gather_rows(block, axis):
    peers, me = lax.axis_size(axis), lax.axis_index(axis)
    got = [block] + [
        lax.ppermute(block, axis, [(i, (i + d) % peers) for i in range(peers)])
        for d in range(peers - 1, 0, -1)
    ]
    stacked = jnp.stack(got)
    rolled = jnp.roll(stacked, me, axis=0)
    return rolled.reshape(peers * block.shape[0], *block.shape[1:])


def bf16_part(values):
    return lax.reduce_precision(values, exponent_bits=8, mantissa_bits=7)


def flipped_columns(part, flip):
    hi = bf16_part(part)
    lo = part - hi
    rows = part.shape[0]
    split = jnp.concatenate([hi, lo], axis=0).astype(bf16)
    pieces = jnp.dot(split, flip, preferred_element_type=f32)
    return pieces[:rows] + pieces[rows:]


def conv_silu(raw_ext, taps, rim, length, backward):
    conv = taps.shape[0]
    summed = None
    for k in range(conv):
        first = rim + conv - 1 - k if backward else rim - (conv - 1) + k
        term = taps[k][None, :] * raw_ext[first : first + length].astype(f32)
        summed = term if summed is None else summed + term
    return jax.nn.silu(summed).astype(bf16)


def intra_kernel(w_ref, x_ref, o_ref):
    lanes = 128
    per_tile = lanes // HEAD_DIM
    rows = x_ref.shape[0]
    owner = lax.broadcasted_iota(jnp.int32, (rows, lanes), 1) // HEAD_DIM
    for g in range(x_ref.shape[1] // lanes):
        tile = x_ref[:, g * lanes : (g + 1) * lanes]
        zero = jnp.zeros_like(tile)
        stacked = jnp.concatenate([jnp.where(owner == t, tile, zero) for t in range(per_tile)], axis=0)
        wide = jnp.concatenate([w_ref[0, g * per_tile + t] for t in range(per_tile)], axis=1)
        o_ref[:, g * lanes : (g + 1) * lanes] = jnp.dot(wide, stacked, preferred_element_type=f32)


def intra_block(weights, x):
    nb, heads, group, _ = weights.shape
    length, inner = x.shape
    return pl.pallas_call(
        intra_kernel,
        out_shape=jax.ShapeDtypeStruct((length, inner), f32),
        grid=(nb,),
        in_specs=[
            pl.BlockSpec((1, heads, group, group), lambda k: (k, 0, 0, 0)),
            pl.BlockSpec((group, inner), lambda k: (k, 0)),
        ],
        out_specs=pl.BlockSpec((group, inner), lambda k: (k, 0)),
    )(weights, x)


def head_spread(values, inner):
    heads = values.shape[-1]
    owner = lax.broadcasted_iota(jnp.int32, (heads, inner), 1) // HEAD_DIM
    spread = (owner == lax.broadcasted_iota(jnp.int32, (heads, inner), 0)).astype(f32)
    return jnp.dot(values, spread, precision=lax.Precision.HIGH)


def local_ssd(x, dt, b_mat, c_mat, rates, backward):
    length, inner = x.shape
    heads = dt.shape[1]
    nb = length // GROUP
    xb = x.reshape(nb, GROUP, heads, HEAD_DIM)
    dtb = dt.reshape(nb, GROUP, heads)
    bb = b_mat.reshape(nb, GROUP, -1)
    cb = c_mat.reshape(nb, GROUP, -1)
    step = -dtb * rates[None, None, :]
    cum = lax.cumsum(step, axis=1, reverse=backward)
    last = cum[:, 0, :] if backward else cum[:, -1, :]
    scores = jnp.einsum("kin,kjn->kij", cb, bb, preferred_element_type=f32)
    rows = lax.broadcasted_iota(jnp.int32, (GROUP, GROUP), 0)
    cols = lax.broadcasted_iota(jnp.int32, (GROUP, GROUP), 1)
    mask = (rows <= cols) if backward else (rows >= cols)
    mask = mask[None, None]
    cum_t = cum.transpose(0, 2, 1)
    gap = jnp.where(mask, cum_t[:, :, :, None] - cum_t[:, :, None, :], 0.0)
    dt_t = dtb.transpose(0, 2, 1)
    weights = jnp.where(mask, scores[:, None] * jnp.exp(gap) * dt_t[:, :, None, :], 0.0).astype(bf16)
    intra = intra_block(weights, x)
    tail = jnp.exp(last[:, None, :] - cum) * dtb
    tail_wide = head_spread(tail.reshape(length, heads), inner).reshape(nb, GROUP, inner)
    scaled = x.reshape(nb, GROUP, inner).astype(f32) * tail_wide
    block_state = jnp.einsum("kjn,kjc->knc", bb.astype(f32), scaled, precision=lax.Precision.HIGH)
    block_decay = head_spread(jnp.exp(last), inner)
    cum_wide = head_spread(jnp.exp(cum).reshape(length, heads), inner)
    return dict(
        cb=cb,
        cum_wide=cum_wide,
        intra=intra,
        block_state=block_state,
        block_decay=block_decay,
    )


def stretch_states(parts, backward):
    block_state, block_decay = parts["block_state"], parts["block_decay"]
    nb = block_state.shape[0]
    order = list(range(nb - 1, -1, -1)) if backward else list(range(nb))
    starts = [None] * nb
    prefix = [None] * nb
    run_state = jnp.zeros_like(block_state[0])
    run_decay = jnp.ones_like(block_decay[0])
    for k in order:
        starts[k] = run_state
        prefix[k] = run_decay
        run_state = block_decay[k][None, :] * run_state + block_state[k]
        run_decay = run_decay * block_decay[k]
    return jnp.stack(starts), jnp.stack(prefix), run_state, run_decay


def pair_combine(earlier, later):
    (a0, s0), (a1, s1) = earlier, later
    return a1 * a0, a1[None, :] * s0 + s1


def scan_over(axis, own_decay, own_state, backward):
    peers = lax.axis_size(axis)
    step = -1 if backward else 1
    own = (own_decay, own_state)
    holder_parity = 0 if backward else 1
    first = shifted((own_decay, own_state.astype(bf16)), axis, step, 1 - holder_parity)
    first = (first[0], first[1].astype(f32))
    me = lax.axis_index(axis)
    holder = (me % 2 == 0) if backward else (me % 2 == 1)
    total = pair_combine(first, own)
    ex_decay = jnp.ones_like(own_decay)
    ex_state = jnp.zeros_like(own_state)
    in_decay, in_state = total
    distance = 2
    while distance < peers:
        got_decay, got_state = shifted(
            (in_decay, in_state.astype(bf16)), axis, step * distance, holder_parity
        )
        got_state = got_state.astype(f32)
        ex_state = ex_decay[None, :] * got_state + ex_state
        ex_decay = ex_decay * got_decay
        if distance * 2 < peers:
            in_state = in_decay[None, :] * got_state + in_state
            in_decay = in_decay * got_decay
        distance *= 2
    handed = shifted(ex_state.astype(bf16), axis, -step, holder_parity).astype(f32)
    mine = first[0][None, :] * ex_state + first[1]
    return jnp.where(holder, mine, handed)


def strand_output(parts, starts, prefix, carry, x, d_wide):
    start_states = starts + prefix[:, None, :] * carry[None]
    carried = jnp.einsum(
        "kin,knc->kic", parts["cb"].astype(f32), start_states, precision=lax.Precision.HIGH
    )
    length, inner = x.shape
    carried = carried.reshape(length, inner)
    return parts["intra"] + parts["cum_wide"] * carried + d_wide[None, :] * x.astype(f32)


def per_device(
    hidden,
    base_ids,
    embed,
    w_x,
    w_z,
    w_bc,
    w_dt,
    dt_bias,
    decay_rate,
    conv_x,
    conv_bc,
    d_skip,
    norm_gain,
    w_out,
):
    inner = w_x.shape[1]
    state = w_bc.shape[1] // 2
    conv = conv_x.shape[0]
    onehot = (base_ids[:, None] == jnp.arange(embed.shape[0], dtype=jnp.int32)[None, :]).astype(bf16)
    mixed_in = (hidden.astype(f32) + jnp.dot(onehot, embed, preferred_element_type=f32)).astype(bf16)
    rim = 8
    peers = lax.axis_size("ch")
    both_axes = ("ctx", "ch")
    count = lax.axis_size(both_axes)
    before, after = [], []
    for h in range(peers):
        ahead = [(q, q + h + 1) for q in range(count) if q % peers == peers - 1 and q + h + 1 < count]
        behind = [(q, q - peers + h) for q in range(count) if q % peers == 0 and q - peers + h >= 0]
        before.append(lax.ppermute(mixed_in[-rim:], both_axes, ahead))
        after.append(lax.ppermute(mixed_in[:rim], both_axes, behind))
    me = lax.axis_index("ch")
    u = gather_rows(mixed_in, "ch")
    u_ext = jnp.concatenate(
        [
            jnp.stack(before)[me],
            u,
            jnp.stack(after)[me],
        ],
        axis=0,
    )
    length, width = u.shape
    flip = flip_matrix(width)
    u_ext_flip = jnp.dot(u_ext, flip, preferred_element_type=f32).astype(bf16)
    both_ext = jnp.concatenate([u_ext, u_ext_flip], axis=0)
    both = jnp.concatenate([u_ext[rim : rim + length], u_ext_flip[rim : rim + length]], axis=0)
    x_raw = jnp.dot(both_ext, w_x, preferred_element_type=f32).astype(bf16)
    bc_raw = jnp.dot(both_ext, w_bc, preferred_element_type=f32).astype(bf16)
    z_all = jnp.dot(both, w_z, preferred_element_type=f32).astype(bf16)
    dt_all = jax.nn.softplus(jnp.dot(both, w_dt, preferred_element_type=f32) + dt_bias[None, :])
    ext = length + 2 * rim
    d_wide = head_spread(d_skip[None, :], inner)[0]

    outs = []
    sums = []
    for backward in (False, True):
        rows = slice(length, 2 * length) if backward else slice(0, length)
        ext_rows = slice(ext, 2 * ext) if backward else slice(0, ext)
        x_c = conv_silu(x_raw[ext_rows], conv_x, rim, length, backward)
        bc_c = conv_silu(bc_raw[ext_rows], conv_bc, rim, length, backward)
        parts = local_ssd(x_c, dt_all[rows], bc_c[:, :state], bc_c[:, state:], decay_rate, backward)
        starts, prefix, end_state, end_decay = stretch_states(parts, backward)
        carry = scan_over("ctx", end_decay, end_state, backward)
        y = strand_output(parts, starts, prefix, carry, x_c, d_wide)
        gated = (y * jax.nn.silu(z_all[rows].astype(f32))).astype(bf16).astype(f32)
        outs.append(gated)
        sums.append(jnp.sum(gated * gated, axis=1))
    total = lax.psum(jnp.stack(sums), "ch")
    full_inner = inner * lax.axis_size("ch")
    gain = norm_gain.astype(f32)[None, :]
    normed = [
        (g * lax.rsqrt(t / full_inner + norm_eps)[:, None] * gain).astype(bf16)
        for g, t in zip(outs, total)
    ]
    own_rows = length // peers

    def partial_for(normed_pair, target):
        nf = lax.dynamic_slice_in_dim(normed_pair[0], target * own_rows, own_rows, axis=0)
        nb_ = lax.dynamic_slice_in_dim(normed_pair[1], target * own_rows, own_rows, axis=0)
        out_f = jnp.dot(nf, w_out, preferred_element_type=f32)
        out_b = jnp.dot(nb_, w_out, preferred_element_type=f32)
        return out_f + flipped_columns(out_b, flip)

    received = []
    sent_all = []
    for d in range(1, peers):
        sent = partial_for(normed, (me + d) % peers).astype(bf16)
        sent_all.append(sent)
        route = [(i, (i + d) % peers) for i in range(peers)]
        received.append(lax.ppermute(sent, "ch", route))
    _, normed_later = lax.optimization_barrier((sent_all, normed))
    summed = partial_for(normed_later, me)
    for r in received:
        summed = summed + r.astype(f32)
    return summed.astype(bf16)


def solution(mesh):
    placed = (
        P(("ctx", "ch"), None),
        P(("ctx", "ch")),
        P(),
        P(None, "ch"),
        P(None, "ch"),
        P(),
        P(None, "ch"),
        P("ch"),
        P("ch"),
        P(None, "ch"),
        P(),
        P("ch"),
        P("ch"),
        P("ch", None),
    )
    return jax.shard_map(
        per_device, mesh=mesh, in_specs=placed, out_specs=P(("ctx", "ch"), None), check_vma=False
    )
```

```python
import jax
import jax.numpy as jnp
from jax import lax
from jax.experimental import pallas as pl
from jax.sharding import PartitionSpec as P

HEAD_DIM = 64
GROUP = 128

exact_dot = lax.Precision.HIGHEST
norm_eps = 1e-05
f32 = jnp.float32
bf16 = jnp.bfloat16


def flip_matrix(n):
    rows = lax.broadcasted_iota(jnp.int32, (n, n), 0)
    cols = lax.broadcasted_iota(jnp.int32, (n, n), 1)
    return (rows + cols == n - 1).astype(bf16)


def shifted(block, axis, distance, parity=None):
    devices = range(lax.axis_size(axis))
    route = [
        (i, i + distance)
        for i in devices
        if i + distance in devices and (parity is None or i % 2 == parity)
    ]
    return lax.ppermute(block, axis, route)


def gather_rows(block, axis):
    peers, me = lax.axis_size(axis), lax.axis_index(axis)
    got = [block] + [
        lax.ppermute(block, axis, [(i, (i + d) % peers) for i in range(peers)])
        for d in range(peers - 1, 0, -1)
    ]
    stacked = jnp.stack(got)
    rolled = jnp.roll(stacked, me, axis=0)
    return rolled.reshape(peers * block.shape[0], *block.shape[1:])


def bf16_part(values):
    return lax.reduce_precision(values, exponent_bits=8, mantissa_bits=7)


def flipped_columns(part, flip):
    hi = bf16_part(part)
    lo = part - hi
    rows = part.shape[0]
    split = jnp.concatenate([hi, lo], axis=0).astype(bf16)
    pieces = jnp.dot(split, flip, preferred_element_type=f32)
    return pieces[:rows] + pieces[rows:]


def conv_silu(raw_ext, taps, rim, length, backward):
    conv = taps.shape[0]
    summed = None
    for k in range(conv):
        first = rim + conv - 1 - k if backward else rim - (conv - 1) + k
        term = taps[k][None, :] * raw_ext[first : first + length].astype(f32)
        summed = term if summed is None else summed + term
    return jax.nn.silu(summed).astype(bf16)


def intra_kernel(w_ref, x_ref, o_ref):
    lanes = 128
    per_tile = lanes // HEAD_DIM
    rows = x_ref.shape[0]
    owner = lax.broadcasted_iota(jnp.int32, (rows, lanes), 1) // HEAD_DIM
    for g in range(x_ref.shape[1] // lanes):
        tile = x_ref[:, g * lanes : (g + 1) * lanes]
        zero = jnp.zeros_like(tile)
        stacked = jnp.concatenate([jnp.where(owner == t, tile, zero) for t in range(per_tile)], axis=0)
        wide = jnp.concatenate([w_ref[0, g * per_tile + t] for t in range(per_tile)], axis=1)
        o_ref[:, g * lanes : (g + 1) * lanes] = jnp.dot(wide, stacked, preferred_element_type=f32)


def intra_block(weights, x):
    nb, heads, group, _ = weights.shape
    length, inner = x.shape
    return pl.pallas_call(
        intra_kernel,
        out_shape=jax.ShapeDtypeStruct((length, inner), f32),
        grid=(nb,),
        in_specs=[
            pl.BlockSpec((1, heads, group, group), lambda k: (k, 0, 0, 0)),
            pl.BlockSpec((group, inner), lambda k: (k, 0)),
        ],
        out_specs=pl.BlockSpec((group, inner), lambda k: (k, 0)),
    )(weights, x)


def head_spread(values, inner):
    heads = values.shape[-1]
    owner = lax.broadcasted_iota(jnp.int32, (heads, inner), 1) // HEAD_DIM
    spread = (owner == lax.broadcasted_iota(jnp.int32, (heads, inner), 0)).astype(f32)
    return jnp.dot(values, spread, precision=lax.Precision.HIGH)


def local_ssd(x, dt, b_mat, c_mat, rates, backward):
    length, inner = x.shape
    heads = dt.shape[1]
    nb = length // GROUP
    xb = x.reshape(nb, GROUP, heads, HEAD_DIM)
    dtb = dt.reshape(nb, GROUP, heads)
    bb = b_mat.reshape(nb, GROUP, -1)
    cb = c_mat.reshape(nb, GROUP, -1)
    step = -dtb * rates[None, None, :]
    cum = lax.cumsum(step, axis=1, reverse=backward)
    last = cum[:, 0, :] if backward else cum[:, -1, :]
    scores = jnp.einsum("kin,kjn->kij", cb, bb, preferred_element_type=f32)
    rows = lax.broadcasted_iota(jnp.int32, (GROUP, GROUP), 0)
    cols = lax.broadcasted_iota(jnp.int32, (GROUP, GROUP), 1)
    mask = (rows <= cols) if backward else (rows >= cols)
    mask = mask[None, None]
    cum_t = cum.transpose(0, 2, 1)
    gap = jnp.where(mask, cum_t[:, :, :, None] - cum_t[:, :, None, :], 0.0)
    dt_t = dtb.transpose(0, 2, 1)
    weights = jnp.where(mask, scores[:, None] * jnp.exp(gap) * dt_t[:, :, None, :], 0.0).astype(bf16)
    intra = intra_block(weights, x)
    tail = jnp.exp(last[:, None, :] - cum) * dtb
    tail_wide = head_spread(tail.reshape(length, heads), inner).reshape(nb, GROUP, inner)
    scaled = x.reshape(nb, GROUP, inner).astype(f32) * tail_wide
    block_state = jnp.einsum("kjn,kjc->knc", bb.astype(f32), scaled, precision=lax.Precision.HIGH)
    block_decay = head_spread(jnp.exp(last), inner)
    cum_wide = head_spread(jnp.exp(cum).reshape(length, heads), inner)
    return dict(
        cb=cb,
        cum_wide=cum_wide,
        intra=intra,
        block_state=block_state,
        block_decay=block_decay,
    )


def stretch_states(parts, backward):
    block_state, block_decay = parts["block_state"], parts["block_decay"]
    nb = block_state.shape[0]
    order = list(range(nb - 1, -1, -1)) if backward else list(range(nb))
    starts = [None] * nb
    prefix = [None] * nb
    run_state = jnp.zeros_like(block_state[0])
    run_decay = jnp.ones_like(block_decay[0])
    for k in order:
        starts[k] = run_state
        prefix[k] = run_decay
        run_state = block_decay[k][None, :] * run_state + block_state[k]
        run_decay = run_decay * block_decay[k]
    return jnp.stack(starts), jnp.stack(prefix), run_state, run_decay


def pair_combine(earlier, later):
    (a0, s0), (a1, s1) = earlier, later
    return a1 * a0, a1[None, :] * s0 + s1


def scan_over(axis, own_decay, own_state, backward):
    peers = lax.axis_size(axis)
    step = -1 if backward else 1
    own = (own_decay, own_state)
    holder_parity = 0 if backward else 1
    first = shifted((own_decay, own_state.astype(bf16)), axis, step, 1 - holder_parity)
    first = (first[0], first[1].astype(f32))
    me = lax.axis_index(axis)
    holder = (me % 2 == 0) if backward else (me % 2 == 1)
    total = pair_combine(first, own)
    ex_decay = jnp.ones_like(own_decay)
    ex_state = jnp.zeros_like(own_state)
    in_decay, in_state = total
    distance = 2
    while distance < peers:
        got_decay, got_state = shifted(
            (in_decay, in_state.astype(bf16)), axis, step * distance, holder_parity
        )
        got_state = got_state.astype(f32)
        ex_state = ex_decay[None, :] * got_state + ex_state
        ex_decay = ex_decay * got_decay
        if distance * 2 < peers:
            in_state = in_decay[None, :] * got_state + in_state
            in_decay = in_decay * got_decay
        distance *= 2
    handed = shifted(ex_state.astype(bf16), axis, -step, holder_parity).astype(f32)
    mine = first[0][None, :] * ex_state + first[1]
    return jnp.where(holder, mine, handed)


def strand_output(parts, starts, prefix, carry, x, d_wide):
    start_states = starts + prefix[:, None, :] * carry[None]
    carried = jnp.einsum(
        "kin,knc->kic", parts["cb"].astype(f32), start_states, precision=lax.Precision.HIGH
    )
    length, inner = x.shape
    carried = carried.reshape(length, inner)
    return parts["intra"] + parts["cum_wide"] * carried + d_wide[None, :] * x.astype(f32)


def per_device(
    hidden,
    base_ids,
    embed,
    w_x,
    w_z,
    w_bc,
    w_dt,
    dt_bias,
    decay_rate,
    conv_x,
    conv_bc,
    d_skip,
    norm_gain,
    w_out,
):
    inner = w_x.shape[1]
    state = w_bc.shape[1] // 2
    conv = conv_x.shape[0]
    onehot = (base_ids[:, None] == jnp.arange(embed.shape[0], dtype=jnp.int32)[None, :]).astype(bf16)
    mixed_in = (hidden.astype(f32) + jnp.dot(onehot, embed, preferred_element_type=f32)).astype(bf16)
    rim = 8
    peers = lax.axis_size("ch")
    both_axes = ("ctx", "ch")
    count = lax.axis_size(both_axes)
    before, after = [], []
    for h in range(peers):
        ahead = [(q, q + h + 1) for q in range(count) if q % peers == peers - 1 and q + h + 1 < count]
        behind = [(q, q - peers + h) for q in range(count) if q % peers == 0 and q - peers + h >= 0]
        before.append(lax.ppermute(mixed_in[-rim:], both_axes, ahead))
        after.append(lax.ppermute(mixed_in[:rim], both_axes, behind))
    me = lax.axis_index("ch")
    u = gather_rows(mixed_in, "ch")
    u_ext = jnp.concatenate(
        [
            jnp.stack(before)[me],
            u,
            jnp.stack(after)[me],
        ],
        axis=0,
    )
    length, width = u.shape
    flip = flip_matrix(width)
    u_ext_flip = jnp.dot(u_ext, flip, preferred_element_type=f32).astype(bf16)
    both_ext = jnp.concatenate([u_ext, u_ext_flip], axis=0)
    both = jnp.concatenate([u_ext[rim : rim + length], u_ext_flip[rim : rim + length]], axis=0)
    x_raw = jnp.dot(both_ext, w_x, preferred_element_type=f32).astype(bf16)
    bc_raw = jnp.dot(both_ext, w_bc, preferred_element_type=f32).astype(bf16)
    z_all = jnp.dot(both, w_z, preferred_element_type=f32).astype(bf16)
    dt_all = jax.nn.softplus(jnp.dot(both, w_dt, preferred_element_type=f32) + dt_bias[None, :])
    ext = length + 2 * rim
    d_wide = head_spread(d_skip[None, :], inner)[0]

    outs = []
    sums = []
    for backward in (False, True):
        rows = slice(length, 2 * length) if backward else slice(0, length)
        ext_rows = slice(ext, 2 * ext) if backward else slice(0, ext)
        x_c = conv_silu(x_raw[ext_rows], conv_x, rim, length, backward)
        bc_c = conv_silu(bc_raw[ext_rows], conv_bc, rim, length, backward)
        parts = local_ssd(x_c, dt_all[rows], bc_c[:, :state], bc_c[:, state:], decay_rate, backward)
        starts, prefix, end_state, end_decay = stretch_states(parts, backward)
        carry = scan_over("ctx", end_decay, end_state, backward)
        y = strand_output(parts, starts, prefix, carry, x_c, d_wide)
        gated = (y * jax.nn.silu(z_all[rows].astype(f32))).astype(bf16).astype(f32)
        outs.append(gated)
        sums.append(jnp.sum(gated * gated, axis=1))
    total = lax.psum(jnp.stack(sums), "ch")
    full_inner = inner * lax.axis_size("ch")
    gain = norm_gain.astype(f32)[None, :]
    normed = [
        (g * lax.rsqrt(t / full_inner + norm_eps)[:, None] * gain).astype(bf16)
        for g, t in zip(outs, total)
    ]
    own_rows = length // peers

    def partial_for(normed_pair, target):
        nf = lax.dynamic_slice_in_dim(normed_pair[0], target * own_rows, own_rows, axis=0)
        nb_ = lax.dynamic_slice_in_dim(normed_pair[1], target * own_rows, own_rows, axis=0)
        out_both = jnp.dot(jnp.concatenate([nf, nb_], axis=0), w_out, preferred_element_type=f32)
        return out_both[:own_rows] + flipped_columns(out_both[own_rows:], flip)

    received = []
    sent_all = []
    for d in range(1, peers):
        sent = partial_for(normed, (me + d) % peers).astype(bf16)
        sent_all.append(sent)
        route = [(i, (i + d) % peers) for i in range(peers)]
        received.append(lax.ppermute(sent, "ch", route))
    _, normed_later = lax.optimization_barrier((sent_all, normed))
    summed = partial_for(normed_later, me)
    for r in received:
        summed = summed + r.astype(f32)
    return summed.astype(bf16)


def solution(mesh):
    placed = (
        P(("ctx", "ch"), None),
        P(("ctx", "ch")),
        P(),
        P(None, "ch"),
        P(None, "ch"),
        P(),
        P(None, "ch"),
        P("ch"),
        P("ch"),
        P(None, "ch"),
        P(),
        P("ch"),
        P("ch"),
        P("ch", None),
    )
    return jax.shard_map(
        per_device, mesh=mesh, in_specs=placed, out_specs=P(("ctx", "ch"), None), check_vma=False
    )
```

```python
import jax
import jax.numpy as jnp
from jax import lax
from jax.experimental import pallas as pl
from jax.sharding import PartitionSpec as P

HEAD_DIM = 64
GROUP = 128

exact_dot = lax.Precision.HIGHEST
norm_eps = 1e-05
f32 = jnp.float32
bf16 = jnp.bfloat16


def flip_matrix(n):
    rows = lax.broadcasted_iota(jnp.int32, (n, n), 0)
    cols = lax.broadcasted_iota(jnp.int32, (n, n), 1)
    return (rows + cols == n - 1).astype(bf16)


def shifted(block, axis, distance, parity=None):
    devices = range(lax.axis_size(axis))
    route = [
        (i, i + distance)
        for i in devices
        if i + distance in devices and (parity is None or i % 2 == parity)
    ]
    return lax.ppermute(block, axis, route)


def gather_rows(block, axis):
    peers, me = lax.axis_size(axis), lax.axis_index(axis)
    got = [block] + [
        lax.ppermute(block, axis, [(i, (i + d) % peers) for i in range(peers)])
        for d in range(peers - 1, 0, -1)
    ]
    stacked = jnp.stack(got)
    rolled = jnp.roll(stacked, me, axis=0)
    return rolled.reshape(peers * block.shape[0], *block.shape[1:])


def bf16_part(values):
    return lax.reduce_precision(values, exponent_bits=8, mantissa_bits=7)


def flipped_columns(part, flip):
    hi = bf16_part(part)
    lo = part - hi
    rows = part.shape[0]
    split = jnp.concatenate([hi, lo], axis=0).astype(bf16)
    pieces = jnp.dot(split, flip, preferred_element_type=f32)
    return pieces[:rows] + pieces[rows:]


def conv_silu(raw_ext, taps, rim, length, backward):
    conv = taps.shape[0]
    summed = None
    for k in range(conv):
        first = rim + conv - 1 - k if backward else rim - (conv - 1) + k
        term = taps[k][None, :] * raw_ext[first : first + length].astype(f32)
        summed = term if summed is None else summed + term
    return jax.nn.silu(summed).astype(bf16)


def intra_kernel(w_ref, x_ref, o_ref):
    lanes = 128
    per_tile = lanes // HEAD_DIM
    rows = x_ref.shape[0]
    owner = lax.broadcasted_iota(jnp.int32, (rows, lanes), 1) // HEAD_DIM
    for g in range(x_ref.shape[1] // lanes):
        tile = x_ref[:, g * lanes : (g + 1) * lanes]
        zero = jnp.zeros_like(tile)
        stacked = jnp.concatenate([jnp.where(owner == t, tile, zero) for t in range(per_tile)], axis=0)
        wide = jnp.concatenate([w_ref[0, g * per_tile + t] for t in range(per_tile)], axis=1)
        o_ref[:, g * lanes : (g + 1) * lanes] = jnp.dot(wide, stacked, preferred_element_type=f32)


def intra_block(weights, x):
    nb, heads, group, _ = weights.shape
    length, inner = x.shape
    return pl.pallas_call(
        intra_kernel,
        out_shape=jax.ShapeDtypeStruct((length, inner), f32),
        grid=(nb,),
        in_specs=[
            pl.BlockSpec((1, heads, group, group), lambda k: (k, 0, 0, 0)),
            pl.BlockSpec((group, inner), lambda k: (k, 0)),
        ],
        out_specs=pl.BlockSpec((group, inner), lambda k: (k, 0)),
    )(weights, x)


def head_spread(values, inner):
    heads = values.shape[-1]
    owner = lax.broadcasted_iota(jnp.int32, (heads, inner), 1) // HEAD_DIM
    spread = (owner == lax.broadcasted_iota(jnp.int32, (heads, inner), 0)).astype(f32)
    return jnp.dot(values, spread, precision=lax.Precision.HIGH)


def local_ssd(x, dt, b_mat, c_mat, rates, backward):
    length, inner = x.shape
    heads = dt.shape[1]
    nb = length // GROUP
    xb = x.reshape(nb, GROUP, heads, HEAD_DIM)
    dtb = dt.reshape(nb, GROUP, heads)
    bb = b_mat.reshape(nb, GROUP, -1)
    cb = c_mat.reshape(nb, GROUP, -1)
    step = -dtb * rates[None, None, :]
    cum = lax.cumsum(step, axis=1, reverse=backward)
    last = cum[:, 0, :] if backward else cum[:, -1, :]
    scores = jnp.einsum("kin,kjn->kij", cb, bb, preferred_element_type=f32)
    rows = lax.broadcasted_iota(jnp.int32, (GROUP, GROUP), 0)
    cols = lax.broadcasted_iota(jnp.int32, (GROUP, GROUP), 1)
    mask = (rows <= cols) if backward else (rows >= cols)
    mask = mask[None, None]
    cum_t = cum.transpose(0, 2, 1)
    gap = jnp.where(mask, cum_t[:, :, :, None] - cum_t[:, :, None, :], 0.0)
    dt_t = dtb.transpose(0, 2, 1)
    weights = jnp.where(mask, scores[:, None] * jnp.exp(gap) * dt_t[:, :, None, :], 0.0).astype(bf16)
    intra = intra_block(weights, x)
    tail = jnp.exp(last[:, None, :] - cum) * dtb
    tail_wide = head_spread(tail.reshape(length, heads), inner).reshape(nb, GROUP, inner)
    scaled = x.reshape(nb, GROUP, inner).astype(f32) * tail_wide
    block_state = jnp.einsum("kjn,kjc->knc", bb, scaled.astype(bf16), preferred_element_type=f32)
    block_decay = head_spread(jnp.exp(last), inner)
    cum_wide = head_spread(jnp.exp(cum).reshape(length, heads), inner)
    return dict(
        cb=cb,
        cum_wide=cum_wide,
        intra=intra,
        block_state=block_state,
        block_decay=block_decay,
    )


def stretch_states(parts, backward):
    block_state, block_decay = parts["block_state"], parts["block_decay"]
    nb = block_state.shape[0]
    order = list(range(nb - 1, -1, -1)) if backward else list(range(nb))
    starts = [None] * nb
    prefix = [None] * nb
    run_state = jnp.zeros_like(block_state[0])
    run_decay = jnp.ones_like(block_decay[0])
    for k in order:
        starts[k] = run_state
        prefix[k] = run_decay
        run_state = block_decay[k][None, :] * run_state + block_state[k]
        run_decay = run_decay * block_decay[k]
    return jnp.stack(starts), jnp.stack(prefix), run_state, run_decay


def pair_combine(earlier, later):
    (a0, s0), (a1, s1) = earlier, later
    return a1 * a0, a1[None, :] * s0 + s1


def scan_over(axis, own_decay, own_state, backward):
    peers = lax.axis_size(axis)
    step = -1 if backward else 1
    own = (own_decay, own_state)
    holder_parity = 0 if backward else 1
    first = shifted((own_decay, own_state.astype(bf16)), axis, step, 1 - holder_parity)
    first = (first[0], first[1].astype(f32))
    me = lax.axis_index(axis)
    holder = (me % 2 == 0) if backward else (me % 2 == 1)
    total = pair_combine(first, own)
    ex_decay = jnp.ones_like(own_decay)
    ex_state = jnp.zeros_like(own_state)
    in_decay, in_state = total
    distance = 2
    while distance < peers:
        got_decay, got_state = shifted(
            (in_decay, in_state.astype(bf16)), axis, step * distance, holder_parity
        )
        got_state = got_state.astype(f32)
        ex_state = ex_decay[None, :] * got_state + ex_state
        ex_decay = ex_decay * got_decay
        if distance * 2 < peers:
            in_state = in_decay[None, :] * got_state + in_state
            in_decay = in_decay * got_decay
        distance *= 2
    handed = shifted(ex_state.astype(bf16), axis, -step, holder_parity).astype(f32)
    mine = first[0][None, :] * ex_state + first[1]
    return jnp.where(holder, mine, handed)


def strand_output(parts, starts, prefix, carry, x, d_wide):
    start_states = starts + prefix[:, None, :] * carry[None]
    carried = jnp.einsum(
        "kin,knc->kic", parts["cb"].astype(f32), start_states, precision=lax.Precision.HIGH
    )
    length, inner = x.shape
    carried = carried.reshape(length, inner)
    return parts["intra"] + parts["cum_wide"] * carried + d_wide[None, :] * x.astype(f32)


def per_device(
    hidden,
    base_ids,
    embed,
    w_x,
    w_z,
    w_bc,
    w_dt,
    dt_bias,
    decay_rate,
    conv_x,
    conv_bc,
    d_skip,
    norm_gain,
    w_out,
):
    inner = w_x.shape[1]
    state = w_bc.shape[1] // 2
    conv = conv_x.shape[0]
    onehot = (base_ids[:, None] == jnp.arange(embed.shape[0], dtype=jnp.int32)[None, :]).astype(bf16)
    mixed_in = (hidden.astype(f32) + jnp.dot(onehot, embed, preferred_element_type=f32)).astype(bf16)
    rim = 8
    peers = lax.axis_size("ch")
    both_axes = ("ctx", "ch")
    count = lax.axis_size(both_axes)
    before, after = [], []
    for h in range(peers):
        ahead = [(q, q + h + 1) for q in range(count) if q % peers == peers - 1 and q + h + 1 < count]
        behind = [(q, q - peers + h) for q in range(count) if q % peers == 0 and q - peers + h >= 0]
        before.append(lax.ppermute(mixed_in[-rim:], both_axes, ahead))
        after.append(lax.ppermute(mixed_in[:rim], both_axes, behind))
    me = lax.axis_index("ch")
    u = gather_rows(mixed_in, "ch")
    u_ext = jnp.concatenate(
        [
            jnp.stack(before)[me],
            u,
            jnp.stack(after)[me],
        ],
        axis=0,
    )
    length, width = u.shape
    flip = flip_matrix(width)
    u_ext_flip = jnp.dot(u_ext, flip, preferred_element_type=f32).astype(bf16)
    both_ext = jnp.concatenate([u_ext, u_ext_flip], axis=0)
    both = jnp.concatenate([u_ext[rim : rim + length], u_ext_flip[rim : rim + length]], axis=0)
    x_raw = jnp.dot(both_ext, w_x, preferred_element_type=f32).astype(bf16)
    bc_raw = jnp.dot(both_ext, w_bc, preferred_element_type=f32).astype(bf16)
    z_all = jnp.dot(both, w_z, preferred_element_type=f32).astype(bf16)
    dt_all = jax.nn.softplus(jnp.dot(both, w_dt, preferred_element_type=f32) + dt_bias[None, :])
    ext = length + 2 * rim
    d_wide = head_spread(d_skip[None, :], inner)[0]

    outs = []
    sums = []
    for backward in (False, True):
        rows = slice(length, 2 * length) if backward else slice(0, length)
        ext_rows = slice(ext, 2 * ext) if backward else slice(0, ext)
        x_c = conv_silu(x_raw[ext_rows], conv_x, rim, length, backward)
        bc_c = conv_silu(bc_raw[ext_rows], conv_bc, rim, length, backward)
        parts = local_ssd(x_c, dt_all[rows], bc_c[:, :state], bc_c[:, state:], decay_rate, backward)
        starts, prefix, end_state, end_decay = stretch_states(parts, backward)
        carry = scan_over("ctx", end_decay, end_state, backward)
        y = strand_output(parts, starts, prefix, carry, x_c, d_wide)
        gated = (y * jax.nn.silu(z_all[rows].astype(f32))).astype(bf16).astype(f32)
        outs.append(gated)
        sums.append(jnp.sum(gated * gated, axis=1))
    total = lax.psum(jnp.stack(sums), "ch")
    full_inner = inner * lax.axis_size("ch")
    gain = norm_gain.astype(f32)[None, :]
    normed = [
        (g * lax.rsqrt(t / full_inner + norm_eps)[:, None] * gain).astype(bf16)
        for g, t in zip(outs, total)
    ]
    own_rows = length // peers

    def partial_for(normed_pair, target):
        nf = lax.dynamic_slice_in_dim(normed_pair[0], target * own_rows, own_rows, axis=0)
        nb_ = lax.dynamic_slice_in_dim(normed_pair[1], target * own_rows, own_rows, axis=0)
        out_both = jnp.dot(jnp.concatenate([nf, nb_], axis=0), w_out, preferred_element_type=f32)
        return out_both[:own_rows] + flipped_columns(out_both[own_rows:], flip)

    received = []
    sent_all = []
    for d in range(1, peers):
        sent = partial_for(normed, (me + d) % peers).astype(bf16)
        sent_all.append(sent)
        route = [(i, (i + d) % peers) for i in range(peers)]
        received.append(lax.ppermute(sent, "ch", route))
    _, normed_later = lax.optimization_barrier((sent_all, normed))
    summed = partial_for(normed_later, me)
    for r in received:
        summed = summed + r.astype(f32)
    return summed.astype(bf16)


def solution(mesh):
    placed = (
        P(("ctx", "ch"), None),
        P(("ctx", "ch")),
        P(),
        P(None, "ch"),
        P(None, "ch"),
        P(),
        P(None, "ch"),
        P("ch"),
        P("ch"),
        P(None, "ch"),
        P(),
        P("ch"),
        P("ch"),
        P("ch", None),
    )
    return jax.shard_map(
        per_device, mesh=mesh, in_specs=placed, out_specs=P(("ctx", "ch"), None), check_vma=False
    )
```
